32 devices in a mesh: groups: 2 (over y), ctx: 4 (over z), head: 4 (over x, core).
Axes of the slice: x: 2, y: 2, z: 4, core: 2. Of those that a mesh axis runs over, the one named last changes fastest.
Arguments:
- queries: bfloat16 [1024, 8192], P(('groups', 'ctx'), 'head'), parts along dimension 0, may hold values from -6 to 6
- key_states: bfloat16 [1024, 1024], P(('groups', 'ctx'), 'head'), parts along dimension 0, may hold values from -8.5 to 8.5
- value_states: bfloat16 [1024, 1024], P(('groups', 'ctx'), 'head'), parts along dimension 0, may hold values from -6 to 6
- out_grad: bfloat16 [1024, 8192], P(('groups', 'ctx'), 'head'), parts along dimension 0, may hold values from -6 to 6
- mask_flags: int32 [8, 4], P('groups'), parts along dimension 0, may hold values from 0 to 1, as said below
- shard_blocks: int32 [8], P('groups'), parts along dimension 0, may hold values from 0 to 3, each once
- key_proj: bfloat16 [8192, 1024], P(None, 'head'), may hold values from -0.1875 to 0.1875
- value_proj: bfloat16 [8192, 1024], P(None, 'head'), may hold values from -0.1875 to 0.1875
Outputs:
- query_grad: bfloat16 [1024, 8192], P(('groups', 'ctx'), 'head'), parts along dimension 0
- key_grad: bfloat16 [1024, 1024], P(('groups', 'ctx'), 'head'), parts along dimension 0
- value_grad: bfloat16 [1024, 1024], P(('groups', 'ctx'), 'head'), parts along dimension 0
- input_grad_t: bfloat16 [8192, 1024], P('head', ('groups', 'ctx')), parts along dimension 1
The draws below stay inside these ranges and needn't reach their ends.
There are 2 independent parts, one for each index of `groups`. The reference program is written for one: setup_inputs(seed, part) draws one part's arguments, and reference() takes and returns one part's arrays. A program takes and returns all parts, laid end to end along the dimension named above; an argument that names none is the same for every part. Nothing has to cross between parts.
Inputs may be any that keep to these rules, and one draw needn't show every extreme that they name: mask_flags[b, b] = 1 for every block b. `shard_blocks`: a permutation of the block numbers.
All inputs are finite; a program needn't handle non-finite values.
Results may differ from the reference program's by a relative error of at most 0.039.
Values may be sent and summed in bfloat16 or wider, within the bound.
No kernel may reach another device: no remote copies, remote signals or barrier semaphores. Data moves between devices by JAX's collectives and lax.ppermute only.
A program may use at most 64 MiB of HBM per device.

```python
import jax
import jax.numpy as jnp
from jax import lax

D = 8192
QH = 64
KVH = 8
HD = 128
BLK = 128
TOKENS = 512
NB = 4


def draw_queries(key, part):
    full_shape = (TOKENS, QH * HD)
    drawn = jnp.clip(jax.random.normal(jax.random.fold_in(key, 12), full_shape, jnp.float32), -6.0, 6.0)
    return drawn.astype(jnp.bfloat16)


def draw_key_states(key, part):
    full_shape = (TOKENS, KVH * HD)
    drawn = jnp.clip(jax.random.normal(jax.random.fold_in(key, 14), full_shape, jnp.float32), -6.0, 6.0)
    return drawn.astype(jnp.bfloat16)


def draw_mask_flags(key, part):
    levels = jax.random.randint(jax.random.fold_in(key, 21), (NB, 1), 0, 5)
    row_limit = jnp.left_shift(jnp.ones((NB, 1), jnp.int32), levels)
    dice_rolls = jax.random.randint(jax.random.fold_in(key, 22), (NB, NB), 0, 20)
    diagonal_cells = jnp.arange(NB, dtype=jnp.int32)[:, None] == jnp.arange(NB, dtype=jnp.int32)[None, :]
    return jnp.where(diagonal_cells | (dice_rolls < row_limit), 1, 0).astype(jnp.int32)


def block_levels(stream_key, extent, shards, low, top_value):
    gain, own = 1.0, jax.random.fold_in(stream_key, 6)
    for dim, shards_of in shards:
        draws = jnp.exp(jax.random.uniform(jax.random.fold_in(own, dim), (shards_of,), jnp.float32, low / len(shards), top_value / len(shards)))
        gain = gain * jnp.repeat(draws, extent[dim] // shards_of).reshape([-1 if axis == dim else 1 for axis in range(len(extent))])
    return gain


def gaussian(own_key, dims, deviation, bound, pieces=(), kind=jnp.bfloat16):
    values = deviation * jax.random.normal(own_key, dims, jnp.float32)
    if pieces:
        values = values * block_levels(own_key, dims, pieces, -0.22, 0.18)
    return jnp.clip(values, -bound, bound).astype(kind)


def setup_inputs(seed: int = 0, part: int = 0) -> dict:
    key_list = jax.random.split(jax.random.key(seed), 9)
    own_keys = jax.random.split(jax.random.fold_in(key_list[8], part), 9)
    return {
        "queries": draw_queries(jax.random.fold_in(jax.random.fold_in(key_list[8], part), 71), part),
        "key_states": draw_key_states(jax.random.fold_in(jax.random.fold_in(key_list[8], part), 71), part),
        "value_states": gaussian(own_keys[2], (TOKENS, KVH * HD), 1.0, 6.0, ((0, 4), (1, 4))),
        "out_grad": gaussian(own_keys[3], (TOKENS, QH * HD), 1.0, 6.0, ((0, 4), (1, 4))),
        "mask_flags": draw_mask_flags(jax.random.fold_in(jax.random.fold_in(key_list[8], part), 71), part),
        "shard_blocks": jax.random.permutation(own_keys[5], NB).astype(jnp.int32),
        "key_proj": gaussian(key_list[6], (D, KVH * HD), (KVH * HD) ** -0.5, 0.1875, ((1, 4),)),
        "value_proj": gaussian(key_list[7], (D, KVH * HD), (KVH * HD) ** -0.5, 0.1875, ((1, 4),)),
    }


def head_backward(query_head, grad_head, key_head, value_head, allowed):
    inv_root = HD ** -0.5
    scores = jnp.dot(query_head, key_head.T, preferred_element_type=jnp.float32) * inv_root
    scores = jnp.where(allowed, scores, -jnp.inf)
    row_max = jnp.max(scores, axis=-1, keepdims=True)
    shifted = jnp.exp(scores - row_max)
    row_sum = jnp.sum(shifted, axis=-1, keepdims=True)
    log_total = row_max + jnp.log(row_sum)
    probs = jnp.exp(scores - log_total)
    weighted = jnp.dot(shifted.astype(jnp.bfloat16), value_head, preferred_element_type=jnp.float32)
    attended = (weighted / row_sum).astype(jnp.bfloat16)
    attended = lax.optimization_barrier(attended)
    row_delta = jnp.sum(grad_head.astype(jnp.float32) * attended.astype(jnp.float32), axis=-1, keepdims=True)
    dprobs = jnp.dot(grad_head, value_head.T, preferred_element_type=jnp.float32)
    dscores = (probs * (dprobs - row_delta)).astype(jnp.bfloat16)
    query_term = jnp.dot(dscores, key_head, preferred_element_type=jnp.float32) * inv_root
    key_term = jnp.dot(dscores.T, query_head, preferred_element_type=jnp.float32) * inv_root
    value_term = jnp.dot(probs.astype(jnp.bfloat16).T, grad_head, preferred_element_type=jnp.float32)
    return query_term, key_term, value_term


def reference(queries, key_states, value_states, out_grad, mask_flags, shard_blocks, key_proj, value_proj):
    tokens = queries.shape[0]
    group_size = QH // KVH
    layout = jnp.take(jnp.take(mask_flags, shard_blocks, axis=0), shard_blocks, axis=1)
    allowed = jnp.repeat(jnp.repeat(layout > 0, BLK, axis=0), BLK, axis=1)
    query_stack = queries.reshape(tokens, QH, HD).transpose(1, 0, 2)
    grad_stack = out_grad.reshape(tokens, QH, HD).transpose(1, 0, 2)
    key_stack = key_states.reshape(tokens, KVH, HD).transpose(1, 0, 2)
    value_stack = value_states.reshape(tokens, KVH, HD).transpose(1, 0, 2)

    def per_head(inputs):
        query_head, grad_head, head_index = inputs
        kv_index = head_index // group_size
        key_head = lax.dynamic_index_in_dim(key_stack, kv_index, 0, keepdims=False)
        value_head = lax.dynamic_index_in_dim(value_stack, kv_index, 0, keepdims=False)
        return head_backward(query_head, grad_head, key_head, value_head, allowed)

    query_terms, key_terms, value_terms = lax.map(per_head, (query_stack, grad_stack, jnp.arange(QH, dtype=jnp.int32)))
    query_grad = query_terms.transpose(1, 0, 2).reshape(tokens, QH * HD).astype(jnp.bfloat16)
    key_sum = jnp.sum(key_terms.reshape(KVH, group_size, tokens, HD), axis=1)
    value_sum = jnp.sum(value_terms.reshape(KVH, group_size, tokens, HD), axis=1)
    key_grad = key_sum.transpose(1, 0, 2).reshape(tokens, KVH * HD).astype(jnp.bfloat16)
    value_grad = value_sum.transpose(1, 0, 2).reshape(tokens, KVH * HD).astype(jnp.bfloat16)
    input_grad_t = (jnp.dot(key_proj, key_grad.T, preferred_element_type=jnp.float32)
                    + jnp.dot(value_proj, value_grad.T, preferred_element_type=jnp.float32)).astype(jnp.bfloat16)
    return (query_grad, key_grad, value_grad, input_grad_t)
```

```python
import math

import jax
import jax.numpy as jnp
from jax import lax
from jax.sharding import PartitionSpec as P

HD = 128
BLK = 128


masked_score = -1e30


def select_rows(lookup, picked):
    onehot = (picked[:, None] == lax.iota(jnp.int32, lookup.shape[0])[None, :]).astype(jnp.int32)
    return jnp.sum(onehot[:, :, None] * lookup[None, :, :], axis=1)


def select_cols(lookup, picked):
    onehot = (picked[:, None] == lax.iota(jnp.int32, lookup.shape[1])[None, :]).astype(jnp.int32)
    return jnp.sum(lookup[:, None, :] * onehot[None, :, :], axis=2)


def local(
    queries, key_states, value_states, out_grad, mask_flags, shard_blocks, key_proj, value_proj
):
    rows_here = queries.shape[0]
    kv_cols = key_states.shape[1]
    kv_heads = kv_cols // HD
    group_size = queries.shape[1] // kv_cols
    inv_root = HD ** (-0.5)
    position = lax.axis_index("ctx")
    query_heads = queries.reshape(rows_here, kv_heads, group_size, HD)
    grad_heads = out_grad.reshape(rows_here, kv_heads, group_size, HD)
    own_blocks = lax.dynamic_slice_in_dim(
        shard_blocks, position * (rows_here // BLK), rows_here // BLK
    )
    own_flags = select_rows(mask_flags, own_blocks)

    kv_rows = lax.all_gather(
        jnp.concatenate([key_states, value_states], axis=1), "ctx", axis=0, tiled=True
    )
    row_count = kv_rows.shape[0]
    step_rows = math.gcd(row_count, 512)
    steps = row_count // step_rows

    def chunk(offset):
        block = lax.dynamic_slice_in_dim(kv_rows, offset, step_rows)
        key_heads = block[:, :kv_cols].reshape(step_rows, kv_heads, HD)
        value_heads = block[:, kv_cols:].reshape(step_rows, kv_heads, HD)
        their_blocks = lax.dynamic_slice_in_dim(shard_blocks, offset // BLK, step_rows // BLK)
        pair_flags = select_cols(own_flags, their_blocks) > 0
        allowed = jnp.repeat(jnp.repeat(pair_flags, BLK, axis=0), BLK, axis=1)
        scores = (
            jnp.einsum("qkgd,tkd->kgqt", query_heads, key_heads, preferred_element_type=jnp.float32)
            * inv_root
        )
        scores = jnp.where(allowed[None, None], scores, masked_score)
        return key_heads, value_heads, allowed, scores

    def forward_stats(offset, current):
        row_max, row_sum, weighted = current
        key_heads, value_heads, allowed, scores = chunk(offset)
        new_max = jnp.maximum(row_max, jnp.max(scores, axis=-1))
        rescale = jnp.exp(row_max - new_max)
        shifted = jnp.where(allowed[None, None], jnp.exp(scores - new_max[..., None]), 0.0)
        row_sum = row_sum * rescale + jnp.sum(shifted, axis=-1)
        weighted = weighted * rescale[..., None] + jnp.einsum(
            "kgqt,tkd->kgqd",
            shifted.astype(jnp.bfloat16),
            value_heads,
            preferred_element_type=jnp.float32,
        )
        return (new_max, row_sum, weighted)

    def backward_chunk(offset, log_total, row_delta, scores_given=None):
        key_heads, value_heads, allowed, scores = chunk(offset)
        if scores_given is not None:
            scores = scores_given
        probs = jnp.exp(scores - log_total[..., None])
        dprobs = jnp.einsum(
            "qkgd,tkd->kgqt", grad_heads, value_heads, preferred_element_type=jnp.float32
        )
        dscores = (probs * (dprobs - row_delta[..., None])).astype(jnp.bfloat16)
        probs_low = probs.astype(jnp.bfloat16)
        query_term = (
            jnp.einsum("kgqt,tkd->qkgd", dscores, key_heads, preferred_element_type=jnp.float32)
            * inv_root
        )
        key_term = (
            jnp.einsum("kgqt,qkgd->tkd", dscores, query_heads, preferred_element_type=jnp.float32)
            * inv_root
        )
        value_term = jnp.einsum(
            "kgqt,qkgd->tkd", probs_low, grad_heads, preferred_element_type=jnp.float32
        )
        kv_term = jnp.concatenate(
            [key_term.reshape(step_rows, kv_cols), value_term.reshape(step_rows, kv_cols)], axis=1
        )
        return query_term, kv_term

    start_stats = (
        jnp.full((kv_heads, group_size, rows_here), masked_score, jnp.float32),
        jnp.zeros((kv_heads, group_size, rows_here), jnp.float32),
        jnp.zeros((kv_heads, group_size, rows_here, HD), jnp.float32),
    )
    if steps == 1:
        key_heads, value_heads, allowed, scores = chunk(0)
        row_max = jnp.max(scores, axis=-1)
        shifted = jnp.exp(scores - row_max[..., None])
        row_sum = jnp.sum(shifted, axis=-1)
        weighted = jnp.einsum(
            "kgqt,tkd->kgqd",
            shifted.astype(jnp.bfloat16),
            value_heads,
            preferred_element_type=jnp.float32,
        )
    else:
        row_max, row_sum, weighted = lax.fori_loop(
            0, steps, lambda i, c: forward_stats(i * step_rows, c), start_stats
        )
        scores = None
    log_total = row_max + jnp.log(row_sum)
    attended = (weighted / row_sum[..., None]).astype(jnp.bfloat16)
    row_delta = jnp.einsum(
        "kgqd,qkgd->kgq", attended, grad_heads, preferred_element_type=jnp.float32
    )

    if steps == 1:
        query_acc, kv_acc = backward_chunk(0, log_total, row_delta, scores)
    else:

        def backward_visit(turn_index, current):
            query_now, kv_now = current
            offset = turn_index * step_rows
            query_term, kv_term = backward_chunk(offset, log_total, row_delta)
            kv_now = lax.dynamic_update_slice_in_dim(kv_now, kv_term, offset, 0)
            return (query_now + query_term, kv_now)

        query_acc, kv_acc = lax.fori_loop(
            0,
            steps,
            backward_visit,
            (
                jnp.zeros((rows_here, kv_heads, group_size, HD), jnp.float32),
                jnp.zeros((row_count, 2 * kv_cols), jnp.float32),
            ),
        )

    kv_grad = lax.psum_scatter(kv_acc, "ctx", scatter_dimension=0, tiled=True)
    query_grad = query_acc.reshape(rows_here, -1).astype(jnp.bfloat16)
    key_grad = kv_grad[:, :kv_cols].astype(jnp.bfloat16)
    value_grad = kv_grad[:, kv_cols:].astype(jnp.bfloat16)
    contraction = (((1,), (1,)), ((), ()))
    partial = (
        lax.dot_general(key_proj, key_grad, contraction, preferred_element_type=jnp.float32)
        + lax.dot_general(value_proj, value_grad, contraction, preferred_element_type=jnp.float32)
    ).astype(jnp.bfloat16)
    input_grad_t = lax.psum_scatter(partial, "head", scatter_dimension=0, tiled=True)
    return (query_grad, key_grad, value_grad, input_grad_t)


def solution(mesh):
    return jax.shard_map(
        local,
        mesh=mesh,
        in_specs=(
            P(("groups", "ctx"), "head"),
            P(("groups", "ctx"), "head"),
            P(("groups", "ctx"), "head"),
            P(("groups", "ctx"), "head"),
            P("groups", None),
            P("groups"),
            P(None, "head"),
            P(None, "head"),
        ),
        out_specs=(
            P(("groups", "ctx"), "head"),
            P(("groups", "ctx"), "head"),
            P(("groups", "ctx"), "head"),
            P("head", ("groups", "ctx")),
        ),
        check_vma=False,
    )
```

```python
import math

import jax
import jax.numpy as jnp
from jax import lax
from jax.sharding import PartitionSpec as P

HD = 128
BLK = 128


masked_score = -1e30


def select_rows(lookup, picked):
    onehot = (picked[:, None] == lax.iota(jnp.int32, lookup.shape[0])[None, :]).astype(jnp.int32)
    return jnp.sum(onehot[:, :, None] * lookup[None, :, :], axis=1)


def select_cols(lookup, picked):
    onehot = (picked[:, None] == lax.iota(jnp.int32, lookup.shape[1])[None, :]).astype(jnp.int32)
    return jnp.sum(lookup[:, None, :] * onehot[None, :, :], axis=2)


def pick(vector, picked):
    onehot = (picked[:, None] == lax.iota(jnp.int32, vector.shape[0])[None, :]).astype(jnp.int32)
    return jnp.sum(onehot * vector[None, :], axis=1)


def shifted_pairs(count, steps):
    return [(source, (source + steps) % count) for source in range(count)]


def gather_slots(block, axis):
    count = lax.axis_size(axis)
    position = lax.axis_index(axis)
    if count > 8:
        gathered = lax.all_gather(block, axis, axis=0, tiled=True)
        return gathered, lax.iota(jnp.int32, count)
    pieces = [block] + [
        lax.ppermute(block, axis, shifted_pairs(count, steps)) for steps in range(1, count)
    ]
    sources = (position - lax.iota(jnp.int32, count)) % count
    return jnp.concatenate(pieces, axis=0), sources


def scatter_slots(slots, axis):
    count = lax.axis_size(axis)
    if count > 8:
        return lax.psum_scatter(slots, axis, scatter_dimension=0, tiled=True)
    rows = slots.shape[0] // count
    total = slots[:rows]
    for steps in range(1, count):
        total = total + lax.ppermute(
            slots[steps * rows : (steps + 1) * rows], axis, shifted_pairs(count, -steps)
        )
    return total


def head_reduce(key_proj, value_proj, key_grad, value_grad):
    count = lax.axis_size("head")
    position = lax.axis_index("head")
    depth = count.bit_length() - 1
    contraction = (((1,), (1,)), ((), ()))
    if count == 1 or count != 1 << depth:
        partial = lax.dot_general(
            key_proj, key_grad, contraction, preferred_element_type=jnp.float32
        ) + lax.dot_general(value_proj, value_grad, contraction, preferred_element_type=jnp.float32)
        return lax.psum_scatter(partial, "head", scatter_dimension=0, tiled=True).astype(
            jnp.bfloat16
        )
    block = key_proj.shape[0] // count
    key_split = key_proj.reshape(count // 2, 2, block, key_proj.shape[1])
    value_split = value_proj.reshape(count // 2, 2, block, value_proj.shape[1])

    def project(half):
        return jnp.einsum(
            "arf,tf->art",
            lax.dynamic_index_in_dim(key_split, half, 1, keepdims=False),
            key_grad,
            preferred_element_type=jnp.float32,
        ) + jnp.einsum(
            "arf,tf->art",
            lax.dynamic_index_in_dim(value_split, half, 1, keepdims=False),
            value_grad,
            preferred_element_type=jnp.float32,
        )

    own_bit = position % 2
    sent = project(1 - own_bit)
    kept = project(own_bit)
    current = kept + lax.ppermute(sent, "head", [(i, i ^ 1) for i in range(count)])
    for level in range(1, depth):
        current = current.reshape(-1, 2, block, current.shape[-1])
        own_bit = (position // (1 << level)) % 2
        kept = lax.dynamic_index_in_dim(current, own_bit, 1, keepdims=False)
        sent = lax.dynamic_index_in_dim(current, 1 - own_bit, 1, keepdims=False)
        arrived = lax.ppermute(
            sent.astype(jnp.bfloat16), "head", [(i, i ^ (1 << level)) for i in range(count)]
        )
        current = kept + arrived.astype(jnp.float32)
    return current.reshape(block, -1).astype(jnp.bfloat16)


def local(
    queries, key_states, value_states, out_grad, mask_flags, shard_blocks, key_proj, value_proj
):
    rows_here = queries.shape[0]
    kv_cols = key_states.shape[1]
    kv_heads = kv_cols // HD
    group_size = queries.shape[1] // kv_cols
    inv_root = HD ** (-0.5)
    position = lax.axis_index("ctx")
    query_heads = queries.reshape(rows_here, kv_heads, group_size, HD)
    grad_heads = out_grad.reshape(rows_here, kv_heads, group_size, HD)
    own_blocks = lax.dynamic_slice_in_dim(
        shard_blocks, position * (rows_here // BLK), rows_here // BLK
    )
    own_flags = select_rows(mask_flags, own_blocks)

    kv_rows, sources = gather_slots(
        jnp.concatenate([key_states, value_states], axis=1), "ctx"
    )
    row_count = kv_rows.shape[0]
    blocks_here = rows_here // BLK
    key_blocks = lax.iota(jnp.int32, row_count // BLK)
    key_doc_blocks = pick(
        shard_blocks,
        pick(sources, key_blocks // blocks_here) * blocks_here + key_blocks % blocks_here,
    )
    step_rows = math.gcd(row_count, 512)
    steps = row_count // step_rows

    def chunk(offset):
        block = lax.dynamic_slice_in_dim(kv_rows, offset, step_rows)
        key_heads = block[:, :kv_cols].reshape(step_rows, kv_heads, HD)
        value_heads = block[:, kv_cols:].reshape(step_rows, kv_heads, HD)
        their_blocks = lax.dynamic_slice_in_dim(key_doc_blocks, offset // BLK, step_rows // BLK)
        pair_flags = select_cols(own_flags, their_blocks) > 0
        allowed = jnp.repeat(jnp.repeat(pair_flags, BLK, axis=0), BLK, axis=1)
        scores = (
            jnp.einsum("qkgd,tkd->kgqt", query_heads, key_heads, preferred_element_type=jnp.float32)
            * inv_root
        )
        scores = jnp.where(allowed[None, None], scores, masked_score)
        return key_heads, value_heads, allowed, scores

    def forward_stats(offset, current):
        row_max, row_sum, weighted = current
        key_heads, value_heads, allowed, scores = chunk(offset)
        new_max = jnp.maximum(row_max, jnp.max(scores, axis=-1))
        rescale = jnp.exp(row_max - new_max)
        shifted = jnp.where(allowed[None, None], jnp.exp(scores - new_max[..., None]), 0.0)
        row_sum = row_sum * rescale + jnp.sum(shifted, axis=-1)
        weighted = weighted * rescale[..., None] + jnp.einsum(
            "kgqt,tkd->kgqd",
            shifted.astype(jnp.bfloat16),
            value_heads,
            preferred_element_type=jnp.float32,
        )
        return (new_max, row_sum, weighted)

    def backward_chunk(offset, log_total, row_delta, scores_given=None):
        key_heads, value_heads, allowed, scores = chunk(offset)
        if scores_given is not None:
            scores = scores_given
        probs = jnp.exp(scores - log_total[..., None])
        dprobs = jnp.einsum(
            "qkgd,tkd->kgqt", grad_heads, value_heads, preferred_element_type=jnp.float32
        )
        dscores = (probs * (dprobs - row_delta[..., None])).astype(jnp.bfloat16)
        probs_low = probs.astype(jnp.bfloat16)
        query_term = (
            jnp.einsum("kgqt,tkd->qkgd", dscores, key_heads, preferred_element_type=jnp.float32)
            * inv_root
        )
        key_term = (
            jnp.einsum("kgqt,qkgd->tkd", dscores, query_heads, preferred_element_type=jnp.float32)
            * inv_root
        )
        value_term = jnp.einsum(
            "kgqt,qkgd->tkd", probs_low, grad_heads, preferred_element_type=jnp.float32
        )
        kv_term = jnp.concatenate(
            [key_term.reshape(step_rows, kv_cols), value_term.reshape(step_rows, kv_cols)], axis=1
        )
        return query_term, kv_term

    start_stats = (
        jnp.full((kv_heads, group_size, rows_here), masked_score, jnp.float32),
        jnp.zeros((kv_heads, group_size, rows_here), jnp.float32),
        jnp.zeros((kv_heads, group_size, rows_here, HD), jnp.float32),
    )
    if steps == 1:
        key_heads, value_heads, allowed, scores = chunk(0)
        row_max = jnp.max(scores, axis=-1)
        shifted = jnp.exp(scores - row_max[..., None])
        row_sum = jnp.sum(shifted, axis=-1)
        weighted = jnp.einsum(
            "kgqt,tkd->kgqd",
            shifted.astype(jnp.bfloat16),
            value_heads,
            preferred_element_type=jnp.float32,
        )
    else:
        row_max, row_sum, weighted = lax.fori_loop(
            0, steps, lambda i, c: forward_stats(i * step_rows, c), start_stats
        )
        scores = None
    log_total = row_max + jnp.log(row_sum)
    attended = (weighted / row_sum[..., None]).astype(jnp.bfloat16)
    row_delta = jnp.einsum(
        "kgqd,qkgd->kgq", attended, grad_heads, preferred_element_type=jnp.float32
    )

    if steps == 1:
        query_acc, kv_acc = backward_chunk(0, log_total, row_delta, scores)
    else:

        def backward_visit(turn_index, current):
            query_now, kv_now = current
            offset = turn_index * step_rows
            query_term, kv_term = backward_chunk(offset, log_total, row_delta)
            kv_now = lax.dynamic_update_slice_in_dim(kv_now, kv_term, offset, 0)
            return (query_now + query_term, kv_now)

        query_acc, kv_acc = lax.fori_loop(
            0,
            steps,
            backward_visit,
            (
                jnp.zeros((rows_here, kv_heads, group_size, HD), jnp.float32),
                jnp.zeros((row_count, 2 * kv_cols), jnp.float32),
            ),
        )

    kv_grad = scatter_slots(kv_acc, "ctx")
    query_grad = query_acc.reshape(rows_here, -1).astype(jnp.bfloat16)
    key_grad = kv_grad[:, :kv_cols].astype(jnp.bfloat16)
    value_grad = kv_grad[:, kv_cols:].astype(jnp.bfloat16)
    input_grad_t = head_reduce(key_proj, value_proj, key_grad, value_grad)
    return (query_grad, key_grad, value_grad, input_grad_t)


def solution(mesh):
    return jax.shard_map(
        local,
        mesh=mesh,
        in_specs=(
            P(("groups", "ctx"), "head"),
            P(("groups", "ctx"), "head"),
            P(("groups", "ctx"), "head"),
            P(("groups", "ctx"), "head"),
            P("groups", None),
            P("groups"),
            P(None, "head"),
            P(None, "head"),
        ),
        out_specs=(
            P(("groups", "ctx"), "head"),
            P(("groups", "ctx"), "head"),
            P(("groups", "ctx"), "head"),
            P("head", ("groups", "ctx")),
        ),
        check_vma=False,
    )
```

```python
import math

import jax
import jax.numpy as jnp
from jax import lax
from jax.sharding import PartitionSpec as P

HD = 128
BLK = 128


masked_score = -1e30


def select_rows(lookup, picked):
    onehot = (picked[:, None] == lax.iota(jnp.int32, lookup.shape[0])[None, :]).astype(jnp.int32)
    return jnp.sum(onehot[:, :, None] * lookup[None, :, :], axis=1)


def select_cols(lookup, picked):
    onehot = (picked[:, None] == lax.iota(jnp.int32, lookup.shape[1])[None, :]).astype(jnp.int32)
    return jnp.sum(lookup[:, None, :] * onehot[None, :, :], axis=2)


def pick(vector, picked):
    onehot = (picked[:, None] == lax.iota(jnp.int32, vector.shape[0])[None, :]).astype(jnp.int32)
    return jnp.sum(onehot * vector[None, :], axis=1)


def shifted_pairs(count, steps):
    return [(source, (source + steps) % count) for source in range(count)]


def gather_slots(block, axis):
    count = lax.axis_size(axis)
    position = lax.axis_index(axis)
    if count > 8:
        gathered = lax.all_gather(block, axis, axis=0, tiled=True)
        return gathered, lax.iota(jnp.int32, count)
    pieces = [block] + [
        lax.ppermute(block, axis, shifted_pairs(count, steps)) for steps in range(1, count)
    ]
    sources = (position - lax.iota(jnp.int32, count)) % count
    return jnp.concatenate(pieces, axis=0), sources


def scatter_slots(slots, axis):
    count = lax.axis_size(axis)
    if count > 8:
        return lax.psum_scatter(slots, axis, scatter_dimension=0, tiled=True)
    rows = slots.shape[0] // count
    total = slots[:rows]
    for steps in range(1, count):
        total = total + lax.ppermute(
            slots[steps * rows : (steps + 1) * rows].astype(jnp.bfloat16),
            axis,
            shifted_pairs(count, -steps),
        ).astype(jnp.float32)
    return total


def head_reduce(key_proj, value_proj, key_grad, value_grad):
    count = lax.axis_size("head")
    position = lax.axis_index("head")
    depth = count.bit_length() - 1
    contraction = (((1,), (1,)), ((), ()))
    if count == 1 or count != 1 << depth:
        partial = lax.dot_general(
            key_proj, key_grad, contraction, preferred_element_type=jnp.float32
        ) + lax.dot_general(value_proj, value_grad, contraction, preferred_element_type=jnp.float32)
        return lax.psum_scatter(partial, "head", scatter_dimension=0, tiled=True).astype(
            jnp.bfloat16
        )
    block = key_proj.shape[0] // count
    key_split = key_proj.reshape(count // 2, 2, block, key_proj.shape[1])
    value_split = value_proj.reshape(count // 2, 2, block, value_proj.shape[1])

    def project(half):
        return jnp.einsum(
            "arf,tf->art",
            lax.dynamic_index_in_dim(key_split, half, 1, keepdims=False),
            key_grad,
            preferred_element_type=jnp.float32,
        ) + jnp.einsum(
            "arf,tf->art",
            lax.dynamic_index_in_dim(value_split, half, 1, keepdims=False),
            value_grad,
            preferred_element_type=jnp.float32,
        )

    own_bit = position % 2
    sent = project(1 - own_bit)
    kept = project(own_bit)
    current = kept + lax.ppermute(sent, "head", [(i, i ^ 1) for i in range(count)])
    for level in range(1, depth):
        current = current.reshape(-1, 2, block, current.shape[-1])
        own_bit = (position // (1 << level)) % 2
        kept = lax.dynamic_index_in_dim(current, own_bit, 1, keepdims=False)
        sent = lax.dynamic_index_in_dim(current, 1 - own_bit, 1, keepdims=False)
        arrived = lax.ppermute(
            sent.astype(jnp.bfloat16), "head", [(i, i ^ (1 << level)) for i in range(count)]
        )
        current = kept + arrived.astype(jnp.float32)
    return current.reshape(block, -1).astype(jnp.bfloat16)


def local(
    queries, key_states, value_states, out_grad, mask_flags, shard_blocks, key_proj, value_proj
):
    rows_here = queries.shape[0]
    kv_cols = key_states.shape[1]
    kv_heads = kv_cols // HD
    group_size = queries.shape[1] // kv_cols
    inv_root = HD ** (-0.5)
    position = lax.axis_index("ctx")
    query_heads = queries.reshape(rows_here, kv_heads, group_size, HD)
    grad_heads = out_grad.reshape(rows_here, kv_heads, group_size, HD)
    own_blocks = lax.dynamic_slice_in_dim(
        shard_blocks, position * (rows_here // BLK), rows_here // BLK
    )
    own_flags = select_rows(mask_flags, own_blocks)

    kv_rows, sources = gather_slots(
        jnp.concatenate([key_states, value_states], axis=1), "ctx"
    )
    row_count = kv_rows.shape[0]
    blocks_here = rows_here // BLK
    key_blocks = lax.iota(jnp.int32, row_count // BLK)
    key_doc_blocks = pick(
        shard_blocks,
        pick(sources, key_blocks // blocks_here) * blocks_here + key_blocks % blocks_here,
    )
    step_rows = math.gcd(row_count, 512)
    steps = row_count // step_rows

    def chunk(offset):
        block = lax.dynamic_slice_in_dim(kv_rows, offset, step_rows)
        key_heads = block[:, :kv_cols].reshape(step_rows, kv_heads, HD)
        value_heads = block[:, kv_cols:].reshape(step_rows, kv_heads, HD)
        their_blocks = lax.dynamic_slice_in_dim(key_doc_blocks, offset // BLK, step_rows // BLK)
        pair_flags = select_cols(own_flags, their_blocks) > 0
        allowed = jnp.repeat(jnp.repeat(pair_flags, BLK, axis=0), BLK, axis=1)
        scores = (
            jnp.einsum("qkgd,tkd->kgqt", query_heads, key_heads, preferred_element_type=jnp.float32)
            * inv_root
        )
        scores = jnp.where(allowed[None, None], scores, masked_score)
        return key_heads, value_heads, allowed, scores

    def forward_stats(offset, current):
        row_max, row_sum, weighted = current
        key_heads, value_heads, allowed, scores = chunk(offset)
        new_max = jnp.maximum(row_max, jnp.max(scores, axis=-1))
        rescale = jnp.exp(row_max - new_max)
        shifted = jnp.where(allowed[None, None], jnp.exp(scores - new_max[..., None]), 0.0)
        row_sum = row_sum * rescale + jnp.sum(shifted, axis=-1)
        weighted = weighted * rescale[..., None] + jnp.einsum(
            "kgqt,tkd->kgqd",
            shifted.astype(jnp.bfloat16),
            value_heads,
            preferred_element_type=jnp.float32,
        )
        return (new_max, row_sum, weighted)

    def backward_chunk(offset, log_total, row_delta, scores_given=None):
        key_heads, value_heads, allowed, scores = chunk(offset)
        if scores_given is not None:
            scores = scores_given
        probs = jnp.exp(scores - log_total[..., None])
        dprobs = jnp.einsum(
            "qkgd,tkd->kgqt", grad_heads, value_heads, preferred_element_type=jnp.float32
        )
        dscores = (probs * (dprobs - row_delta[..., None])).astype(jnp.bfloat16)
        probs_low = probs.astype(jnp.bfloat16)
        query_term = (
            jnp.einsum("kgqt,tkd->qkgd", dscores, key_heads, preferred_element_type=jnp.float32)
            * inv_root
        )
        key_term = (
            jnp.einsum("kgqt,qkgd->tkd", dscores, query_heads, preferred_element_type=jnp.float32)
            * inv_root
        )
        value_term = jnp.einsum(
            "kgqt,qkgd->tkd", probs_low, grad_heads, preferred_element_type=jnp.float32
        )
        kv_term = jnp.concatenate(
            [key_term.reshape(step_rows, kv_cols), value_term.reshape(step_rows, kv_cols)], axis=1
        )
        return query_term, kv_term

    start_stats = (
        jnp.full((kv_heads, group_size, rows_here), masked_score, jnp.float32),
        jnp.zeros((kv_heads, group_size, rows_here), jnp.float32),
        jnp.zeros((kv_heads, group_size, rows_here, HD), jnp.float32),
    )
    if steps == 1:
        key_heads, value_heads, allowed, scores = chunk(0)
        row_max = jnp.max(scores, axis=-1)
        shifted = jnp.exp(scores - row_max[..., None])
        row_sum = jnp.sum(shifted, axis=-1)
        weighted = jnp.einsum(
            "kgqt,tkd->kgqd",
            shifted.astype(jnp.bfloat16),
            value_heads,
            preferred_element_type=jnp.float32,
        )
    else:
        row_max, row_sum, weighted = lax.fori_loop(
            0, steps, lambda i, c: forward_stats(i * step_rows, c), start_stats
        )
        scores = None
    log_total = row_max + jnp.log(row_sum)
    attended = (weighted / row_sum[..., None]).astype(jnp.bfloat16)
    row_delta = jnp.einsum(
        "kgqd,qkgd->kgq", attended, grad_heads, preferred_element_type=jnp.float32
    )

    if steps == 1:
        query_acc, kv_acc = backward_chunk(0, log_total, row_delta, scores)
    else:

        def backward_visit(turn_index, current):
            query_now, kv_now = current
            offset = turn_index * step_rows
            query_term, kv_term = backward_chunk(offset, log_total, row_delta)
            kv_now = lax.dynamic_update_slice_in_dim(kv_now, kv_term, offset, 0)
            return (query_now + query_term, kv_now)

        query_acc, kv_acc = lax.fori_loop(
            0,
            steps,
            backward_visit,
            (
                jnp.zeros((rows_here, kv_heads, group_size, HD), jnp.float32),
                jnp.zeros((row_count, 2 * kv_cols), jnp.float32),
            ),
        )

    kv_grad = scatter_slots(kv_acc, "ctx")
    query_grad = query_acc.reshape(rows_here, -1).astype(jnp.bfloat16)
    key_grad = kv_grad[:, :kv_cols].astype(jnp.bfloat16)
    value_grad = kv_grad[:, kv_cols:].astype(jnp.bfloat16)
    input_grad_t = head_reduce(key_proj, value_proj, key_grad, value_grad)
    return (query_grad, key_grad, value_grad, input_grad_t)


def solution(mesh):
    return jax.shard_map(
        local,
        mesh=mesh,
        in_specs=(
            P(("groups", "ctx"), "head"),
            P(("groups", "ctx"), "head"),
            P(("groups", "ctx"), "head"),
            P(("groups", "ctx"), "head"),
            P("groups", None),
            P("groups"),
            P(None, "head"),
            P(None, "head"),
        ),
        out_specs=(
            P(("groups", "ctx"), "head"),
            P(("groups", "ctx"), "head"),
            P(("groups", "ctx"), "head"),
            P("head", ("groups", "ctx")),
        ),
        check_vma=False,
    )
```

```python
import math

import jax
import jax.numpy as jnp
from jax import lax
from jax.sharding import PartitionSpec as P

HD = 128
BLK = 128


masked_score = -1e30


def select_rows(lookup, picked):
    onehot = (picked[:, None] == lax.iota(jnp.int32, lookup.shape[0])[None, :]).astype(jnp.int32)
    return jnp.sum(onehot[:, :, None] * lookup[None, :, :], axis=1)


def select_cols(lookup, picked):
    onehot = (picked[:, None] == lax.iota(jnp.int32, lookup.shape[1])[None, :]).astype(jnp.int32)
    return jnp.sum(lookup[:, None, :] * onehot[None, :, :], axis=2)


def pick(vector, picked):
    onehot = (picked[:, None] == lax.iota(jnp.int32, vector.shape[0])[None, :]).astype(jnp.int32)
    return jnp.sum(onehot * vector[None, :], axis=1)


def shifted_pairs(count, steps):
    return [(source, (source + steps) % count) for source in range(count)]


def gather_slots(block, axis):
    count = lax.axis_size(axis)
    position = lax.axis_index(axis)
    if count > 8:
        gathered = lax.all_gather(block, axis, axis=0, tiled=True)
        return gathered, lax.iota(jnp.int32, count)
    pieces = [block] + [
        lax.ppermute(block, axis, shifted_pairs(count, steps)) for steps in range(1, count)
    ]
    sources = (position - lax.iota(jnp.int32, count)) % count
    return jnp.concatenate(pieces, axis=0), sources


def scatter_slots(slots, axis):
    count = lax.axis_size(axis)
    if count > 8:
        return lax.psum_scatter(slots, axis, scatter_dimension=0, tiled=True)
    rows = slots.shape[0] // count
    total = slots[:rows]
    for steps in range(1, count):
        total = total + lax.ppermute(
            slots[steps * rows : (steps + 1) * rows].astype(jnp.bfloat16),
            axis,
            shifted_pairs(count, -steps),
        ).astype(jnp.float32)
    return total


def head_reduce(key_proj, value_proj, key_grad, value_grad):
    count = lax.axis_size("head")
    position = lax.axis_index("head")
    depth = count.bit_length() - 1
    contraction = (((1,), (1,)), ((), ()))
    if count == 1 or count != 1 << depth:
        partial = lax.dot_general(
            key_proj, key_grad, contraction, preferred_element_type=jnp.float32
        ) + lax.dot_general(value_proj, value_grad, contraction, preferred_element_type=jnp.float32)
        return lax.psum_scatter(partial, "head", scatter_dimension=0, tiled=True).astype(
            jnp.bfloat16
        )
    block = key_proj.shape[0] // count
    key_split = key_proj.reshape(count // 2, 2, block, key_proj.shape[1])
    value_split = value_proj.reshape(count // 2, 2, block, value_proj.shape[1])

    def project(half):
        return jnp.einsum(
            "arf,tf->art",
            lax.dynamic_index_in_dim(key_split, half, 1, keepdims=False),
            key_grad,
            preferred_element_type=jnp.float32,
        ) + jnp.einsum(
            "arf,tf->art",
            lax.dynamic_index_in_dim(value_split, half, 1, keepdims=False),
            value_grad,
            preferred_element_type=jnp.float32,
        )

    own_bit = position % 2
    sent = project(1 - own_bit)
    kept = project(own_bit)
    current = kept + lax.ppermute(sent, "head", [(i, i ^ 1) for i in range(count)])
    for level in range(1, depth):
        current = current.reshape(-1, 2, block, current.shape[-1])
        own_bit = (position // (1 << level)) % 2
        kept = lax.dynamic_index_in_dim(current, own_bit, 1, keepdims=False)
        sent = lax.dynamic_index_in_dim(current, 1 - own_bit, 1, keepdims=False)
        arrived = lax.ppermute(
            sent.astype(jnp.bfloat16), "head", [(i, i ^ (1 << level)) for i in range(count)]
        )
        current = kept + arrived.astype(jnp.float32)
    return current.reshape(block, -1).astype(jnp.bfloat16)


def local(
    queries, key_states, value_states, out_grad, mask_flags, shard_blocks, key_proj, value_proj
):
    rows_here = queries.shape[0]
    kv_cols = key_states.shape[1]
    kv_heads = kv_cols // HD
    group_size = queries.shape[1] // kv_cols
    inv_root = HD ** (-0.5)
    position = lax.axis_index("ctx")
    query_heads = queries.reshape(rows_here, kv_heads, group_size, HD)
    grad_heads = out_grad.reshape(rows_here, kv_heads, group_size, HD)
    own_blocks = lax.dynamic_slice_in_dim(
        shard_blocks, position * (rows_here // BLK), rows_here // BLK
    )
    own_flags = select_rows(mask_flags, own_blocks)

    kv_rows, sources = gather_slots(
        jnp.concatenate([key_states, value_states], axis=1), "ctx"
    )
    row_count = kv_rows.shape[0]
    blocks_here = rows_here // BLK
    key_blocks = lax.iota(jnp.int32, row_count // BLK)
    key_doc_blocks = pick(
        shard_blocks,
        pick(sources, key_blocks // blocks_here) * blocks_here + key_blocks % blocks_here,
    )
    step_rows = math.gcd(row_count, 512)
    steps = row_count // step_rows

    def chunk(offset):
        block = lax.dynamic_slice_in_dim(kv_rows, offset, step_rows)
        key_heads = block[:, :kv_cols].reshape(step_rows, kv_heads, HD)
        value_heads = block[:, kv_cols:].reshape(step_rows, kv_heads, HD)
        their_blocks = lax.dynamic_slice_in_dim(key_doc_blocks, offset // BLK, step_rows // BLK)
        pair_flags = select_cols(own_flags, their_blocks) > 0
        allowed = jnp.repeat(jnp.repeat(pair_flags, BLK, axis=0), BLK, axis=1)
        scores = (
            jnp.einsum("qkgd,tkd->kgqt", query_heads, key_heads, preferred_element_type=jnp.float32)
            * inv_root
        )
        scores = jnp.where(allowed[None, None], scores, masked_score)
        return key_heads, value_heads, allowed, scores

    def forward_stats(offset, current):
        row_max, row_sum, weighted = current
        key_heads, value_heads, allowed, scores = chunk(offset)
        new_max = jnp.maximum(row_max, jnp.max(scores, axis=-1))
        rescale = jnp.exp(row_max - new_max)
        shifted = jnp.where(allowed[None, None], jnp.exp(scores - new_max[..., None]), 0.0)
        row_sum = row_sum * rescale + jnp.sum(shifted, axis=-1)
        weighted = weighted * rescale[..., None] + jnp.einsum(
            "kgqt,tkd->kgqd",
            shifted.astype(jnp.bfloat16),
            value_heads,
            preferred_element_type=jnp.float32,
        )
        return (new_max, row_sum, weighted)

    def backward_chunk(offset, log_total, row_delta, scores_given=None):
        key_heads, value_heads, allowed, scores = chunk(offset)
        if scores_given is not None:
            scores = scores_given
        probs = jnp.exp(scores - log_total[..., None])
        dprobs = jnp.einsum(
            "qkgd,tkd->kgqt", grad_heads, value_heads, preferred_element_type=jnp.float32
        )
        dscores = (probs * (dprobs - row_delta[..., None])).astype(jnp.bfloat16)
        probs_low = probs.astype(jnp.bfloat16)
        query_term = (
            jnp.einsum("kgqt,tkd->qkgd", dscores, key_heads, preferred_element_type=jnp.float32)
            * inv_root
        )
        key_term = (
            jnp.einsum("kgqt,qkgd->tkd", dscores, query_heads, preferred_element_type=jnp.float32)
            * inv_root
        )
        value_term = jnp.einsum(
            "kgqt,qkgd->tkd", probs_low, grad_heads, preferred_element_type=jnp.float32
        )
        kv_term = jnp.concatenate(
            [key_term.reshape(step_rows, kv_cols), value_term.reshape(step_rows, kv_cols)], axis=1
        )
        return query_term, kv_term

    start_stats = (
        jnp.full((kv_heads, group_size, rows_here), masked_score, jnp.float32),
        jnp.zeros((kv_heads, group_size, rows_here), jnp.float32),
        jnp.zeros((kv_heads, group_size, rows_here, HD), jnp.float32),
    )
    if steps == 1:
        key_heads, value_heads, allowed, scores = chunk(0)
        row_max = jnp.max(scores, axis=-1)
        shifted = jnp.exp(scores - row_max[..., None])
        row_sum = jnp.sum(shifted, axis=-1)
        weighted = jnp.einsum(
            "kgqt,tkd->kgqd",
            shifted.astype(jnp.bfloat16),
            value_heads,
            preferred_element_type=jnp.float32,
        )
    else:
        row_max, row_sum, weighted = lax.fori_loop(
            0, steps, lambda i, c: forward_stats(i * step_rows, c), start_stats
        )
        scores = None
    log_total = row_max + jnp.log(row_sum)
    attended = (weighted / row_sum[..., None]).astype(jnp.bfloat16)
    row_delta = jnp.einsum(
        "kgqd,qkgd->kgq", attended, grad_heads, preferred_element_type=jnp.float32
    )

    if steps == 1:
        query_acc, kv_acc = backward_chunk(0, log_total, row_delta, scores)
    else:

        def backward_visit(turn_index, current):
            query_now, kv_now = current
            offset = turn_index * step_rows
            query_term, kv_term = backward_chunk(offset, log_total, row_delta)
            kv_now = lax.dynamic_update_slice_in_dim(kv_now, kv_term, offset, 0)
            return (query_now + query_term, kv_now)

        query_acc, kv_acc = lax.fori_loop(
            0,
            steps,
            backward_visit,
            (
                jnp.zeros((rows_here, kv_heads, group_size, HD), jnp.float32),
                jnp.zeros((row_count, 2 * kv_cols), jnp.float32),
            ),
        )

    query_grad = query_acc.reshape(rows_here, -1).astype(jnp.bfloat16)
    slot_count = row_count // rows_here
    parts = 2 if rows_here % 16 == 0 else 1
    part_rows = rows_here // parts
    slots = kv_acc.reshape(slot_count, rows_here, 2 * kv_cols)
    key_parts, value_parts, input_parts = [], [], []
    for part in range(parts):
        sending = slots[:, part * part_rows : (part + 1) * part_rows].reshape(-1, 2 * kv_cols)
        if key_parts:
            sending, _ = lax.optimization_barrier((sending, key_parts[-1]))
        kv_grad = scatter_slots(sending, "ctx")
        key_parts.append(kv_grad[:, :kv_cols].astype(jnp.bfloat16))
        value_parts.append(kv_grad[:, kv_cols:].astype(jnp.bfloat16))
        input_parts.append(head_reduce(key_proj, value_proj, key_parts[-1], value_parts[-1]))
    key_grad = jnp.concatenate(key_parts, axis=0)
    value_grad = jnp.concatenate(value_parts, axis=0)
    input_grad_t = jnp.concatenate(input_parts, axis=1)
    return (query_grad, key_grad, value_grad, input_grad_t)


def solution(mesh):
    return jax.shard_map(
        local,
        mesh=mesh,
        in_specs=(
            P(("groups", "ctx"), "head"),
            P(("groups", "ctx"), "head"),
            P(("groups", "ctx"), "head"),
            P(("groups", "ctx"), "head"),
            P("groups", None),
            P("groups"),
            P(None, "head"),
            P(None, "head"),
        ),
        out_specs=(
            P(("groups", "ctx"), "head"),
            P(("groups", "ctx"), "head"),
            P(("groups", "ctx"), "head"),
            P("head", ("groups", "ctx")),
        ),
        check_vma=False,
    )
```

```python
import math

import jax
import jax.numpy as jnp
from jax import lax
from jax.experimental import pallas as pl
from jax.sharding import PartitionSpec as P

HD = 128
BLK = 128


masked_score = -1e30


def select_rows(lookup, picked):
    onehot = (picked[:, None] == lax.iota(jnp.int32, lookup.shape[0])[None, :]).astype(jnp.int32)
    return jnp.sum(onehot[:, :, None] * lookup[None, :, :], axis=1)


def select_cols(lookup, picked):
    onehot = (picked[:, None] == lax.iota(jnp.int32, lookup.shape[1])[None, :]).astype(jnp.int32)
    return jnp.sum(lookup[:, None, :] * onehot[None, :, :], axis=2)


def pick(vector, picked):
    onehot = (picked[:, None] == lax.iota(jnp.int32, vector.shape[0])[None, :]).astype(jnp.int32)
    return jnp.sum(onehot * vector[None, :], axis=1)


def shifted_pairs(count, steps):
    return [(source, (source + steps) % count) for source in range(count)]


def gather_slots(block, axis):
    count = lax.axis_size(axis)
    position = lax.axis_index(axis)
    if count > 8:
        gathered = lax.all_gather(block, axis, axis=0, tiled=True)
        return gathered, lax.iota(jnp.int32, count)
    pieces = [block] + [
        lax.ppermute(block, axis, shifted_pairs(count, steps)) for steps in range(1, count)
    ]
    sources = (position - lax.iota(jnp.int32, count)) % count
    return jnp.concatenate(pieces, axis=0), sources


def scatter_slots(slots, axis):
    count = lax.axis_size(axis)
    if count > 8:
        return lax.psum_scatter(slots, axis, scatter_dimension=0, tiled=True)
    rows = slots.shape[0] // count
    total = slots[:rows]
    for steps in range(1, count):
        total = total + lax.ppermute(
            slots[steps * rows : (steps + 1) * rows].astype(jnp.bfloat16),
            axis,
            shifted_pairs(count, -steps),
        ).astype(jnp.float32)
    return total


def head_reduce(key_proj, value_proj, key_grad, value_grad):
    count = lax.axis_size("head")
    position = lax.axis_index("head")
    depth = count.bit_length() - 1
    contraction = (((1,), (1,)), ((), ()))
    if count == 1 or count != 1 << depth:
        partial = lax.dot_general(
            key_proj, key_grad, contraction, preferred_element_type=jnp.float32
        ) + lax.dot_general(value_proj, value_grad, contraction, preferred_element_type=jnp.float32)
        return lax.psum_scatter(partial, "head", scatter_dimension=0, tiled=True).astype(
            jnp.bfloat16
        )
    block = key_proj.shape[0] // count
    key_split = key_proj.reshape(count // 2, 2, block, key_proj.shape[1])
    value_split = value_proj.reshape(count // 2, 2, block, value_proj.shape[1])

    def project(half):
        return jnp.einsum(
            "arf,tf->art",
            lax.dynamic_index_in_dim(key_split, half, 1, keepdims=False),
            key_grad,
            preferred_element_type=jnp.float32,
        ) + jnp.einsum(
            "arf,tf->art",
            lax.dynamic_index_in_dim(value_split, half, 1, keepdims=False),
            value_grad,
            preferred_element_type=jnp.float32,
        )

    own_bit = position % 2
    sent = project(1 - own_bit)
    kept = project(own_bit)
    current = kept + lax.ppermute(sent, "head", [(i, i ^ 1) for i in range(count)])
    for level in range(1, depth):
        current = current.reshape(-1, 2, block, current.shape[-1])
        own_bit = (position // (1 << level)) % 2
        kept = lax.dynamic_index_in_dim(current, own_bit, 1, keepdims=False)
        sent = lax.dynamic_index_in_dim(current, 1 - own_bit, 1, keepdims=False)
        arrived = lax.ppermute(
            sent.astype(jnp.bfloat16), "head", [(i, i ^ (1 << level)) for i in range(count)]
        )
        current = kept + arrived.astype(jnp.float32)
    return current.reshape(block, -1).astype(jnp.bfloat16)


def attention_kernel(query_ref, grad_ref, kv_ref, mask_ref, query_out, kv_out):
    inv_root = HD ** (-0.5)
    kv_cols = kv_ref.shape[1] // 2
    kv_heads = kv_cols // HD
    group_size = query_ref.shape[1] // kv_cols
    allowed = mask_ref[...] > 0
    across = (((1,), (1,)), ((), ()))
    for kv_head in range(kv_heads):
        key_head = kv_ref[:, kv_head * HD : (kv_head + 1) * HD]
        value_head = kv_ref[:, kv_cols + kv_head * HD : kv_cols + (kv_head + 1) * HD]
        key_sum = jnp.zeros(key_head.shape, jnp.float32)
        value_sum = jnp.zeros(value_head.shape, jnp.float32)
        for member in range(group_size):
            first = (kv_head * group_size + member) * HD
            query_head = query_ref[:, first : first + HD]
            grad_head = grad_ref[:, first : first + HD]
            scores = (
                lax.dot_general(query_head, key_head, across, preferred_element_type=jnp.float32)
                * inv_root
            )
            scores = jnp.where(allowed, scores, masked_score)
            row_max = jnp.max(scores, axis=1, keepdims=True)
            shifted = jnp.exp(scores - row_max)
            row_sum = jnp.sum(shifted, axis=1, keepdims=True)
            weighted = jnp.dot(
                shifted.astype(jnp.bfloat16), value_head, preferred_element_type=jnp.float32
            )
            attended = (weighted / row_sum).astype(jnp.bfloat16)
            probs = jnp.exp(scores - (row_max + jnp.log(row_sum)))
            row_delta = jnp.sum(
                grad_head.astype(jnp.float32) * attended.astype(jnp.float32), axis=1, keepdims=True
            )
            dprobs = lax.dot_general(
                grad_head, value_head, across, preferred_element_type=jnp.float32
            )
            dscores = probs * (dprobs - row_delta)
            query_term = (
                jnp.dot(dscores.astype(jnp.bfloat16), key_head, preferred_element_type=jnp.float32)
                * inv_root
            )
            query_out[:, first : first + HD] = query_term.astype(jnp.bfloat16)
            key_sum = key_sum + jnp.dot(
                dscores.T.astype(jnp.bfloat16), query_head, preferred_element_type=jnp.float32
            )
            value_sum = value_sum + jnp.dot(
                probs.T.astype(jnp.bfloat16), grad_head, preferred_element_type=jnp.float32
            )
        kv_out[:, kv_head * HD : (kv_head + 1) * HD] = key_sum * inv_root
        kv_out[:, kv_cols + kv_head * HD : kv_cols + (kv_head + 1) * HD] = value_sum


def attention_block(queries, out_grad, kv_rows, allowed, interpret=False):
    return pl.pallas_call(
        attention_kernel,
        out_shape=(
            jax.ShapeDtypeStruct(queries.shape, jnp.bfloat16),
            jax.ShapeDtypeStruct(kv_rows.shape, jnp.float32),
        ),
        interpret=interpret,
    )(queries, out_grad, kv_rows, allowed.astype(jnp.int32))


def local(
    queries, key_states, value_states, out_grad, mask_flags, shard_blocks, key_proj, value_proj
):
    rows_here = queries.shape[0]
    kv_cols = key_states.shape[1]
    kv_heads = kv_cols // HD
    group_size = queries.shape[1] // kv_cols
    inv_root = HD ** (-0.5)
    position = lax.axis_index("ctx")
    query_heads = queries.reshape(rows_here, kv_heads, group_size, HD)
    grad_heads = out_grad.reshape(rows_here, kv_heads, group_size, HD)
    own_blocks = lax.dynamic_slice_in_dim(
        shard_blocks, position * (rows_here // BLK), rows_here // BLK
    )
    own_flags = select_rows(mask_flags, own_blocks)

    kv_rows, sources = gather_slots(
        jnp.concatenate([key_states, value_states], axis=1), "ctx"
    )
    row_count = kv_rows.shape[0]
    blocks_here = rows_here // BLK
    key_blocks = lax.iota(jnp.int32, row_count // BLK)
    key_doc_blocks = pick(
        shard_blocks,
        pick(sources, key_blocks // blocks_here) * blocks_here + key_blocks % blocks_here,
    )
    step_rows = math.gcd(row_count, 512)
    steps = row_count // step_rows

    def chunk(offset):
        block = lax.dynamic_slice_in_dim(kv_rows, offset, step_rows)
        key_heads = block[:, :kv_cols].reshape(step_rows, kv_heads, HD)
        value_heads = block[:, kv_cols:].reshape(step_rows, kv_heads, HD)
        their_blocks = lax.dynamic_slice_in_dim(key_doc_blocks, offset // BLK, step_rows // BLK)
        pair_flags = select_cols(own_flags, their_blocks) > 0
        allowed = jnp.repeat(jnp.repeat(pair_flags, BLK, axis=0), BLK, axis=1)
        scores = (
            jnp.einsum("qkgd,tkd->kgqt", query_heads, key_heads, preferred_element_type=jnp.float32)
            * inv_root
        )
        scores = jnp.where(allowed[None, None], scores, masked_score)
        return key_heads, value_heads, allowed, scores

    def forward_stats(offset, current):
        row_max, row_sum, weighted = current
        key_heads, value_heads, allowed, scores = chunk(offset)
        new_max = jnp.maximum(row_max, jnp.max(scores, axis=-1))
        rescale = jnp.exp(row_max - new_max)
        shifted = jnp.where(allowed[None, None], jnp.exp(scores - new_max[..., None]), 0.0)
        row_sum = row_sum * rescale + jnp.sum(shifted, axis=-1)
        weighted = weighted * rescale[..., None] + jnp.einsum(
            "kgqt,tkd->kgqd",
            shifted.astype(jnp.bfloat16),
            value_heads,
            preferred_element_type=jnp.float32,
        )
        return (new_max, row_sum, weighted)

    def backward_chunk(offset, log_total, row_delta, scores_given=None):
        key_heads, value_heads, allowed, scores = chunk(offset)
        if scores_given is not None:
            scores = scores_given
        probs = jnp.exp(scores - log_total[..., None])
        dprobs = jnp.einsum(
            "qkgd,tkd->kgqt", grad_heads, value_heads, preferred_element_type=jnp.float32
        )
        dscores = (probs * (dprobs - row_delta[..., None])).astype(jnp.bfloat16)
        probs_low = probs.astype(jnp.bfloat16)
        query_term = (
            jnp.einsum("kgqt,tkd->qkgd", dscores, key_heads, preferred_element_type=jnp.float32)
            * inv_root
        )
        key_term = (
            jnp.einsum("kgqt,qkgd->tkd", dscores, query_heads, preferred_element_type=jnp.float32)
            * inv_root
        )
        value_term = jnp.einsum(
            "kgqt,qkgd->tkd", probs_low, grad_heads, preferred_element_type=jnp.float32
        )
        kv_term = jnp.concatenate(
            [key_term.reshape(step_rows, kv_cols), value_term.reshape(step_rows, kv_cols)], axis=1
        )
        return query_term, kv_term

    if steps == 1:
        allowed = chunk(0)[2]
        query_grad, kv_acc = attention_block(queries, out_grad, kv_rows, allowed)
    else:
        start_stats = (
            jnp.full((kv_heads, group_size, rows_here), masked_score, jnp.float32),
            jnp.zeros((kv_heads, group_size, rows_here), jnp.float32),
            jnp.zeros((kv_heads, group_size, rows_here, HD), jnp.float32),
        )
        row_max, row_sum, weighted = lax.fori_loop(
            0, steps, lambda i, c: forward_stats(i * step_rows, c), start_stats
        )
        log_total = row_max + jnp.log(row_sum)
        attended = (weighted / row_sum[..., None]).astype(jnp.bfloat16)
        row_delta = jnp.einsum(
            "kgqd,qkgd->kgq", attended, grad_heads, preferred_element_type=jnp.float32
        )

        def backward_visit(turn_index, current):
            query_now, kv_now = current
            offset = turn_index * step_rows
            query_term, kv_term = backward_chunk(offset, log_total, row_delta)
            kv_now = lax.dynamic_update_slice_in_dim(kv_now, kv_term, offset, 0)
            return (query_now + query_term, kv_now)

        query_acc, kv_acc = lax.fori_loop(
            0,
            steps,
            backward_visit,
            (
                jnp.zeros((rows_here, kv_heads, group_size, HD), jnp.float32),
                jnp.zeros((row_count, 2 * kv_cols), jnp.float32),
            ),
        )
        query_grad = query_acc.reshape(rows_here, -1).astype(jnp.bfloat16)

    kv_grad = scatter_slots(kv_acc, "ctx")
    key_grad = kv_grad[:, :kv_cols].astype(jnp.bfloat16)
    value_grad = kv_grad[:, kv_cols:].astype(jnp.bfloat16)
    input_grad_t = head_reduce(key_proj, value_proj, key_grad, value_grad)
    return (query_grad, key_grad, value_grad, input_grad_t)


def solution(mesh):
    return jax.shard_map(
        local,
        mesh=mesh,
        in_specs=(
            P(("groups", "ctx"), "head"),
            P(("groups", "ctx"), "head"),
            P(("groups", "ctx"), "head"),
            P(("groups", "ctx"), "head"),
            P("groups", None),
            P("groups"),
            P(None, "head"),
            P(None, "head"),
        ),
        out_specs=(
            P(("groups", "ctx"), "head"),
            P(("groups", "ctx"), "head"),
            P(("groups", "ctx"), "head"),
            P("head", ("groups", "ctx")),
        ),
        check_vma=False,
    )
```

```python
import math

import jax
import jax.numpy as jnp
from jax import lax
from jax.experimental import pallas as pl
from jax.sharding import PartitionSpec as P

HD = 128
BLK = 128


masked_score = -1e30


def select_rows(lookup, picked):
    onehot = (picked[:, None] == lax.iota(jnp.int32, lookup.shape[0])[None, :]).astype(jnp.int32)
    return jnp.sum(onehot[:, :, None] * lookup[None, :, :], axis=1)


def select_cols(lookup, picked):
    onehot = (picked[:, None] == lax.iota(jnp.int32, lookup.shape[1])[None, :]).astype(jnp.int32)
    return jnp.sum(lookup[:, None, :] * onehot[None, :, :], axis=2)


def pick(vector, picked):
    onehot = (picked[:, None] == lax.iota(jnp.int32, vector.shape[0])[None, :]).astype(jnp.int32)
    return jnp.sum(onehot * vector[None, :], axis=1)


def shifted_pairs(count, steps):
    return [(source, (source + steps) % count) for source in range(count)]


def gather_slots(block, axis):
    count = lax.axis_size(axis)
    position = lax.axis_index(axis)
    if count > 8:
        gathered = lax.all_gather(block, axis, axis=0, tiled=True)
        return gathered, lax.iota(jnp.int32, count)
    pieces = [block] + [
        lax.ppermute(block, axis, shifted_pairs(count, steps)) for steps in range(1, count)
    ]
    sources = (position - lax.iota(jnp.int32, count)) % count
    return jnp.concatenate(pieces, axis=0), sources


def scatter_slots(slots, axis):
    count = lax.axis_size(axis)
    if count > 8:
        return lax.psum_scatter(slots, axis, scatter_dimension=0, tiled=True)
    rows = slots.shape[0] // count
    total = slots[:rows]
    for steps in range(1, count):
        total = total + lax.ppermute(
            slots[steps * rows : (steps + 1) * rows].astype(jnp.bfloat16),
            axis,
            shifted_pairs(count, -steps),
        ).astype(jnp.float32)
    return total


def head_reduce(key_proj, value_proj, key_grad, value_grad):
    count = lax.axis_size("head")
    position = lax.axis_index("head")
    depth = count.bit_length() - 1
    contraction = (((1,), (1,)), ((), ()))
    if count == 1 or count != 1 << depth:
        partial = lax.dot_general(
            key_proj, key_grad, contraction, preferred_element_type=jnp.float32
        ) + lax.dot_general(value_proj, value_grad, contraction, preferred_element_type=jnp.float32)
        return lax.psum_scatter(partial, "head", scatter_dimension=0, tiled=True).astype(
            jnp.bfloat16
        )
    block = key_proj.shape[0] // count
    key_split = key_proj.reshape(count // 2, 2, block, key_proj.shape[1])
    value_split = value_proj.reshape(count // 2, 2, block, value_proj.shape[1])

    def project(half):
        return jnp.einsum(
            "arf,tf->art",
            lax.dynamic_index_in_dim(key_split, half, 1, keepdims=False),
            key_grad,
            preferred_element_type=jnp.float32,
        ) + jnp.einsum(
            "arf,tf->art",
            lax.dynamic_index_in_dim(value_split, half, 1, keepdims=False),
            value_grad,
            preferred_element_type=jnp.float32,
        )

    own_bit = position % 2
    sent = project(1 - own_bit)
    kept = project(own_bit)
    current = kept + lax.ppermute(sent, "head", [(i, i ^ 1) for i in range(count)])
    for level in range(1, depth):
        current = current.reshape(-1, 2, block, current.shape[-1])
        own_bit = (position // (1 << level)) % 2
        kept = lax.dynamic_index_in_dim(current, own_bit, 1, keepdims=False)
        sent = lax.dynamic_index_in_dim(current, 1 - own_bit, 1, keepdims=False)
        arrived = lax.ppermute(
            sent.astype(jnp.bfloat16), "head", [(i, i ^ (1 << level)) for i in range(count)]
        )
        current = kept + arrived.astype(jnp.float32)
    return current.reshape(block, -1).astype(jnp.bfloat16)


def attention_kernel(query_ref, grad_ref, kv_ref, mask_ref, query_out, kv_out):
    inv_root = HD ** (-0.5)
    kv_cols = kv_ref.shape[1] // 2
    kv_heads = kv_cols // HD
    group_size = query_ref.shape[1] // kv_cols
    allowed = mask_ref[...] > 0
    across = (((1,), (1,)), ((), ()))
    down = (((0,), (0,)), ((), ()))
    for kv_head in range(kv_heads):
        key_head = kv_ref[:, kv_head * HD : (kv_head + 1) * HD]
        value_head = kv_ref[:, kv_cols + kv_head * HD : kv_cols + (kv_head + 1) * HD]
        key_sum = jnp.zeros(key_head.shape, jnp.float32)
        value_sum = jnp.zeros(value_head.shape, jnp.float32)
        for member in range(group_size):
            first = (kv_head * group_size + member) * HD
            query_head = query_ref[:, first : first + HD]
            grad_head = grad_ref[:, first : first + HD]
            scores = (
                lax.dot_general(query_head, key_head, across, preferred_element_type=jnp.float32)
                * inv_root
            )
            scores = jnp.where(allowed, scores, masked_score)
            row_max = jnp.max(scores, axis=1, keepdims=True)
            shifted = jnp.exp(scores - row_max)
            row_sum = jnp.sum(shifted, axis=1, keepdims=True)
            weighted = jnp.dot(
                shifted.astype(jnp.bfloat16), value_head, preferred_element_type=jnp.float32
            )
            attended = (weighted / row_sum).astype(jnp.bfloat16)
            probs = shifted * (1.0 / row_sum)
            row_delta = jnp.sum(
                grad_head.astype(jnp.float32) * attended.astype(jnp.float32), axis=1, keepdims=True
            )
            dprobs = lax.dot_general(
                grad_head, value_head, across, preferred_element_type=jnp.float32
            )
            dscores = probs * (dprobs - row_delta)
            query_term = (
                jnp.dot(dscores.astype(jnp.bfloat16), key_head, preferred_element_type=jnp.float32)
                * inv_root
            )
            query_out[:, first : first + HD] = query_term.astype(jnp.bfloat16)
            key_sum = key_sum + lax.dot_general(
                dscores.astype(jnp.bfloat16), query_head, down, preferred_element_type=jnp.float32
            )
            value_sum = value_sum + lax.dot_general(
                probs.astype(jnp.bfloat16), grad_head, down, preferred_element_type=jnp.float32
            )
        kv_out[:, kv_head * HD : (kv_head + 1) * HD] = key_sum * inv_root
        kv_out[:, kv_cols + kv_head * HD : kv_cols + (kv_head + 1) * HD] = value_sum


def attention_block(queries, out_grad, kv_rows, allowed, interpret=False):
    return pl.pallas_call(
        attention_kernel,
        out_shape=(
            jax.ShapeDtypeStruct(queries.shape, jnp.bfloat16),
            jax.ShapeDtypeStruct(kv_rows.shape, jnp.float32),
        ),
        interpret=interpret,
    )(queries, out_grad, kv_rows, allowed.astype(jnp.int32))


def local(
    queries, key_states, value_states, out_grad, mask_flags, shard_blocks, key_proj, value_proj
):
    rows_here = queries.shape[0]
    kv_cols = key_states.shape[1]
    kv_heads = kv_cols // HD
    group_size = queries.shape[1] // kv_cols
    inv_root = HD ** (-0.5)
    position = lax.axis_index("ctx")
    query_heads = queries.reshape(rows_here, kv_heads, group_size, HD)
    grad_heads = out_grad.reshape(rows_here, kv_heads, group_size, HD)
    own_blocks = lax.dynamic_slice_in_dim(
        shard_blocks, position * (rows_here // BLK), rows_here // BLK
    )
    own_flags = select_rows(mask_flags, own_blocks)

    kv_rows, sources = gather_slots(
        jnp.concatenate([key_states, value_states], axis=1), "ctx"
    )
    row_count = kv_rows.shape[0]
    blocks_here = rows_here // BLK
    key_blocks = lax.iota(jnp.int32, row_count // BLK)
    key_doc_blocks = pick(
        shard_blocks,
        pick(sources, key_blocks // blocks_here) * blocks_here + key_blocks % blocks_here,
    )
    step_rows = math.gcd(row_count, 512)
    steps = row_count // step_rows

    def chunk(offset):
        block = lax.dynamic_slice_in_dim(kv_rows, offset, step_rows)
        key_heads = block[:, :kv_cols].reshape(step_rows, kv_heads, HD)
        value_heads = block[:, kv_cols:].reshape(step_rows, kv_heads, HD)
        their_blocks = lax.dynamic_slice_in_dim(key_doc_blocks, offset // BLK, step_rows // BLK)
        pair_flags = select_cols(own_flags, their_blocks) > 0
        allowed = jnp.repeat(jnp.repeat(pair_flags, BLK, axis=0), BLK, axis=1)
        scores = (
            jnp.einsum("qkgd,tkd->kgqt", query_heads, key_heads, preferred_element_type=jnp.float32)
            * inv_root
        )
        scores = jnp.where(allowed[None, None], scores, masked_score)
        return key_heads, value_heads, allowed, scores

    def forward_stats(offset, current):
        row_max, row_sum, weighted = current
        key_heads, value_heads, allowed, scores = chunk(offset)
        new_max = jnp.maximum(row_max, jnp.max(scores, axis=-1))
        rescale = jnp.exp(row_max - new_max)
        shifted = jnp.where(allowed[None, None], jnp.exp(scores - new_max[..., None]), 0.0)
        row_sum = row_sum * rescale + jnp.sum(shifted, axis=-1)
        weighted = weighted * rescale[..., None] + jnp.einsum(
            "kgqt,tkd->kgqd",
            shifted.astype(jnp.bfloat16),
            value_heads,
            preferred_element_type=jnp.float32,
        )
        return (new_max, row_sum, weighted)

    def backward_chunk(offset, log_total, row_delta, scores_given=None):
        key_heads, value_heads, allowed, scores = chunk(offset)
        if scores_given is not None:
            scores = scores_given
        probs = jnp.exp(scores - log_total[..., None])
        dprobs = jnp.einsum(
            "qkgd,tkd->kgqt", grad_heads, value_heads, preferred_element_type=jnp.float32
        )
        dscores = (probs * (dprobs - row_delta[..., None])).astype(jnp.bfloat16)
        probs_low = probs.astype(jnp.bfloat16)
        query_term = (
            jnp.einsum("kgqt,tkd->qkgd", dscores, key_heads, preferred_element_type=jnp.float32)
            * inv_root
        )
        key_term = (
            jnp.einsum("kgqt,qkgd->tkd", dscores, query_heads, preferred_element_type=jnp.float32)
            * inv_root
        )
        value_term = jnp.einsum(
            "kgqt,qkgd->tkd", probs_low, grad_heads, preferred_element_type=jnp.float32
        )
        kv_term = jnp.concatenate(
            [key_term.reshape(step_rows, kv_cols), value_term.reshape(step_rows, kv_cols)], axis=1
        )
        return query_term, kv_term

    if steps == 1:
        allowed = chunk(0)[2]
        query_grad, kv_acc = attention_block(queries, out_grad, kv_rows, allowed)
    else:
        start_stats = (
            jnp.full((kv_heads, group_size, rows_here), masked_score, jnp.float32),
            jnp.zeros((kv_heads, group_size, rows_here), jnp.float32),
            jnp.zeros((kv_heads, group_size, rows_here, HD), jnp.float32),
        )
        row_max, row_sum, weighted = lax.fori_loop(
            0, steps, lambda i, c: forward_stats(i * step_rows, c), start_stats
        )
        log_total = row_max + jnp.log(row_sum)
        attended = (weighted / row_sum[..., None]).astype(jnp.bfloat16)
        row_delta = jnp.einsum(
            "kgqd,qkgd->kgq", attended, grad_heads, preferred_element_type=jnp.float32
        )

        def backward_visit(turn_index, current):
            query_now, kv_now = current
            offset = turn_index * step_rows
            query_term, kv_term = backward_chunk(offset, log_total, row_delta)
            kv_now = lax.dynamic_update_slice_in_dim(kv_now, kv_term, offset, 0)
            return (query_now + query_term, kv_now)

        query_acc, kv_acc = lax.fori_loop(
            0,
            steps,
            backward_visit,
            (
                jnp.zeros((rows_here, kv_heads, group_size, HD), jnp.float32),
                jnp.zeros((row_count, 2 * kv_cols), jnp.float32),
            ),
        )
        query_grad = query_acc.reshape(rows_here, -1).astype(jnp.bfloat16)

    kv_grad = scatter_slots(kv_acc, "ctx")
    key_grad = kv_grad[:, :kv_cols].astype(jnp.bfloat16)
    value_grad = kv_grad[:, kv_cols:].astype(jnp.bfloat16)
    input_grad_t = head_reduce(key_proj, value_proj, key_grad, value_grad)
    return (query_grad, key_grad, value_grad, input_grad_t)


def solution(mesh):
    return jax.shard_map(
        local,
        mesh=mesh,
        in_specs=(
            P(("groups", "ctx"), "head"),
            P(("groups", "ctx"), "head"),
            P(("groups", "ctx"), "head"),
            P(("groups", "ctx"), "head"),
            P("groups", None),
            P("groups"),
            P(None, "head"),
            P(None, "head"),
        ),
        out_specs=(
            P(("groups", "ctx"), "head"),
            P(("groups", "ctx"), "head"),
            P(("groups", "ctx"), "head"),
            P("head", ("groups", "ctx")),
        ),
        check_vma=False,
    )
```

```python
import math

import jax
import jax.numpy as jnp
from jax import lax
from jax.experimental import pallas as pl
from jax.experimental.pallas import tpu as pltpu
from jax.sharding import PartitionSpec as P

HD = 128
BLK = 128


masked_score = -1e30


def select_rows(lookup, picked):
    onehot = (picked[:, None] == lax.iota(jnp.int32, lookup.shape[0])[None, :]).astype(jnp.int32)
    return jnp.sum(onehot[:, :, None] * lookup[None, :, :], axis=1)


def select_cols(lookup, picked):
    onehot = (picked[:, None] == lax.iota(jnp.int32, lookup.shape[1])[None, :]).astype(jnp.int32)
    return jnp.sum(lookup[:, None, :] * onehot[None, :, :], axis=2)


def pick(vector, picked):
    onehot = (picked[:, None] == lax.iota(jnp.int32, vector.shape[0])[None, :]).astype(jnp.int32)
    return jnp.sum(onehot * vector[None, :], axis=1)


def shifted_pairs(count, steps):
    return [(source, (source + steps) % count) for source in range(count)]


def gather_slots(block, axis):
    count = lax.axis_size(axis)
    position = lax.axis_index(axis)
    if count > 8:
        gathered = lax.all_gather(block, axis, axis=0, tiled=True)
        return gathered, lax.iota(jnp.int32, count)
    pieces = [block] + [
        lax.ppermute(block, axis, shifted_pairs(count, steps)) for steps in range(1, count)
    ]
    sources = (position - lax.iota(jnp.int32, count)) % count
    return jnp.concatenate(pieces, axis=0), sources


def scatter_slots(slots, axis):
    count = lax.axis_size(axis)
    if count > 8:
        return lax.psum_scatter(slots, axis, scatter_dimension=0, tiled=True)
    rows = slots.shape[0] // count
    total = slots[:rows]
    for steps in range(1, count):
        total = total + lax.ppermute(
            slots[steps * rows : (steps + 1) * rows].astype(jnp.bfloat16),
            axis,
            shifted_pairs(count, -steps),
        ).astype(jnp.float32)
    return total


def projection_kernel(order_ref, key_ref, value_ref, key_grad_ref, value_grad_ref, out_ref):
    across = (((1,), (1,)), ((), ()))
    out_ref[...] = lax.dot_general(
        key_ref[...], key_grad_ref[...], across, preferred_element_type=jnp.float32
    ) + lax.dot_general(
        value_ref[...], value_grad_ref[...], across, preferred_element_type=jnp.float32
    )


def project_rows(key_proj, value_proj, key_grad, value_grad, blocks, block_rows):
    sub = math.gcd(block_rows, 1024)
    per = block_rows // sub
    features = key_proj.shape[1]
    tokens = key_grad.shape[0]

    def weight_rows(i, j, order):
        return (order[i] * per + j, 0)

    def whole(i, j, order):
        return (0, 0)

    grid_spec = pltpu.PrefetchScalarGridSpec(
        num_scalar_prefetch=1,
        grid=(blocks.shape[0], per),
        in_specs=[
            pl.BlockSpec((sub, features), weight_rows),
            pl.BlockSpec((sub, features), weight_rows),
            pl.BlockSpec((tokens, features), whole),
            pl.BlockSpec((tokens, features), whole),
        ],
        out_specs=pl.BlockSpec((sub, tokens), lambda i, j, order: (i * per + j, 0)),
    )
    return pl.pallas_call(
        projection_kernel,
        grid_spec=grid_spec,
        out_shape=jax.ShapeDtypeStruct((blocks.shape[0] * block_rows, tokens), jnp.float32),
    )(blocks, key_proj, value_proj, key_grad, value_grad)


def head_reduce(key_proj, value_proj, key_grad, value_grad):
    count = lax.axis_size("head")
    position = lax.axis_index("head")
    depth = count.bit_length() - 1
    contraction = (((1,), (1,)), ((), ()))
    if count == 1 or count != 1 << depth:
        partial = lax.dot_general(
            key_proj, key_grad, contraction, preferred_element_type=jnp.float32
        ) + lax.dot_general(value_proj, value_grad, contraction, preferred_element_type=jnp.float32)
        return lax.psum_scatter(partial, "head", scatter_dimension=0, tiled=True).astype(
            jnp.bfloat16
        )
    block = key_proj.shape[0] // count
    upper = lax.iota(jnp.int32, count // 2) * 2

    def project(half):
        return project_rows(key_proj, value_proj, key_grad, value_grad, upper + half, block).reshape(
            count // 2, block, -1
        )

    own_bit = position % 2
    sent = project(1 - own_bit)
    kept = project(own_bit)
    current = kept + lax.ppermute(sent, "head", [(i, i ^ 1) for i in range(count)])
    for level in range(1, depth):
        current = current.reshape(-1, 2, block, current.shape[-1])
        own_bit = (position // (1 << level)) % 2
        kept = lax.dynamic_index_in_dim(current, own_bit, 1, keepdims=False)
        sent = lax.dynamic_index_in_dim(current, 1 - own_bit, 1, keepdims=False)
        arrived = lax.ppermute(
            sent.astype(jnp.bfloat16), "head", [(i, i ^ (1 << level)) for i in range(count)]
        )
        current = kept + arrived.astype(jnp.float32)
    return current.reshape(block, -1).astype(jnp.bfloat16)


def attention_kernel(query_ref, grad_ref, kv_ref, mask_ref, query_out, kv_out):
    inv_root = HD ** (-0.5)
    kv_cols = kv_ref.shape[1] // 2
    kv_heads = kv_cols // HD
    group_size = query_ref.shape[1] // kv_cols
    allowed = mask_ref[...] > 0
    across = (((1,), (1,)), ((), ()))
    down = (((0,), (0,)), ((), ()))
    for kv_head in range(kv_heads):
        key_head = kv_ref[:, kv_head * HD : (kv_head + 1) * HD]
        value_head = kv_ref[:, kv_cols + kv_head * HD : kv_cols + (kv_head + 1) * HD]
        key_sum = jnp.zeros(key_head.shape, jnp.float32)
        value_sum = jnp.zeros(value_head.shape, jnp.float32)
        for member in range(group_size):
            first = (kv_head * group_size + member) * HD
            query_head = query_ref[:, first : first + HD]
            grad_head = grad_ref[:, first : first + HD]
            scores = (
                lax.dot_general(query_head, key_head, across, preferred_element_type=jnp.float32)
                * inv_root
            )
            scores = jnp.where(allowed, scores, masked_score)
            row_max = jnp.max(scores, axis=1, keepdims=True)
            shifted = jnp.exp(scores - row_max)
            row_sum = jnp.sum(shifted, axis=1, keepdims=True)
            weighted = jnp.dot(
                shifted.astype(jnp.bfloat16), value_head, preferred_element_type=jnp.float32
            )
            attended = (weighted / row_sum).astype(jnp.bfloat16)
            probs = shifted * (1.0 / row_sum)
            row_delta = jnp.sum(
                grad_head.astype(jnp.float32) * attended.astype(jnp.float32), axis=1, keepdims=True
            )
            dprobs = lax.dot_general(
                grad_head, value_head, across, preferred_element_type=jnp.float32
            )
            dscores = probs * (dprobs - row_delta)
            query_term = (
                jnp.dot(dscores.astype(jnp.bfloat16), key_head, preferred_element_type=jnp.float32)
                * inv_root
            )
            query_out[:, first : first + HD] = query_term.astype(jnp.bfloat16)
            key_sum = key_sum + lax.dot_general(
                dscores.astype(jnp.bfloat16), query_head, down, preferred_element_type=jnp.float32
            )
            value_sum = value_sum + lax.dot_general(
                probs.astype(jnp.bfloat16), grad_head, down, preferred_element_type=jnp.float32
            )
        kv_out[:, kv_head * HD : (kv_head + 1) * HD] = key_sum * inv_root
        kv_out[:, kv_cols + kv_head * HD : kv_cols + (kv_head + 1) * HD] = value_sum


def attention_block(queries, out_grad, kv_rows, allowed, interpret=False):
    return pl.pallas_call(
        attention_kernel,
        out_shape=(
            jax.ShapeDtypeStruct(queries.shape, jnp.bfloat16),
            jax.ShapeDtypeStruct(kv_rows.shape, jnp.float32),
        ),
        interpret=interpret,
    )(queries, out_grad, kv_rows, allowed.astype(jnp.int32))


def local(
    queries, key_states, value_states, out_grad, mask_flags, shard_blocks, key_proj, value_proj
):
    rows_here = queries.shape[0]
    kv_cols = key_states.shape[1]
    kv_heads = kv_cols // HD
    group_size = queries.shape[1] // kv_cols
    inv_root = HD ** (-0.5)
    position = lax.axis_index("ctx")
    query_heads = queries.reshape(rows_here, kv_heads, group_size, HD)
    grad_heads = out_grad.reshape(rows_here, kv_heads, group_size, HD)
    own_blocks = lax.dynamic_slice_in_dim(
        shard_blocks, position * (rows_here // BLK), rows_here // BLK
    )
    own_flags = select_rows(mask_flags, own_blocks)

    kv_rows, sources = gather_slots(
        jnp.concatenate([key_states, value_states], axis=1), "ctx"
    )
    row_count = kv_rows.shape[0]
    blocks_here = rows_here // BLK
    key_blocks = lax.iota(jnp.int32, row_count // BLK)
    key_doc_blocks = pick(
        shard_blocks,
        pick(sources, key_blocks // blocks_here) * blocks_here + key_blocks % blocks_here,
    )
    step_rows = math.gcd(row_count, 512)
    steps = row_count // step_rows

    def chunk(offset):
        block = lax.dynamic_slice_in_dim(kv_rows, offset, step_rows)
        key_heads = block[:, :kv_cols].reshape(step_rows, kv_heads, HD)
        value_heads = block[:, kv_cols:].reshape(step_rows, kv_heads, HD)
        their_blocks = lax.dynamic_slice_in_dim(key_doc_blocks, offset // BLK, step_rows // BLK)
        pair_flags = select_cols(own_flags, their_blocks) > 0
        allowed = jnp.repeat(jnp.repeat(pair_flags, BLK, axis=0), BLK, axis=1)
        scores = (
            jnp.einsum("qkgd,tkd->kgqt", query_heads, key_heads, preferred_element_type=jnp.float32)
            * inv_root
        )
        scores = jnp.where(allowed[None, None], scores, masked_score)
        return key_heads, value_heads, allowed, scores

    def forward_stats(offset, current):
        row_max, row_sum, weighted = current
        key_heads, value_heads, allowed, scores = chunk(offset)
        new_max = jnp.maximum(row_max, jnp.max(scores, axis=-1))
        rescale = jnp.exp(row_max - new_max)
        shifted = jnp.where(allowed[None, None], jnp.exp(scores - new_max[..., None]), 0.0)
        row_sum = row_sum * rescale + jnp.sum(shifted, axis=-1)
        weighted = weighted * rescale[..., None] + jnp.einsum(
            "kgqt,tkd->kgqd",
            shifted.astype(jnp.bfloat16),
            value_heads,
            preferred_element_type=jnp.float32,
        )
        return (new_max, row_sum, weighted)

    def backward_chunk(offset, log_total, row_delta, scores_given=None):
        key_heads, value_heads, allowed, scores = chunk(offset)
        if scores_given is not None:
            scores = scores_given
        probs = jnp.exp(scores - log_total[..., None])
        dprobs = jnp.einsum(
            "qkgd,tkd->kgqt", grad_heads, value_heads, preferred_element_type=jnp.float32
        )
        dscores = (probs * (dprobs - row_delta[..., None])).astype(jnp.bfloat16)
        probs_low = probs.astype(jnp.bfloat16)
        query_term = (
            jnp.einsum("kgqt,tkd->qkgd", dscores, key_heads, preferred_element_type=jnp.float32)
            * inv_root
        )
        key_term = (
            jnp.einsum("kgqt,qkgd->tkd", dscores, query_heads, preferred_element_type=jnp.float32)
            * inv_root
        )
        value_term = jnp.einsum(
            "kgqt,qkgd->tkd", probs_low, grad_heads, preferred_element_type=jnp.float32
        )
        kv_term = jnp.concatenate(
            [key_term.reshape(step_rows, kv_cols), value_term.reshape(step_rows, kv_cols)], axis=1
        )
        return query_term, kv_term

    if steps == 1:
        allowed = chunk(0)[2]
        query_grad, kv_acc = attention_block(queries, out_grad, kv_rows, allowed)
    else:
        start_stats = (
            jnp.full((kv_heads, group_size, rows_here), masked_score, jnp.float32),
            jnp.zeros((kv_heads, group_size, rows_here), jnp.float32),
            jnp.zeros((kv_heads, group_size, rows_here, HD), jnp.float32),
        )
        row_max, row_sum, weighted = lax.fori_loop(
            0, steps, lambda i, c: forward_stats(i * step_rows, c), start_stats
        )
        log_total = row_max + jnp.log(row_sum)
        attended = (weighted / row_sum[..., None]).astype(jnp.bfloat16)
        row_delta = jnp.einsum(
            "kgqd,qkgd->kgq", attended, grad_heads, preferred_element_type=jnp.float32
        )

        def backward_visit(turn_index, current):
            query_now, kv_now = current
            offset = turn_index * step_rows
            query_term, kv_term = backward_chunk(offset, log_total, row_delta)
            kv_now = lax.dynamic_update_slice_in_dim(kv_now, kv_term, offset, 0)
            return (query_now + query_term, kv_now)

        query_acc, kv_acc = lax.fori_loop(
            0,
            steps,
            backward_visit,
            (
                jnp.zeros((rows_here, kv_heads, group_size, HD), jnp.float32),
                jnp.zeros((row_count, 2 * kv_cols), jnp.float32),
            ),
        )
        query_grad = query_acc.reshape(rows_here, -1).astype(jnp.bfloat16)

    kv_grad = scatter_slots(kv_acc, "ctx")
    key_grad = kv_grad[:, :kv_cols].astype(jnp.bfloat16)
    value_grad = kv_grad[:, kv_cols:].astype(jnp.bfloat16)
    input_grad_t = head_reduce(key_proj, value_proj, key_grad, value_grad)
    return (query_grad, key_grad, value_grad, input_grad_t)


def solution(mesh):
    return jax.shard_map(
        local,
        mesh=mesh,
        in_specs=(
            P(("groups", "ctx"), "head"),
            P(("groups", "ctx"), "head"),
            P(("groups", "ctx"), "head"),
            P(("groups", "ctx"), "head"),
            P("groups", None),
            P("groups"),
            P(None, "head"),
            P(None, "head"),
        ),
        out_specs=(
            P(("groups", "ctx"), "head"),
            P(("groups", "ctx"), "head"),
            P(("groups", "ctx"), "head"),
            P("head", ("groups", "ctx")),
        ),
        check_vma=False,
    )
```

```python
import math

import jax
import jax.numpy as jnp
from jax import lax
from jax.experimental import pallas as pl
from jax.experimental.pallas import tpu as pltpu
from jax.sharding import PartitionSpec as P

HD = 128
BLK = 128


masked_score = -1e30


def select_rows(lookup, picked):
    onehot = (picked[:, None] == lax.iota(jnp.int32, lookup.shape[0])[None, :]).astype(jnp.int32)
    return jnp.sum(onehot[:, :, None] * lookup[None, :, :], axis=1)


def select_cols(lookup, picked):
    onehot = (picked[:, None] == lax.iota(jnp.int32, lookup.shape[1])[None, :]).astype(jnp.int32)
    return jnp.sum(lookup[:, None, :] * onehot[None, :, :], axis=2)


def pick(vector, picked):
    onehot = (picked[:, None] == lax.iota(jnp.int32, vector.shape[0])[None, :]).astype(jnp.int32)
    return jnp.sum(onehot * vector[None, :], axis=1)


def shifted_pairs(count, steps):
    return [(source, (source + steps) % count) for source in range(count)]


def gather_slots(block, axis):
    count = lax.axis_size(axis)
    position = lax.axis_index(axis)
    if count > 8:
        gathered = lax.all_gather(block, axis, axis=0, tiled=True)
        return gathered, lax.iota(jnp.int32, count)
    pieces = [block] + [
        lax.ppermute(block, axis, shifted_pairs(count, steps)) for steps in range(1, count)
    ]
    sources = (position - lax.iota(jnp.int32, count)) % count
    return jnp.concatenate(pieces, axis=0), sources


def scatter_slots(slots, axis):
    count = lax.axis_size(axis)
    if count > 8:
        return lax.psum_scatter(slots, axis, scatter_dimension=0, tiled=True)
    rows = slots.shape[0] // count
    total = slots[:rows]
    for steps in range(1, count):
        total = total + lax.ppermute(
            slots[steps * rows : (steps + 1) * rows].astype(jnp.bfloat16),
            axis,
            shifted_pairs(count, -steps),
        ).astype(jnp.float32)
    return total


def projection_kernel(order_ref, key_ref, value_ref, key_grad_ref, value_grad_ref, out_ref):
    out_ref[...] = jnp.dot(
        key_ref[...], key_grad_ref[...], preferred_element_type=jnp.float32
    ) + jnp.dot(value_ref[...], value_grad_ref[...], preferred_element_type=jnp.float32)


def project_rows(key_proj, value_proj, key_grad, value_grad, blocks, block_rows):
    sub = math.gcd(block_rows, 2048)
    per = block_rows // sub
    features = key_proj.shape[1]
    tokens = key_grad.shape[0]

    def weight_rows(i, j, order):
        return (order[i] * per + j, 0)

    def whole(i, j, order):
        return (0, 0)

    grid_spec = pltpu.PrefetchScalarGridSpec(
        num_scalar_prefetch=1,
        grid=(blocks.shape[0], per),
        in_specs=[
            pl.BlockSpec((sub, features), weight_rows),
            pl.BlockSpec((sub, features), weight_rows),
            pl.BlockSpec((features, tokens), whole),
            pl.BlockSpec((features, tokens), whole),
        ],
        out_specs=pl.BlockSpec((sub, tokens), lambda i, j, order: (i * per + j, 0)),
    )
    return pl.pallas_call(
        projection_kernel,
        grid_spec=grid_spec,
        out_shape=jax.ShapeDtypeStruct((blocks.shape[0] * block_rows, tokens), jnp.float32),
    )(blocks, key_proj, value_proj, key_grad.T, value_grad.T)


def head_reduce(key_proj, value_proj, key_grad, value_grad):
    count = lax.axis_size("head")
    position = lax.axis_index("head")
    depth = count.bit_length() - 1
    contraction = (((1,), (1,)), ((), ()))
    if count == 1 or count != 1 << depth:
        partial = lax.dot_general(
            key_proj, key_grad, contraction, preferred_element_type=jnp.float32
        ) + lax.dot_general(value_proj, value_grad, contraction, preferred_element_type=jnp.float32)
        return lax.psum_scatter(partial, "head", scatter_dimension=0, tiled=True).astype(
            jnp.bfloat16
        )
    block = key_proj.shape[0] // count
    upper = lax.iota(jnp.int32, count // 2) * 2

    def project(half):
        return project_rows(key_proj, value_proj, key_grad, value_grad, upper + half, block).reshape(
            count // 2, block, -1
        )

    own_bit = position % 2
    sent = project(1 - own_bit)
    kept = project(own_bit)
    current = kept + lax.ppermute(sent, "head", [(i, i ^ 1) for i in range(count)])
    for level in range(1, depth):
        current = current.reshape(-1, 2, block, current.shape[-1])
        own_bit = (position // (1 << level)) % 2
        kept = lax.dynamic_index_in_dim(current, own_bit, 1, keepdims=False)
        sent = lax.dynamic_index_in_dim(current, 1 - own_bit, 1, keepdims=False)
        arrived = lax.ppermute(
            sent.astype(jnp.bfloat16), "head", [(i, i ^ (1 << level)) for i in range(count)]
        )
        current = kept + arrived.astype(jnp.float32)
    return current.reshape(block, -1).astype(jnp.bfloat16)


def attention_kernel(query_ref, grad_ref, kv_ref, mask_ref, query_out, kv_out):
    inv_root = HD ** (-0.5)
    kv_cols = kv_ref.shape[1] // 2
    kv_heads = kv_cols // HD
    group_size = query_ref.shape[1] // kv_cols
    allowed = mask_ref[...] > 0
    across = (((1,), (1,)), ((), ()))
    down = (((0,), (0,)), ((), ()))
    for kv_head in range(kv_heads):
        key_head = kv_ref[:, kv_head * HD : (kv_head + 1) * HD]
        value_head = kv_ref[:, kv_cols + kv_head * HD : kv_cols + (kv_head + 1) * HD]
        key_sum = jnp.zeros(key_head.shape, jnp.float32)
        value_sum = jnp.zeros(value_head.shape, jnp.float32)
        for member in range(group_size):
            first = (kv_head * group_size + member) * HD
            query_head = query_ref[:, first : first + HD]
            grad_head = grad_ref[:, first : first + HD]
            scores = (
                lax.dot_general(query_head, key_head, across, preferred_element_type=jnp.float32)
                * inv_root
            )
            scores = jnp.where(allowed, scores, masked_score)
            row_max = jnp.max(scores, axis=1, keepdims=True)
            shifted = jnp.exp(scores - row_max)
            row_sum = jnp.sum(shifted, axis=1, keepdims=True)
            weighted = jnp.dot(
                shifted.astype(jnp.bfloat16), value_head, preferred_element_type=jnp.float32
            )
            attended = (weighted / row_sum).astype(jnp.bfloat16)
            probs = shifted * (1.0 / row_sum)
            row_delta = jnp.sum(
                grad_head.astype(jnp.float32) * attended.astype(jnp.float32), axis=1, keepdims=True
            )
            dprobs = lax.dot_general(
                grad_head, value_head, across, preferred_element_type=jnp.float32
            )
            dscores = probs * (dprobs - row_delta)
            query_term = (
                jnp.dot(dscores.astype(jnp.bfloat16), key_head, preferred_element_type=jnp.float32)
                * inv_root
            )
            query_out[:, first : first + HD] = query_term.astype(jnp.bfloat16)
            key_sum = key_sum + lax.dot_general(
                dscores.astype(jnp.bfloat16), query_head, down, preferred_element_type=jnp.float32
            )
            value_sum = value_sum + lax.dot_general(
                probs.astype(jnp.bfloat16), grad_head, down, preferred_element_type=jnp.float32
            )
        kv_out[:, kv_head * HD : (kv_head + 1) * HD] = key_sum * inv_root
        kv_out[:, kv_cols + kv_head * HD : kv_cols + (kv_head + 1) * HD] = value_sum


def attention_block(queries, out_grad, kv_rows, allowed, interpret=False):
    return pl.pallas_call(
        attention_kernel,
        out_shape=(
            jax.ShapeDtypeStruct(queries.shape, jnp.bfloat16),
            jax.ShapeDtypeStruct(kv_rows.shape, jnp.float32),
        ),
        interpret=interpret,
    )(queries, out_grad, kv_rows, allowed.astype(jnp.int32))


def local(
    queries, key_states, value_states, out_grad, mask_flags, shard_blocks, key_proj, value_proj
):
    rows_here = queries.shape[0]
    kv_cols = key_states.shape[1]
    kv_heads = kv_cols // HD
    group_size = queries.shape[1] // kv_cols
    inv_root = HD ** (-0.5)
    position = lax.axis_index("ctx")
    query_heads = queries.reshape(rows_here, kv_heads, group_size, HD)
    grad_heads = out_grad.reshape(rows_here, kv_heads, group_size, HD)
    own_blocks = lax.dynamic_slice_in_dim(
        shard_blocks, position * (rows_here // BLK), rows_here // BLK
    )
    own_flags = select_rows(mask_flags, own_blocks)

    kv_rows, sources = gather_slots(
        jnp.concatenate([key_states, value_states], axis=1), "ctx"
    )
    row_count = kv_rows.shape[0]
    blocks_here = rows_here // BLK
    key_blocks = lax.iota(jnp.int32, row_count // BLK)
    key_doc_blocks = pick(
        shard_blocks,
        pick(sources, key_blocks // blocks_here) * blocks_here + key_blocks % blocks_here,
    )
    step_rows = math.gcd(row_count, 512)
    steps = row_count // step_rows

    def chunk(offset):
        block = lax.dynamic_slice_in_dim(kv_rows, offset, step_rows)
        key_heads = block[:, :kv_cols].reshape(step_rows, kv_heads, HD)
        value_heads = block[:, kv_cols:].reshape(step_rows, kv_heads, HD)
        their_blocks = lax.dynamic_slice_in_dim(key_doc_blocks, offset // BLK, step_rows // BLK)
        pair_flags = select_cols(own_flags, their_blocks) > 0
        allowed = jnp.repeat(jnp.repeat(pair_flags, BLK, axis=0), BLK, axis=1)
        scores = (
            jnp.einsum("qkgd,tkd->kgqt", query_heads, key_heads, preferred_element_type=jnp.float32)
            * inv_root
        )
        scores = jnp.where(allowed[None, None], scores, masked_score)
        return key_heads, value_heads, allowed, scores

    def forward_stats(offset, current):
        row_max, row_sum, weighted = current
        key_heads, value_heads, allowed, scores = chunk(offset)
        new_max = jnp.maximum(row_max, jnp.max(scores, axis=-1))
        rescale = jnp.exp(row_max - new_max)
        shifted = jnp.where(allowed[None, None], jnp.exp(scores - new_max[..., None]), 0.0)
        row_sum = row_sum * rescale + jnp.sum(shifted, axis=-1)
        weighted = weighted * rescale[..., None] + jnp.einsum(
            "kgqt,tkd->kgqd",
            shifted.astype(jnp.bfloat16),
            value_heads,
            preferred_element_type=jnp.float32,
        )
        return (new_max, row_sum, weighted)

    def backward_chunk(offset, log_total, row_delta, scores_given=None):
        key_heads, value_heads, allowed, scores = chunk(offset)
        if scores_given is not None:
            scores = scores_given
        probs = jnp.exp(scores - log_total[..., None])
        dprobs = jnp.einsum(
            "qkgd,tkd->kgqt", grad_heads, value_heads, preferred_element_type=jnp.float32
        )
        dscores = (probs * (dprobs - row_delta[..., None])).astype(jnp.bfloat16)
        probs_low = probs.astype(jnp.bfloat16)
        query_term = (
            jnp.einsum("kgqt,tkd->qkgd", dscores, key_heads, preferred_element_type=jnp.float32)
            * inv_root
        )
        key_term = (
            jnp.einsum("kgqt,qkgd->tkd", dscores, query_heads, preferred_element_type=jnp.float32)
            * inv_root
        )
        value_term = jnp.einsum(
            "kgqt,qkgd->tkd", probs_low, grad_heads, preferred_element_type=jnp.float32
        )
        kv_term = jnp.concatenate(
            [key_term.reshape(step_rows, kv_cols), value_term.reshape(step_rows, kv_cols)], axis=1
        )
        return query_term, kv_term

    if steps == 1:
        allowed = chunk(0)[2]
        query_grad, kv_acc = attention_block(queries, out_grad, kv_rows, allowed)
    else:
        start_stats = (
            jnp.full((kv_heads, group_size, rows_here), masked_score, jnp.float32),
            jnp.zeros((kv_heads, group_size, rows_here), jnp.float32),
            jnp.zeros((kv_heads, group_size, rows_here, HD), jnp.float32),
        )
        row_max, row_sum, weighted = lax.fori_loop(
            0, steps, lambda i, c: forward_stats(i * step_rows, c), start_stats
        )
        log_total = row_max + jnp.log(row_sum)
        attended = (weighted / row_sum[..., None]).astype(jnp.bfloat16)
        row_delta = jnp.einsum(
            "kgqd,qkgd->kgq", attended, grad_heads, preferred_element_type=jnp.float32
        )

        def backward_visit(turn_index, current):
            query_now, kv_now = current
            offset = turn_index * step_rows
            query_term, kv_term = backward_chunk(offset, log_total, row_delta)
            kv_now = lax.dynamic_update_slice_in_dim(kv_now, kv_term, offset, 0)
            return (query_now + query_term, kv_now)

        query_acc, kv_acc = lax.fori_loop(
            0,
            steps,
            backward_visit,
            (
                jnp.zeros((rows_here, kv_heads, group_size, HD), jnp.float32),
                jnp.zeros((row_count, 2 * kv_cols), jnp.float32),
            ),
        )
        query_grad = query_acc.reshape(rows_here, -1).astype(jnp.bfloat16)

    kv_grad = scatter_slots(kv_acc, "ctx")
    key_grad = kv_grad[:, :kv_cols].astype(jnp.bfloat16)
    value_grad = kv_grad[:, kv_cols:].astype(jnp.bfloat16)
    input_grad_t = head_reduce(key_proj, value_proj, key_grad, value_grad)
    return (query_grad, key_grad, value_grad, input_grad_t)


def solution(mesh):
    return jax.shard_map(
        local,
        mesh=mesh,
        in_specs=(
            P(("groups", "ctx"), "head"),
            P(("groups", "ctx"), "head"),
            P(("groups", "ctx"), "head"),
            P(("groups", "ctx"), "head"),
            P("groups", None),
            P("groups"),
            P(None, "head"),
            P(None, "head"),
        ),
        out_specs=(
            P(("groups", "ctx"), "head"),
            P(("groups", "ctx"), "head"),
            P(("groups", "ctx"), "head"),
            P("head", ("groups", "ctx")),
        ),
        check_vma=False,
    )
```

```python
import math

import jax
import jax.numpy as jnp
from jax import lax
from jax.experimental import pallas as pl
from jax.sharding import PartitionSpec as P

HD = 128
BLK = 128


masked_score = -1e30


def select_rows(lookup, picked):
    onehot = (picked[:, None] == lax.iota(jnp.int32, lookup.shape[0])[None, :]).astype(jnp.int32)
    return jnp.sum(onehot[:, :, None] * lookup[None, :, :], axis=1)


def select_cols(lookup, picked):
    onehot = (picked[:, None] == lax.iota(jnp.int32, lookup.shape[1])[None, :]).astype(jnp.int32)
    return jnp.sum(lookup[:, None, :] * onehot[None, :, :], axis=2)


def pick(vector, picked):
    onehot = (picked[:, None] == lax.iota(jnp.int32, vector.shape[0])[None, :]).astype(jnp.int32)
    return jnp.sum(onehot * vector[None, :], axis=1)


def shifted_pairs(count, steps):
    return [(source, (source + steps) % count) for source in range(count)]


def gather_slots(block, axis):
    count = lax.axis_size(axis)
    position = lax.axis_index(axis)
    if count > 8:
        gathered = lax.all_gather(block, axis, axis=0, tiled=True)
        return gathered, lax.iota(jnp.int32, count)
    pieces = [block] + [
        lax.ppermute(block, axis, shifted_pairs(count, steps)) for steps in range(1, count)
    ]
    sources = (position - lax.iota(jnp.int32, count)) % count
    return jnp.concatenate(pieces, axis=0), sources


def scatter_slots(slots, axis):
    count = lax.axis_size(axis)
    if count > 8:
        return lax.psum_scatter(slots, axis, scatter_dimension=0, tiled=True)
    rows = slots.shape[0] // count
    total = slots[:rows]
    for steps in range(1, count):
        total = total + lax.ppermute(
            slots[steps * rows : (steps + 1) * rows].astype(jnp.bfloat16),
            axis,
            shifted_pairs(count, -steps),
        ).astype(jnp.float32)
    return total


def head_reduce(key_proj, value_proj, key_grad, value_grad):
    count = lax.axis_size("head")
    position = lax.axis_index("head")
    depth = count.bit_length() - 1
    contraction = (((1,), (1,)), ((), ()))
    if count == 1 or count != 1 << depth:
        partial = lax.dot_general(
            key_proj, key_grad, contraction, preferred_element_type=jnp.float32
        ) + lax.dot_general(value_proj, value_grad, contraction, preferred_element_type=jnp.float32)
        return lax.psum_scatter(partial, "head", scatter_dimension=0, tiled=True).astype(
            jnp.bfloat16
        )
    block = key_proj.shape[0] // count
    key_split = key_proj.reshape(count // 2, 2, block, key_proj.shape[1])
    value_split = value_proj.reshape(count // 2, 2, block, value_proj.shape[1])

    def project(half):
        return jnp.einsum(
            "arf,tf->art",
            lax.dynamic_index_in_dim(key_split, half, 1, keepdims=False),
            key_grad,
            preferred_element_type=jnp.float32,
        ) + jnp.einsum(
            "arf,tf->art",
            lax.dynamic_index_in_dim(value_split, half, 1, keepdims=False),
            value_grad,
            preferred_element_type=jnp.float32,
        )

    own_bit = position % 2
    sent = project(1 - own_bit)
    kept = project(own_bit)
    current = kept + lax.ppermute(sent, "head", [(i, i ^ 1) for i in range(count)])
    for level in range(1, depth):
        current = current.reshape(-1, 2, block, current.shape[-1])
        own_bit = (position // (1 << level)) % 2
        kept = lax.dynamic_index_in_dim(current, own_bit, 1, keepdims=False)
        sent = lax.dynamic_index_in_dim(current, 1 - own_bit, 1, keepdims=False)
        arrived = lax.ppermute(
            sent.astype(jnp.bfloat16), "head", [(i, i ^ (1 << level)) for i in range(count)]
        )
        current = kept + arrived.astype(jnp.float32)
    return current.reshape(block, -1).astype(jnp.bfloat16)


def attention_kernel(query_ref, grad_ref, kv_ref, mask_ref, query_out, kv_out):
    inv_root = HD ** (-0.5)
    kv_cols = kv_ref.shape[1] // 2
    kv_heads = kv_cols // HD
    rows = query_ref.shape[0]
    group_size = query_ref.shape[1] // kv_cols
    allowed = jnp.concatenate([mask_ref[...]] * group_size, axis=0) > 0
    across = (((1,), (1,)), ((), ()))
    down = (((0,), (0,)), ((), ()))
    for kv_head in range(kv_heads):
        key_head = kv_ref[:, kv_head * HD : (kv_head + 1) * HD]
        value_head = kv_ref[:, kv_cols + kv_head * HD : kv_cols + (kv_head + 1) * HD]
        base = kv_head * group_size * HD
        query_stack = jnp.concatenate(
            [query_ref[:, base + m * HD : base + (m + 1) * HD] for m in range(group_size)], axis=0
        )
        grad_stack = jnp.concatenate(
            [grad_ref[:, base + m * HD : base + (m + 1) * HD] for m in range(group_size)], axis=0
        )
        scores = (
            lax.dot_general(query_stack, key_head, across, preferred_element_type=jnp.float32)
            * inv_root
        )
        scores = jnp.where(allowed, scores, masked_score)
        row_max = jnp.max(scores, axis=1, keepdims=True)
        shifted = jnp.exp(scores - row_max)
        row_sum = jnp.sum(shifted, axis=1, keepdims=True)
        weighted = jnp.dot(
            shifted.astype(jnp.bfloat16), value_head, preferred_element_type=jnp.float32
        )
        attended = (weighted / row_sum).astype(jnp.bfloat16)
        probs = shifted * (1.0 / row_sum)
        row_delta = jnp.sum(
            grad_stack.astype(jnp.float32) * attended.astype(jnp.float32), axis=1, keepdims=True
        )
        dprobs = lax.dot_general(grad_stack, value_head, across, preferred_element_type=jnp.float32)
        dscores = (probs * (dprobs - row_delta)).astype(jnp.bfloat16)
        query_term = jnp.dot(dscores, key_head, preferred_element_type=jnp.float32) * inv_root
        for m in range(group_size):
            query_out[:, base + m * HD : base + (m + 1) * HD] = query_term[
                m * rows : (m + 1) * rows
            ].astype(jnp.bfloat16)
        key_sum = lax.dot_general(dscores, query_stack, down, preferred_element_type=jnp.float32)
        value_sum = lax.dot_general(
            probs.astype(jnp.bfloat16), grad_stack, down, preferred_element_type=jnp.float32
        )
        kv_out[:, kv_head * HD : (kv_head + 1) * HD] = key_sum * inv_root
        kv_out[:, kv_cols + kv_head * HD : kv_cols + (kv_head + 1) * HD] = value_sum


def attention_block(queries, out_grad, kv_rows, allowed, interpret=False):
    return pl.pallas_call(
        attention_kernel,
        out_shape=(
            jax.ShapeDtypeStruct(queries.shape, jnp.bfloat16),
            jax.ShapeDtypeStruct(kv_rows.shape, jnp.float32),
        ),
        interpret=interpret,
    )(queries, out_grad, kv_rows, allowed.astype(jnp.int32))


def local(
    queries, key_states, value_states, out_grad, mask_flags, shard_blocks, key_proj, value_proj
):
    rows_here = queries.shape[0]
    kv_cols = key_states.shape[1]
    kv_heads = kv_cols // HD
    group_size = queries.shape[1] // kv_cols
    inv_root = HD ** (-0.5)
    position = lax.axis_index("ctx")
    query_heads = queries.reshape(rows_here, kv_heads, group_size, HD)
    grad_heads = out_grad.reshape(rows_here, kv_heads, group_size, HD)
    own_blocks = lax.dynamic_slice_in_dim(
        shard_blocks, position * (rows_here // BLK), rows_here // BLK
    )
    own_flags = select_rows(mask_flags, own_blocks)

    kv_rows, sources = gather_slots(
        jnp.concatenate([key_states, value_states], axis=1), "ctx"
    )
    row_count = kv_rows.shape[0]
    blocks_here = rows_here // BLK
    key_blocks = lax.iota(jnp.int32, row_count // BLK)
    key_doc_blocks = pick(
        shard_blocks,
        pick(sources, key_blocks // blocks_here) * blocks_here + key_blocks % blocks_here,
    )
    step_rows = math.gcd(row_count, 512)
    steps = row_count // step_rows

    def chunk(offset):
        block = lax.dynamic_slice_in_dim(kv_rows, offset, step_rows)
        key_heads = block[:, :kv_cols].reshape(step_rows, kv_heads, HD)
        value_heads = block[:, kv_cols:].reshape(step_rows, kv_heads, HD)
        their_blocks = lax.dynamic_slice_in_dim(key_doc_blocks, offset // BLK, step_rows // BLK)
        pair_flags = select_cols(own_flags, their_blocks) > 0
        allowed = jnp.repeat(jnp.repeat(pair_flags, BLK, axis=0), BLK, axis=1)
        scores = (
            jnp.einsum("qkgd,tkd->kgqt", query_heads, key_heads, preferred_element_type=jnp.float32)
            * inv_root
        )
        scores = jnp.where(allowed[None, None], scores, masked_score)
        return key_heads, value_heads, allowed, scores

    def forward_stats(offset, current):
        row_max, row_sum, weighted = current
        key_heads, value_heads, allowed, scores = chunk(offset)
        new_max = jnp.maximum(row_max, jnp.max(scores, axis=-1))
        rescale = jnp.exp(row_max - new_max)
        shifted = jnp.where(allowed[None, None], jnp.exp(scores - new_max[..., None]), 0.0)
        row_sum = row_sum * rescale + jnp.sum(shifted, axis=-1)
        weighted = weighted * rescale[..., None] + jnp.einsum(
            "kgqt,tkd->kgqd",
            shifted.astype(jnp.bfloat16),
            value_heads,
            preferred_element_type=jnp.float32,
        )
        return (new_max, row_sum, weighted)

    def backward_chunk(offset, log_total, row_delta, scores_given=None):
        key_heads, value_heads, allowed, scores = chunk(offset)
        if scores_given is not None:
            scores = scores_given
        probs = jnp.exp(scores - log_total[..., None])
        dprobs = jnp.einsum(
            "qkgd,tkd->kgqt", grad_heads, value_heads, preferred_element_type=jnp.float32
        )
        dscores = (probs * (dprobs - row_delta[..., None])).astype(jnp.bfloat16)
        probs_low = probs.astype(jnp.bfloat16)
        query_term = (
            jnp.einsum("kgqt,tkd->qkgd", dscores, key_heads, preferred_element_type=jnp.float32)
            * inv_root
        )
        key_term = (
            jnp.einsum("kgqt,qkgd->tkd", dscores, query_heads, preferred_element_type=jnp.float32)
            * inv_root
        )
        value_term = jnp.einsum(
            "kgqt,qkgd->tkd", probs_low, grad_heads, preferred_element_type=jnp.float32
        )
        kv_term = jnp.concatenate(
            [key_term.reshape(step_rows, kv_cols), value_term.reshape(step_rows, kv_cols)], axis=1
        )
        return query_term, kv_term

    if steps == 1:
        allowed = chunk(0)[2]
        query_grad, kv_acc = attention_block(queries, out_grad, kv_rows, allowed)
    else:
        start_stats = (
            jnp.full((kv_heads, group_size, rows_here), masked_score, jnp.float32),
            jnp.zeros((kv_heads, group_size, rows_here), jnp.float32),
            jnp.zeros((kv_heads, group_size, rows_here, HD), jnp.float32),
        )
        row_max, row_sum, weighted = lax.fori_loop(
            0, steps, lambda i, c: forward_stats(i * step_rows, c), start_stats
        )
        log_total = row_max + jnp.log(row_sum)
        attended = (weighted / row_sum[..., None]).astype(jnp.bfloat16)
        row_delta = jnp.einsum(
            "kgqd,qkgd->kgq", attended, grad_heads, preferred_element_type=jnp.float32
        )

        def backward_visit(turn_index, current):
            query_now, kv_now = current
            offset = turn_index * step_rows
            query_term, kv_term = backward_chunk(offset, log_total, row_delta)
            kv_now = lax.dynamic_update_slice_in_dim(kv_now, kv_term, offset, 0)
            return (query_now + query_term, kv_now)

        query_acc, kv_acc = lax.fori_loop(
            0,
            steps,
            backward_visit,
            (
                jnp.zeros((rows_here, kv_heads, group_size, HD), jnp.float32),
                jnp.zeros((row_count, 2 * kv_cols), jnp.float32),
            ),
        )
        query_grad = query_acc.reshape(rows_here, -1).astype(jnp.bfloat16)

    kv_grad = scatter_slots(kv_acc, "ctx")
    key_grad = kv_grad[:, :kv_cols].astype(jnp.bfloat16)
    value_grad = kv_grad[:, kv_cols:].astype(jnp.bfloat16)
    input_grad_t = head_reduce(key_proj, value_proj, key_grad, value_grad)
    return (query_grad, key_grad, value_grad, input_grad_t)


def solution(mesh):
    return jax.shard_map(
        local,
        mesh=mesh,
        in_specs=(
            P(("groups", "ctx"), "head"),
            P(("groups", "ctx"), "head"),
            P(("groups", "ctx"), "head"),
            P(("groups", "ctx"), "head"),
            P("groups", None),
            P("groups"),
            P(None, "head"),
            P(None, "head"),
        ),
        out_specs=(
            P(("groups", "ctx"), "head"),
            P(("groups", "ctx"), "head"),
            P(("groups", "ctx"), "head"),
            P("head", ("groups", "ctx")),
        ),
        check_vma=False,
    )
```

```python
import math

import jax
import jax.numpy as jnp
from jax import lax
from jax.experimental import pallas as pl
from jax.sharding import PartitionSpec as P

HD = 128
BLK = 128


masked_score = -1e30


def select_rows(lookup, picked):
    onehot = (picked[:, None] == lax.iota(jnp.int32, lookup.shape[0])[None, :]).astype(jnp.int32)
    return jnp.sum(onehot[:, :, None] * lookup[None, :, :], axis=1)


def select_cols(lookup, picked):
    onehot = (picked[:, None] == lax.iota(jnp.int32, lookup.shape[1])[None, :]).astype(jnp.int32)
    return jnp.sum(lookup[:, None, :] * onehot[None, :, :], axis=2)


def pick(vector, picked):
    onehot = (picked[:, None] == lax.iota(jnp.int32, vector.shape[0])[None, :]).astype(jnp.int32)
    return jnp.sum(onehot * vector[None, :], axis=1)


def shifted_pairs(count, steps):
    return [(source, (source + steps) % count) for source in range(count)]


def gather_slots(block, axis):
    count = lax.axis_size(axis)
    position = lax.axis_index(axis)
    if count > 8:
        gathered = lax.all_gather(block, axis, axis=0, tiled=True)
        return gathered, lax.iota(jnp.int32, count)
    pieces = [block] + [
        lax.ppermute(block, axis, shifted_pairs(count, steps)) for steps in range(1, count)
    ]
    sources = (position - lax.iota(jnp.int32, count)) % count
    return jnp.concatenate(pieces, axis=0), sources


def scatter_slots(slots, axis):
    count = lax.axis_size(axis)
    if count > 8:
        return lax.psum_scatter(slots, axis, scatter_dimension=0, tiled=True)
    rows = slots.shape[0] // count
    total = slots[:rows]
    for steps in range(1, count):
        total = total + lax.ppermute(
            slots[steps * rows : (steps + 1) * rows].astype(jnp.bfloat16),
            axis,
            shifted_pairs(count, -steps),
        ).astype(jnp.float32)
    return total


def two_level_reduce(key_proj, value_proj, key_grad, value_grad, block, position):
    across = (((1,), (1,)), ((), ()))
    core_bit = position % 2
    chip_bit = position // 2

    def project(chip, core):
        first = (chip * 2 + core) * block
        return lax.dot_general(
            lax.dynamic_slice_in_dim(key_proj, first, block, 0),
            key_grad,
            across,
            preferred_element_type=jnp.float32,
        ) + lax.dot_general(
            lax.dynamic_slice_in_dim(value_proj, first, block, 0),
            value_grad,
            across,
            preferred_element_type=jnp.float32,
        )

    sibling = [(i, i ^ 1) for i in range(4)]
    partner = [(i, i ^ 2) for i in range(4)]
    for_sibling_send = lax.ppermute(project(1 - chip_bit, 1 - core_bit), "head", sibling)
    chip_sum = project(1 - chip_bit, core_bit) + for_sibling_send
    from_other_chip = lax.ppermute(chip_sum.astype(jnp.bfloat16), "head", partner)
    from_sibling = lax.ppermute(project(chip_bit, 1 - core_bit), "head", sibling)
    total = project(chip_bit, core_bit) + from_sibling + from_other_chip.astype(jnp.float32)
    return total.astype(jnp.bfloat16)


def head_reduce(key_proj, value_proj, key_grad, value_grad):
    count = lax.axis_size("head")
    position = lax.axis_index("head")
    depth = count.bit_length() - 1
    contraction = (((1,), (1,)), ((), ()))
    if count == 1 or count != 1 << depth:
        partial = lax.dot_general(
            key_proj, key_grad, contraction, preferred_element_type=jnp.float32
        ) + lax.dot_general(value_proj, value_grad, contraction, preferred_element_type=jnp.float32)
        return lax.psum_scatter(partial, "head", scatter_dimension=0, tiled=True).astype(
            jnp.bfloat16
        )
    block = key_proj.shape[0] // count
    key_split = key_proj.reshape(count // 2, 2, block, key_proj.shape[1])
    value_split = value_proj.reshape(count // 2, 2, block, value_proj.shape[1])

    def project(half):
        return jnp.einsum(
            "arf,tf->art",
            lax.dynamic_index_in_dim(key_split, half, 1, keepdims=False),
            key_grad,
            preferred_element_type=jnp.float32,
        ) + jnp.einsum(
            "arf,tf->art",
            lax.dynamic_index_in_dim(value_split, half, 1, keepdims=False),
            value_grad,
            preferred_element_type=jnp.float32,
        )

    if depth == 2:
        return two_level_reduce(key_proj, value_proj, key_grad, value_grad, block, position)
    own_bit = position % 2
    sent = project(1 - own_bit)
    kept = project(own_bit)
    current = kept + lax.ppermute(sent, "head", [(i, i ^ 1) for i in range(count)])
    for level in range(1, depth):
        current = current.reshape(-1, 2, block, current.shape[-1])
        own_bit = (position // (1 << level)) % 2
        kept = lax.dynamic_index_in_dim(current, own_bit, 1, keepdims=False)
        sent = lax.dynamic_index_in_dim(current, 1 - own_bit, 1, keepdims=False)
        arrived = lax.ppermute(
            sent.astype(jnp.bfloat16), "head", [(i, i ^ (1 << level)) for i in range(count)]
        )
        current = kept + arrived.astype(jnp.float32)
    return current.reshape(block, -1).astype(jnp.bfloat16)


def attention_kernel(query_ref, grad_ref, kv_ref, mask_ref, query_out, kv_out):
    inv_root = HD ** (-0.5)
    kv_cols = kv_ref.shape[1] // 2
    kv_heads = kv_cols // HD
    rows = query_ref.shape[0]
    group_size = query_ref.shape[1] // kv_cols
    allowed = jnp.concatenate([mask_ref[...]] * group_size, axis=0) > 0
    across = (((1,), (1,)), ((), ()))
    down = (((0,), (0,)), ((), ()))
    for kv_head in range(kv_heads):
        key_head = kv_ref[:, kv_head * HD : (kv_head + 1) * HD]
        value_head = kv_ref[:, kv_cols + kv_head * HD : kv_cols + (kv_head + 1) * HD]
        base = kv_head * group_size * HD
        query_stack = jnp.concatenate(
            [query_ref[:, base + m * HD : base + (m + 1) * HD] for m in range(group_size)], axis=0
        )
        grad_stack = jnp.concatenate(
            [grad_ref[:, base + m * HD : base + (m + 1) * HD] for m in range(group_size)], axis=0
        )
        scores = (
            lax.dot_general(query_stack, key_head, across, preferred_element_type=jnp.float32)
            * inv_root
        )
        scores = jnp.where(allowed, scores, masked_score)
        row_max = jnp.max(scores, axis=1, keepdims=True)
        shifted = jnp.exp(scores - row_max)
        row_sum = jnp.sum(shifted, axis=1, keepdims=True)
        weighted = jnp.dot(
            shifted.astype(jnp.bfloat16), value_head, preferred_element_type=jnp.float32
        )
        attended = (weighted / row_sum).astype(jnp.bfloat16)
        probs = shifted * (1.0 / row_sum)
        row_delta = jnp.sum(
            grad_stack.astype(jnp.float32) * attended.astype(jnp.float32), axis=1, keepdims=True
        )
        dprobs = lax.dot_general(grad_stack, value_head, across, preferred_element_type=jnp.float32)
        dscores = (probs * (dprobs - row_delta)).astype(jnp.bfloat16)
        query_term = jnp.dot(dscores, key_head, preferred_element_type=jnp.float32) * inv_root
        for m in range(group_size):
            query_out[:, base + m * HD : base + (m + 1) * HD] = query_term[
                m * rows : (m + 1) * rows
            ].astype(jnp.bfloat16)
        key_sum = lax.dot_general(dscores, query_stack, down, preferred_element_type=jnp.float32)
        value_sum = lax.dot_general(
            probs.astype(jnp.bfloat16), grad_stack, down, preferred_element_type=jnp.float32
        )
        kv_out[:, kv_head * HD : (kv_head + 1) * HD] = key_sum * inv_root
        kv_out[:, kv_cols + kv_head * HD : kv_cols + (kv_head + 1) * HD] = value_sum


def attention_block(queries, out_grad, kv_rows, allowed, interpret=False):
    return pl.pallas_call(
        attention_kernel,
        out_shape=(
            jax.ShapeDtypeStruct(queries.shape, jnp.bfloat16),
            jax.ShapeDtypeStruct(kv_rows.shape, jnp.float32),
        ),
        interpret=interpret,
    )(queries, out_grad, kv_rows, allowed.astype(jnp.int32))


def local(
    queries, key_states, value_states, out_grad, mask_flags, shard_blocks, key_proj, value_proj
):
    rows_here = queries.shape[0]
    kv_cols = key_states.shape[1]
    kv_heads = kv_cols // HD
    group_size = queries.shape[1] // kv_cols
    inv_root = HD ** (-0.5)
    position = lax.axis_index("ctx")
    query_heads = queries.reshape(rows_here, kv_heads, group_size, HD)
    grad_heads = out_grad.reshape(rows_here, kv_heads, group_size, HD)
    own_blocks = lax.dynamic_slice_in_dim(
        shard_blocks, position * (rows_here // BLK), rows_here // BLK
    )
    own_flags = select_rows(mask_flags, own_blocks)

    kv_rows, sources = gather_slots(
        jnp.concatenate([key_states, value_states], axis=1), "ctx"
    )
    row_count = kv_rows.shape[0]
    blocks_here = rows_here // BLK
    key_blocks = lax.iota(jnp.int32, row_count // BLK)
    key_doc_blocks = pick(
        shard_blocks,
        pick(sources, key_blocks // blocks_here) * blocks_here + key_blocks % blocks_here,
    )
    step_rows = math.gcd(row_count, 512)
    steps = row_count // step_rows

    def chunk(offset):
        block = lax.dynamic_slice_in_dim(kv_rows, offset, step_rows)
        key_heads = block[:, :kv_cols].reshape(step_rows, kv_heads, HD)
        value_heads = block[:, kv_cols:].reshape(step_rows, kv_heads, HD)
        their_blocks = lax.dynamic_slice_in_dim(key_doc_blocks, offset // BLK, step_rows // BLK)
        pair_flags = select_cols(own_flags, their_blocks) > 0
        allowed = jnp.repeat(jnp.repeat(pair_flags, BLK, axis=0), BLK, axis=1)
        scores = (
            jnp.einsum("qkgd,tkd->kgqt", query_heads, key_heads, preferred_element_type=jnp.float32)
            * inv_root
        )
        scores = jnp.where(allowed[None, None], scores, masked_score)
        return key_heads, value_heads, allowed, scores

    def forward_stats(offset, current):
        row_max, row_sum, weighted = current
        key_heads, value_heads, allowed, scores = chunk(offset)
        new_max = jnp.maximum(row_max, jnp.max(scores, axis=-1))
        rescale = jnp.exp(row_max - new_max)
        shifted = jnp.where(allowed[None, None], jnp.exp(scores - new_max[..., None]), 0.0)
        row_sum = row_sum * rescale + jnp.sum(shifted, axis=-1)
        weighted = weighted * rescale[..., None] + jnp.einsum(
            "kgqt,tkd->kgqd",
            shifted.astype(jnp.bfloat16),
            value_heads,
            preferred_element_type=jnp.float32,
        )
        return (new_max, row_sum, weighted)

    def backward_chunk(offset, log_total, row_delta, scores_given=None):
        key_heads, value_heads, allowed, scores = chunk(offset)
        if scores_given is not None:
            scores = scores_given
        probs = jnp.exp(scores - log_total[..., None])
        dprobs = jnp.einsum(
            "qkgd,tkd->kgqt", grad_heads, value_heads, preferred_element_type=jnp.float32
        )
        dscores = (probs * (dprobs - row_delta[..., None])).astype(jnp.bfloat16)
        probs_low = probs.astype(jnp.bfloat16)
        query_term = (
            jnp.einsum("kgqt,tkd->qkgd", dscores, key_heads, preferred_element_type=jnp.float32)
            * inv_root
        )
        key_term = (
            jnp.einsum("kgqt,qkgd->tkd", dscores, query_heads, preferred_element_type=jnp.float32)
            * inv_root
        )
        value_term = jnp.einsum(
            "kgqt,qkgd->tkd", probs_low, grad_heads, preferred_element_type=jnp.float32
        )
        kv_term = jnp.concatenate(
            [key_term.reshape(step_rows, kv_cols), value_term.reshape(step_rows, kv_cols)], axis=1
        )
        return query_term, kv_term

    if steps == 1:
        allowed = chunk(0)[2]
        query_grad, kv_acc = attention_block(queries, out_grad, kv_rows, allowed)
    else:
        start_stats = (
            jnp.full((kv_heads, group_size, rows_here), masked_score, jnp.float32),
            jnp.zeros((kv_heads, group_size, rows_here), jnp.float32),
            jnp.zeros((kv_heads, group_size, rows_here, HD), jnp.float32),
        )
        row_max, row_sum, weighted = lax.fori_loop(
            0, steps, lambda i, c: forward_stats(i * step_rows, c), start_stats
        )
        log_total = row_max + jnp.log(row_sum)
        attended = (weighted / row_sum[..., None]).astype(jnp.bfloat16)
        row_delta = jnp.einsum(
            "kgqd,qkgd->kgq", attended, grad_heads, preferred_element_type=jnp.float32
        )

        def backward_visit(turn_index, current):
            query_now, kv_now = current
            offset = turn_index * step_rows
            query_term, kv_term = backward_chunk(offset, log_total, row_delta)
            kv_now = lax.dynamic_update_slice_in_dim(kv_now, kv_term, offset, 0)
            return (query_now + query_term, kv_now)

        query_acc, kv_acc = lax.fori_loop(
            0,
            steps,
            backward_visit,
            (
                jnp.zeros((rows_here, kv_heads, group_size, HD), jnp.float32),
                jnp.zeros((row_count, 2 * kv_cols), jnp.float32),
            ),
        )
        query_grad = query_acc.reshape(rows_here, -1).astype(jnp.bfloat16)

    kv_grad = scatter_slots(kv_acc, "ctx")
    key_grad = kv_grad[:, :kv_cols].astype(jnp.bfloat16)
    value_grad = kv_grad[:, kv_cols:].astype(jnp.bfloat16)
    input_grad_t = head_reduce(key_proj, value_proj, key_grad, value_grad)
    return (query_grad, key_grad, value_grad, input_grad_t)


def solution(mesh):
    return jax.shard_map(
        local,
        mesh=mesh,
        in_specs=(
            P(("groups", "ctx"), "head"),
            P(("groups", "ctx"), "head"),
            P(("groups", "ctx"), "head"),
            P(("groups", "ctx"), "head"),
            P("groups", None),
            P("groups"),
            P(None, "head"),
            P(None, "head"),
        ),
        out_specs=(
            P(("groups", "ctx"), "head"),
            P(("groups", "ctx"), "head"),
            P(("groups", "ctx"), "head"),
            P("head", ("groups", "ctx")),
        ),
        check_vma=False,
    )
```

```python
import math

import jax
import jax.numpy as jnp
from jax import lax
from jax.experimental import pallas as pl
from jax.sharding import PartitionSpec as P

HD = 128
BLK = 128


masked_score = -1e30


def select_rows(lookup, picked):
    onehot = (picked[:, None] == lax.iota(jnp.int32, lookup.shape[0])[None, :]).astype(jnp.int32)
    return jnp.sum(onehot[:, :, None] * lookup[None, :, :], axis=1)


def select_cols(lookup, picked):
    onehot = (picked[:, None] == lax.iota(jnp.int32, lookup.shape[1])[None, :]).astype(jnp.int32)
    return jnp.sum(lookup[:, None, :] * onehot[None, :, :], axis=2)


def pick(vector, picked):
    onehot = (picked[:, None] == lax.iota(jnp.int32, vector.shape[0])[None, :]).astype(jnp.int32)
    return jnp.sum(onehot * vector[None, :], axis=1)


def shifted_pairs(count, steps):
    return [(source, (source + steps) % count) for source in range(count)]


def gather_slots(block, axis):
    count = lax.axis_size(axis)
    position = lax.axis_index(axis)
    if count > 8:
        gathered = lax.all_gather(block, axis, axis=0, tiled=True)
        return gathered, lax.iota(jnp.int32, count)
    pieces = [block] + [
        lax.ppermute(block, axis, shifted_pairs(count, steps)) for steps in range(1, count)
    ]
    sources = (position - lax.iota(jnp.int32, count)) % count
    return jnp.concatenate(pieces, axis=0), sources


def scatter_slots(slots, axis):
    count = lax.axis_size(axis)
    if count > 8:
        return lax.psum_scatter(slots, axis, scatter_dimension=0, tiled=True)
    rows = slots.shape[0] // count
    total = slots[:rows]
    for steps in range(1, count):
        total = total + lax.ppermute(
            slots[steps * rows : (steps + 1) * rows].astype(jnp.bfloat16),
            axis,
            shifted_pairs(count, -steps),
        ).astype(jnp.float32)
    return total


def scatter_parts(own, sent, axis):
    count = lax.axis_size(axis)
    rows = own.shape[0]
    total = own
    for steps in range(1, count):
        total = total + lax.ppermute(
            sent[(steps - 1) * rows : steps * rows], axis, shifted_pairs(count, -steps)
        ).astype(jnp.float32)
    return total


def head_reduce(key_proj, value_proj, key_grad, value_grad):
    count = lax.axis_size("head")
    position = lax.axis_index("head")
    depth = count.bit_length() - 1
    contraction = (((1,), (1,)), ((), ()))
    if count == 1 or count != 1 << depth:
        partial = lax.dot_general(
            key_proj, key_grad, contraction, preferred_element_type=jnp.float32
        ) + lax.dot_general(value_proj, value_grad, contraction, preferred_element_type=jnp.float32)
        return lax.psum_scatter(partial, "head", scatter_dimension=0, tiled=True).astype(
            jnp.bfloat16
        )
    block = key_proj.shape[0] // count
    key_split = key_proj.reshape(count // 2, 2, block, key_proj.shape[1])
    value_split = value_proj.reshape(count // 2, 2, block, value_proj.shape[1])

    def project(half):
        return jnp.einsum(
            "arf,tf->art",
            lax.dynamic_index_in_dim(key_split, half, 1, keepdims=False),
            key_grad,
            preferred_element_type=jnp.float32,
        ) + jnp.einsum(
            "arf,tf->art",
            lax.dynamic_index_in_dim(value_split, half, 1, keepdims=False),
            value_grad,
            preferred_element_type=jnp.float32,
        )

    own_bit = position % 2
    sent = project(1 - own_bit)
    kept = project(own_bit)
    current = kept + lax.ppermute(sent, "head", [(i, i ^ 1) for i in range(count)])
    for level in range(1, depth):
        current = current.reshape(-1, 2, block, current.shape[-1])
        own_bit = (position // (1 << level)) % 2
        kept = lax.dynamic_index_in_dim(current, own_bit, 1, keepdims=False)
        sent = lax.dynamic_index_in_dim(current, 1 - own_bit, 1, keepdims=False)
        arrived = lax.ppermute(
            sent.astype(jnp.bfloat16), "head", [(i, i ^ (1 << level)) for i in range(count)]
        )
        current = kept + arrived.astype(jnp.float32)
    return current.reshape(block, -1).astype(jnp.bfloat16)


def attention_kernel(query_ref, grad_ref, kv_ref, mask_ref, query_out, own_out, sent_out):
    inv_root = HD ** (-0.5)
    kv_cols = kv_ref.shape[1] // 2
    kv_heads = kv_cols // HD
    rows = query_ref.shape[0]
    group_size = query_ref.shape[1] // kv_cols
    if mask_ref.shape[0] == 1:
        allowed = mask_ref[...] > 0
    else:
        allowed = jnp.concatenate([mask_ref[...]] * group_size, axis=0) > 0
    across = (((1,), (1,)), ((), ()))
    down = (((0,), (0,)), ((), ()))
    for kv_head in range(kv_heads):
        key_head = kv_ref[:, kv_head * HD : (kv_head + 1) * HD]
        value_head = kv_ref[:, kv_cols + kv_head * HD : kv_cols + (kv_head + 1) * HD]
        base = kv_head * group_size * HD
        query_stack = jnp.concatenate(
            [query_ref[:, base + m * HD : base + (m + 1) * HD] for m in range(group_size)], axis=0
        )
        grad_stack = jnp.concatenate(
            [grad_ref[:, base + m * HD : base + (m + 1) * HD] for m in range(group_size)], axis=0
        )
        scores = (
            lax.dot_general(query_stack, key_head, across, preferred_element_type=jnp.float32)
            * inv_root
        )
        scores = jnp.where(allowed, scores, masked_score)
        row_max = jnp.max(scores, axis=1, keepdims=True)
        shifted = jnp.exp(scores - row_max)
        row_sum = jnp.sum(shifted, axis=1, keepdims=True)
        weighted = jnp.dot(
            shifted.astype(jnp.bfloat16), value_head, preferred_element_type=jnp.float32
        )
        attended = (weighted / row_sum).astype(jnp.bfloat16)
        probs = shifted * (1.0 / row_sum)
        row_delta = jnp.sum(
            grad_stack.astype(jnp.float32) * attended.astype(jnp.float32), axis=1, keepdims=True
        )
        dprobs = lax.dot_general(grad_stack, value_head, across, preferred_element_type=jnp.float32)
        dscores = (probs * (dprobs - row_delta)).astype(jnp.bfloat16)
        query_term = jnp.dot(dscores, key_head, preferred_element_type=jnp.float32) * inv_root
        for m in range(group_size):
            query_out[:, base + m * HD : base + (m + 1) * HD] = query_term[
                m * rows : (m + 1) * rows
            ].astype(jnp.bfloat16)
        key_sum = lax.dot_general(dscores, query_stack, down, preferred_element_type=jnp.float32)
        value_sum = lax.dot_general(
            probs.astype(jnp.bfloat16), grad_stack, down, preferred_element_type=jnp.float32
        )
        key_sum = key_sum * inv_root
        key_cols = slice(kv_head * HD, (kv_head + 1) * HD)
        value_cols = slice(kv_cols + kv_head * HD, kv_cols + (kv_head + 1) * HD)
        own_out[:, key_cols] = key_sum[:rows]
        own_out[:, value_cols] = value_sum[:rows]
        sent_out[:, key_cols] = key_sum[rows:].astype(jnp.bfloat16)
        sent_out[:, value_cols] = value_sum[rows:].astype(jnp.bfloat16)


def attention_block(queries, out_grad, kv_rows, allowed, interpret=False):
    rows = queries.shape[0]
    return pl.pallas_call(
        attention_kernel,
        out_shape=(
            jax.ShapeDtypeStruct(queries.shape, jnp.bfloat16),
            jax.ShapeDtypeStruct((rows, kv_rows.shape[1]), jnp.float32),
            jax.ShapeDtypeStruct((kv_rows.shape[0] - rows, kv_rows.shape[1]), jnp.bfloat16),
        ),
        interpret=interpret,
    )(queries, out_grad, kv_rows, allowed.astype(jnp.int32))


def local(
    queries, key_states, value_states, out_grad, mask_flags, shard_blocks, key_proj, value_proj
):
    rows_here = queries.shape[0]
    kv_cols = key_states.shape[1]
    kv_heads = kv_cols // HD
    group_size = queries.shape[1] // kv_cols
    inv_root = HD ** (-0.5)
    position = lax.axis_index("ctx")
    query_heads = queries.reshape(rows_here, kv_heads, group_size, HD)
    grad_heads = out_grad.reshape(rows_here, kv_heads, group_size, HD)
    own_blocks = lax.dynamic_slice_in_dim(
        shard_blocks, position * (rows_here // BLK), rows_here // BLK
    )
    own_flags = select_rows(mask_flags, own_blocks)

    kv_rows, sources = gather_slots(
        jnp.concatenate([key_states, value_states], axis=1), "ctx"
    )
    row_count = kv_rows.shape[0]
    blocks_here = rows_here // BLK
    key_blocks = lax.iota(jnp.int32, row_count // BLK)
    key_doc_blocks = pick(
        shard_blocks,
        pick(sources, key_blocks // blocks_here) * blocks_here + key_blocks % blocks_here,
    )
    step_rows = math.gcd(row_count, 512)
    steps = row_count // step_rows

    def chunk(offset):
        block = lax.dynamic_slice_in_dim(kv_rows, offset, step_rows)
        key_heads = block[:, :kv_cols].reshape(step_rows, kv_heads, HD)
        value_heads = block[:, kv_cols:].reshape(step_rows, kv_heads, HD)
        their_blocks = lax.dynamic_slice_in_dim(key_doc_blocks, offset // BLK, step_rows // BLK)
        pair_flags = select_cols(own_flags, their_blocks) > 0
        allowed = jnp.repeat(jnp.repeat(pair_flags, BLK, axis=0), BLK, axis=1)
        scores = (
            jnp.einsum("qkgd,tkd->kgqt", query_heads, key_heads, preferred_element_type=jnp.float32)
            * inv_root
        )
        scores = jnp.where(allowed[None, None], scores, masked_score)
        return key_heads, value_heads, allowed, scores

    def forward_stats(offset, current):
        row_max, row_sum, weighted = current
        key_heads, value_heads, allowed, scores = chunk(offset)
        new_max = jnp.maximum(row_max, jnp.max(scores, axis=-1))
        rescale = jnp.exp(row_max - new_max)
        shifted = jnp.where(allowed[None, None], jnp.exp(scores - new_max[..., None]), 0.0)
        row_sum = row_sum * rescale + jnp.sum(shifted, axis=-1)
        weighted = weighted * rescale[..., None] + jnp.einsum(
            "kgqt,tkd->kgqd",
            shifted.astype(jnp.bfloat16),
            value_heads,
            preferred_element_type=jnp.float32,
        )
        return (new_max, row_sum, weighted)

    def backward_chunk(offset, log_total, row_delta, scores_given=None):
        key_heads, value_heads, allowed, scores = chunk(offset)
        if scores_given is not None:
            scores = scores_given
        probs = jnp.exp(scores - log_total[..., None])
        dprobs = jnp.einsum(
            "qkgd,tkd->kgqt", grad_heads, value_heads, preferred_element_type=jnp.float32
        )
        dscores = (probs * (dprobs - row_delta[..., None])).astype(jnp.bfloat16)
        probs_low = probs.astype(jnp.bfloat16)
        query_term = (
            jnp.einsum("kgqt,tkd->qkgd", dscores, key_heads, preferred_element_type=jnp.float32)
            * inv_root
        )
        key_term = (
            jnp.einsum("kgqt,qkgd->tkd", dscores, query_heads, preferred_element_type=jnp.float32)
            * inv_root
        )
        value_term = jnp.einsum(
            "kgqt,qkgd->tkd", probs_low, grad_heads, preferred_element_type=jnp.float32
        )
        kv_term = jnp.concatenate(
            [key_term.reshape(step_rows, kv_cols), value_term.reshape(step_rows, kv_cols)], axis=1
        )
        return query_term, kv_term

    if steps == 1 and lax.axis_size("ctx") <= 8:
        if rows_here == BLK:
            column_flags = select_cols(own_flags, key_doc_blocks) > 0
            allowed = jnp.repeat(column_flags, BLK, axis=1)
        else:
            allowed = chunk(0)[2]
        query_grad, own_part, sent_part = attention_block(queries, out_grad, kv_rows, allowed)
        kv_grad = scatter_parts(own_part, sent_part, "ctx")
    else:
        start_stats = (
            jnp.full((kv_heads, group_size, rows_here), masked_score, jnp.float32),
            jnp.zeros((kv_heads, group_size, rows_here), jnp.float32),
            jnp.zeros((kv_heads, group_size, rows_here, HD), jnp.float32),
        )
        row_max, row_sum, weighted = lax.fori_loop(
            0, steps, lambda i, c: forward_stats(i * step_rows, c), start_stats
        )
        log_total = row_max + jnp.log(row_sum)
        attended = (weighted / row_sum[..., None]).astype(jnp.bfloat16)
        row_delta = jnp.einsum(
            "kgqd,qkgd->kgq", attended, grad_heads, preferred_element_type=jnp.float32
        )

        def backward_visit(turn_index, current):
            query_now, kv_now = current
            offset = turn_index * step_rows
            query_term, kv_term = backward_chunk(offset, log_total, row_delta)
            kv_now = lax.dynamic_update_slice_in_dim(kv_now, kv_term, offset, 0)
            return (query_now + query_term, kv_now)

        query_acc, kv_acc = lax.fori_loop(
            0,
            steps,
            backward_visit,
            (
                jnp.zeros((rows_here, kv_heads, group_size, HD), jnp.float32),
                jnp.zeros((row_count, 2 * kv_cols), jnp.float32),
            ),
        )
        query_grad = query_acc.reshape(rows_here, -1).astype(jnp.bfloat16)
        kv_grad = scatter_slots(kv_acc, "ctx")

    key_grad = kv_grad[:, :kv_cols].astype(jnp.bfloat16)
    value_grad = kv_grad[:, kv_cols:].astype(jnp.bfloat16)
    input_grad_t = head_reduce(key_proj, value_proj, key_grad, value_grad)
    return (query_grad, key_grad, value_grad, input_grad_t)


def solution(mesh):
    return jax.shard_map(
        local,
        mesh=mesh,
        in_specs=(
            P(("groups", "ctx"), "head"),
            P(("groups", "ctx"), "head"),
            P(("groups", "ctx"), "head"),
            P(("groups", "ctx"), "head"),
            P("groups", None),
            P("groups"),
            P(None, "head"),
            P(None, "head"),
        ),
        out_specs=(
            P(("groups", "ctx"), "head"),
            P(("groups", "ctx"), "head"),
            P(("groups", "ctx"), "head"),
            P("head", ("groups", "ctx")),
        ),
        check_vma=False,
    )
```

```python
import math

import jax
import jax.numpy as jnp
from jax import lax
from jax.experimental import pallas as pl
from jax.sharding import PartitionSpec as P

HD = 128
BLK = 128


masked_score = -1e30


def select_rows(lookup, picked):
    onehot = (picked[:, None] == lax.iota(jnp.int32, lookup.shape[0])[None, :]).astype(jnp.int32)
    return jnp.sum(onehot[:, :, None] * lookup[None, :, :], axis=1)


def select_cols(lookup, picked):
    onehot = (picked[:, None] == lax.iota(jnp.int32, lookup.shape[1])[None, :]).astype(jnp.int32)
    return jnp.sum(lookup[:, None, :] * onehot[None, :, :], axis=2)


def pick(vector, picked):
    onehot = (picked[:, None] == lax.iota(jnp.int32, vector.shape[0])[None, :]).astype(jnp.int32)
    return jnp.sum(onehot * vector[None, :], axis=1)


def shifted_pairs(count, steps):
    return [(source, (source + steps) % count) for source in range(count)]


def gather_slots(block, axis):
    count = lax.axis_size(axis)
    position = lax.axis_index(axis)
    if count > 8:
        gathered = lax.all_gather(block, axis, axis=0, tiled=True)
        return gathered, lax.iota(jnp.int32, count)
    pieces = [block] + [
        lax.ppermute(block, axis, shifted_pairs(count, steps)) for steps in range(1, count)
    ]
    sources = (position - lax.iota(jnp.int32, count)) % count
    return jnp.concatenate(pieces, axis=0), sources


def scatter_slots(slots, axis):
    count = lax.axis_size(axis)
    if count > 8:
        return lax.psum_scatter(slots, axis, scatter_dimension=0, tiled=True)
    rows = slots.shape[0] // count
    total = slots[:rows]
    for steps in range(1, count):
        total = total + lax.ppermute(
            slots[steps * rows : (steps + 1) * rows].astype(jnp.bfloat16),
            axis,
            shifted_pairs(count, -steps),
        ).astype(jnp.float32)
    return total


def scatter_parts(own, sent, axis):
    count = lax.axis_size(axis)
    rows = own.shape[0]
    total = own
    for steps in range(1, count):
        total = total + lax.ppermute(
            sent[(steps - 1) * rows : steps * rows], axis, shifted_pairs(count, -steps)
        ).astype(jnp.float32)
    return total


def head_reduce(key_proj, value_proj, key_grad, value_grad):
    count = lax.axis_size("head")
    position = lax.axis_index("head")
    depth = count.bit_length() - 1
    contraction = (((1,), (1,)), ((), ()))
    if count == 1 or count != 1 << depth:
        partial = lax.dot_general(
            key_proj, key_grad, contraction, preferred_element_type=jnp.float32
        ) + lax.dot_general(value_proj, value_grad, contraction, preferred_element_type=jnp.float32)
        return lax.psum_scatter(partial, "head", scatter_dimension=0, tiled=True).astype(
            jnp.bfloat16
        )
    block = key_proj.shape[0] // count
    key_split = key_proj.reshape(count // 2, 2, block, key_proj.shape[1])
    value_split = value_proj.reshape(count // 2, 2, block, value_proj.shape[1])

    def project(half):
        return jnp.einsum(
            "arf,tf->art",
            lax.dynamic_index_in_dim(key_split, half, 1, keepdims=False),
            key_grad,
            preferred_element_type=jnp.float32,
        ) + jnp.einsum(
            "arf,tf->art",
            lax.dynamic_index_in_dim(value_split, half, 1, keepdims=False),
            value_grad,
            preferred_element_type=jnp.float32,
        )

    own_bit = position % 2
    sent = project(1 - own_bit)
    kept = project(own_bit)
    current = kept + lax.ppermute(
        sent.astype(jnp.bfloat16), "head", [(i, i ^ 1) for i in range(count)]
    ).astype(jnp.float32)
    for level in range(1, depth):
        current = current.reshape(-1, 2, block, current.shape[-1])
        own_bit = (position // (1 << level)) % 2
        kept = lax.dynamic_index_in_dim(current, own_bit, 1, keepdims=False)
        sent = lax.dynamic_index_in_dim(current, 1 - own_bit, 1, keepdims=False)
        arrived = lax.ppermute(
            sent.astype(jnp.bfloat16), "head", [(i, i ^ (1 << level)) for i in range(count)]
        )
        current = kept + arrived.astype(jnp.float32)
    return current.reshape(block, -1).astype(jnp.bfloat16)


def attention_kernel(query_ref, grad_ref, kv_ref, mask_ref, query_out, own_out, sent_out):
    inv_root = HD ** (-0.5)
    kv_cols = kv_ref.shape[1] // 2
    kv_heads = kv_cols // HD
    rows = query_ref.shape[0]
    group_size = query_ref.shape[1] // kv_cols
    if mask_ref.shape[0] == 1:
        allowed = mask_ref[...] > 0
    else:
        allowed = jnp.concatenate([mask_ref[...]] * group_size, axis=0) > 0
    across = (((1,), (1,)), ((), ()))
    down = (((0,), (0,)), ((), ()))
    for kv_head in range(kv_heads):
        key_head = kv_ref[:, kv_head * HD : (kv_head + 1) * HD]
        value_head = kv_ref[:, kv_cols + kv_head * HD : kv_cols + (kv_head + 1) * HD]
        base = kv_head * group_size * HD
        query_stack = jnp.concatenate(
            [query_ref[:, base + m * HD : base + (m + 1) * HD] for m in range(group_size)], axis=0
        )
        grad_stack = jnp.concatenate(
            [grad_ref[:, base + m * HD : base + (m + 1) * HD] for m in range(group_size)], axis=0
        )
        scores = (
            lax.dot_general(query_stack, key_head, across, preferred_element_type=jnp.float32)
            * inv_root
        )
        scores = jnp.where(allowed, scores, masked_score)
        row_max = jnp.max(scores, axis=1, keepdims=True)
        shifted = jnp.exp(scores - row_max)
        row_sum = jnp.sum(shifted, axis=1, keepdims=True)
        weighted = jnp.dot(
            shifted.astype(jnp.bfloat16), value_head, preferred_element_type=jnp.float32
        )
        attended = (weighted / row_sum).astype(jnp.bfloat16)
        probs = shifted * (1.0 / row_sum)
        row_delta = jnp.sum(
            grad_stack.astype(jnp.float32) * attended.astype(jnp.float32), axis=1, keepdims=True
        )
        dprobs = lax.dot_general(grad_stack, value_head, across, preferred_element_type=jnp.float32)
        dscores = (probs * (dprobs - row_delta)).astype(jnp.bfloat16)
        query_term = jnp.dot(dscores, key_head, preferred_element_type=jnp.float32) * inv_root
        for m in range(group_size):
            query_out[:, base + m * HD : base + (m + 1) * HD] = query_term[
                m * rows : (m + 1) * rows
            ].astype(jnp.bfloat16)
        key_sum = lax.dot_general(dscores, query_stack, down, preferred_element_type=jnp.float32)
        value_sum = lax.dot_general(
            probs.astype(jnp.bfloat16), grad_stack, down, preferred_element_type=jnp.float32
        )
        key_sum = key_sum * inv_root
        key_cols = slice(kv_head * HD, (kv_head + 1) * HD)
        value_cols = slice(kv_cols + kv_head * HD, kv_cols + (kv_head + 1) * HD)
        own_out[:, key_cols] = key_sum[:rows]
        own_out[:, value_cols] = value_sum[:rows]
        sent_out[:, key_cols] = key_sum[rows:].astype(jnp.bfloat16)
        sent_out[:, value_cols] = value_sum[rows:].astype(jnp.bfloat16)


def attention_block(queries, out_grad, kv_rows, allowed, interpret=False):
    rows = queries.shape[0]
    return pl.pallas_call(
        attention_kernel,
        out_shape=(
            jax.ShapeDtypeStruct(queries.shape, jnp.bfloat16),
            jax.ShapeDtypeStruct((rows, kv_rows.shape[1]), jnp.float32),
            jax.ShapeDtypeStruct((kv_rows.shape[0] - rows, kv_rows.shape[1]), jnp.bfloat16),
        ),
        interpret=interpret,
    )(queries, out_grad, kv_rows, allowed.astype(jnp.int32))


def local(
    queries, key_states, value_states, out_grad, mask_flags, shard_blocks, key_proj, value_proj
):
    rows_here = queries.shape[0]
    kv_cols = key_states.shape[1]
    kv_heads = kv_cols // HD
    group_size = queries.shape[1] // kv_cols
    inv_root = HD ** (-0.5)
    position = lax.axis_index("ctx")
    query_heads = queries.reshape(rows_here, kv_heads, group_size, HD)
    grad_heads = out_grad.reshape(rows_here, kv_heads, group_size, HD)
    own_blocks = lax.dynamic_slice_in_dim(
        shard_blocks, position * (rows_here // BLK), rows_here // BLK
    )
    own_flags = select_rows(mask_flags, own_blocks)

    kv_rows, sources = gather_slots(
        jnp.concatenate([key_states, value_states], axis=1), "ctx"
    )
    row_count = kv_rows.shape[0]
    blocks_here = rows_here // BLK
    key_blocks = lax.iota(jnp.int32, row_count // BLK)
    key_doc_blocks = pick(
        shard_blocks,
        pick(sources, key_blocks // blocks_here) * blocks_here + key_blocks % blocks_here,
    )
    step_rows = math.gcd(row_count, 512)
    steps = row_count // step_rows

    def chunk(offset):
        block = lax.dynamic_slice_in_dim(kv_rows, offset, step_rows)
        key_heads = block[:, :kv_cols].reshape(step_rows, kv_heads, HD)
        value_heads = block[:, kv_cols:].reshape(step_rows, kv_heads, HD)
        their_blocks = lax.dynamic_slice_in_dim(key_doc_blocks, offset // BLK, step_rows // BLK)
        pair_flags = select_cols(own_flags, their_blocks) > 0
        allowed = jnp.repeat(jnp.repeat(pair_flags, BLK, axis=0), BLK, axis=1)
        scores = (
            jnp.einsum("qkgd,tkd->kgqt", query_heads, key_heads, preferred_element_type=jnp.float32)
            * inv_root
        )
        scores = jnp.where(allowed[None, None], scores, masked_score)
        return key_heads, value_heads, allowed, scores

    def forward_stats(offset, current):
        row_max, row_sum, weighted = current
        key_heads, value_heads, allowed, scores = chunk(offset)
        new_max = jnp.maximum(row_max, jnp.max(scores, axis=-1))
        rescale = jnp.exp(row_max - new_max)
        shifted = jnp.where(allowed[None, None], jnp.exp(scores - new_max[..., None]), 0.0)
        row_sum = row_sum * rescale + jnp.sum(shifted, axis=-1)
        weighted = weighted * rescale[..., None] + jnp.einsum(
            "kgqt,tkd->kgqd",
            shifted.astype(jnp.bfloat16),
            value_heads,
            preferred_element_type=jnp.float32,
        )
        return (new_max, row_sum, weighted)

    def backward_chunk(offset, log_total, row_delta, scores_given=None):
        key_heads, value_heads, allowed, scores = chunk(offset)
        if scores_given is not None:
            scores = scores_given
        probs = jnp.exp(scores - log_total[..., None])
        dprobs = jnp.einsum(
            "qkgd,tkd->kgqt", grad_heads, value_heads, preferred_element_type=jnp.float32
        )
        dscores = (probs * (dprobs - row_delta[..., None])).astype(jnp.bfloat16)
        probs_low = probs.astype(jnp.bfloat16)
        query_term = (
            jnp.einsum("kgqt,tkd->qkgd", dscores, key_heads, preferred_element_type=jnp.float32)
            * inv_root
        )
        key_term = (
            jnp.einsum("kgqt,qkgd->tkd", dscores, query_heads, preferred_element_type=jnp.float32)
            * inv_root
        )
        value_term = jnp.einsum(
            "kgqt,qkgd->tkd", probs_low, grad_heads, preferred_element_type=jnp.float32
        )
        kv_term = jnp.concatenate(
            [key_term.reshape(step_rows, kv_cols), value_term.reshape(step_rows, kv_cols)], axis=1
        )
        return query_term, kv_term

    if steps == 1 and lax.axis_size("ctx") <= 8:
        if rows_here == BLK:
            column_flags = select_cols(own_flags, key_doc_blocks) > 0
            allowed = jnp.repeat(column_flags, BLK, axis=1)
        else:
            allowed = chunk(0)[2]
        query_grad, own_part, sent_part = attention_block(queries, out_grad, kv_rows, allowed)
        kv_grad = scatter_parts(own_part, sent_part, "ctx")
    else:
        start_stats = (
            jnp.full((kv_heads, group_size, rows_here), masked_score, jnp.float32),
            jnp.zeros((kv_heads, group_size, rows_here), jnp.float32),
            jnp.zeros((kv_heads, group_size, rows_here, HD), jnp.float32),
        )
        row_max, row_sum, weighted = lax.fori_loop(
            0, steps, lambda i, c: forward_stats(i * step_rows, c), start_stats
        )
        log_total = row_max + jnp.log(row_sum)
        attended = (weighted / row_sum[..., None]).astype(jnp.bfloat16)
        row_delta = jnp.einsum(
            "kgqd,qkgd->kgq", attended, grad_heads, preferred_element_type=jnp.float32
        )

        def backward_visit(turn_index, current):
            query_now, kv_now = current
            offset = turn_index * step_rows
            query_term, kv_term = backward_chunk(offset, log_total, row_delta)
            kv_now = lax.dynamic_update_slice_in_dim(kv_now, kv_term, offset, 0)
            return (query_now + query_term, kv_now)

        query_acc, kv_acc = lax.fori_loop(
            0,
            steps,
            backward_visit,
            (
                jnp.zeros((rows_here, kv_heads, group_size, HD), jnp.float32),
                jnp.zeros((row_count, 2 * kv_cols), jnp.float32),
            ),
        )
        query_grad = query_acc.reshape(rows_here, -1).astype(jnp.bfloat16)
        kv_grad = scatter_slots(kv_acc, "ctx")

    key_grad = kv_grad[:, :kv_cols].astype(jnp.bfloat16)
    value_grad = kv_grad[:, kv_cols:].astype(jnp.bfloat16)
    input_grad_t = head_reduce(key_proj, value_proj, key_grad, value_grad)
    return (query_grad, key_grad, value_grad, input_grad_t)


def solution(mesh):
    return jax.shard_map(
        local,
        mesh=mesh,
        in_specs=(
            P(("groups", "ctx"), "head"),
            P(("groups", "ctx"), "head"),
            P(("groups", "ctx"), "head"),
            P(("groups", "ctx"), "head"),
            P("groups", None),
            P("groups"),
            P(None, "head"),
            P(None, "head"),
        ),
        out_specs=(
            P(("groups", "ctx"), "head"),
            P(("groups", "ctx"), "head"),
            P(("groups", "ctx"), "head"),
            P("head", ("groups", "ctx")),
        ),
        check_vma=False,
    )
```

```python
import math

import jax
import jax.numpy as jnp
from jax import lax
from jax.experimental import pallas as pl
from jax.sharding import PartitionSpec as P

HD = 128
BLK = 128


masked_score = -1e30


def select_rows(lookup, picked):
    onehot = (picked[:, None] == lax.iota(jnp.int32, lookup.shape[0])[None, :]).astype(jnp.int32)
    return jnp.sum(onehot[:, :, None] * lookup[None, :, :], axis=1)


def select_cols(lookup, picked):
    onehot = (picked[:, None] == lax.iota(jnp.int32, lookup.shape[1])[None, :]).astype(jnp.int32)
    return jnp.sum(lookup[:, None, :] * onehot[None, :, :], axis=2)


def pick(vector, picked):
    onehot = (picked[:, None] == lax.iota(jnp.int32, vector.shape[0])[None, :]).astype(jnp.int32)
    return jnp.sum(onehot * vector[None, :], axis=1)


def shifted_pairs(count, steps):
    return [(source, (source + steps) % count) for source in range(count)]


def gather_slots(block, axis):
    count = lax.axis_size(axis)
    position = lax.axis_index(axis)
    if count > 8:
        gathered = lax.all_gather(block, axis, axis=0, tiled=True)
        return gathered, lax.iota(jnp.int32, count)
    pieces = [block] + [
        lax.ppermute(block, axis, shifted_pairs(count, steps)) for steps in range(1, count)
    ]
    sources = (position - lax.iota(jnp.int32, count)) % count
    return jnp.concatenate(pieces, axis=0), sources


def scatter_slots(slots, axis):
    count = lax.axis_size(axis)
    if count > 8:
        return lax.psum_scatter(slots, axis, scatter_dimension=0, tiled=True)
    rows = slots.shape[0] // count
    total = slots[:rows]
    for steps in range(1, count):
        total = total + lax.ppermute(
            slots[steps * rows : (steps + 1) * rows].astype(jnp.bfloat16),
            axis,
            shifted_pairs(count, -steps),
        ).astype(jnp.float32)
    return total


def scatter_parts(own, sent, axis):
    count = lax.axis_size(axis)
    position = lax.axis_index(axis)
    rows = own.shape[0]
    slots = jnp.concatenate([jnp.zeros(own.shape, jnp.bfloat16), sent], axis=0).reshape(
        count, rows, -1
    )
    by_device = jnp.take(slots, (position - lax.iota(jnp.int32, count)) % count, axis=0)
    arrived = lax.all_to_all(by_device, axis, 0, 0, tiled=True)
    return own + jnp.sum(arrived.astype(jnp.float32), axis=0)


def head_reduce(key_proj, value_proj, key_grad, value_grad):
    count = lax.axis_size("head")
    position = lax.axis_index("head")
    depth = count.bit_length() - 1
    contraction = (((1,), (1,)), ((), ()))
    if count == 1 or count != 1 << depth:
        partial = lax.dot_general(
            key_proj, key_grad, contraction, preferred_element_type=jnp.float32
        ) + lax.dot_general(value_proj, value_grad, contraction, preferred_element_type=jnp.float32)
        return lax.psum_scatter(partial, "head", scatter_dimension=0, tiled=True).astype(
            jnp.bfloat16
        )
    block = key_proj.shape[0] // count
    key_split = key_proj.reshape(count // 2, 2, block, key_proj.shape[1])
    value_split = value_proj.reshape(count // 2, 2, block, value_proj.shape[1])

    def project(half):
        return jnp.einsum(
            "arf,tf->art",
            lax.dynamic_index_in_dim(key_split, half, 1, keepdims=False),
            key_grad,
            preferred_element_type=jnp.float32,
        ) + jnp.einsum(
            "arf,tf->art",
            lax.dynamic_index_in_dim(value_split, half, 1, keepdims=False),
            value_grad,
            preferred_element_type=jnp.float32,
        )

    own_bit = position % 2
    sent = project(1 - own_bit)
    kept = project(own_bit)
    current = kept + lax.ppermute(
        sent.astype(jnp.bfloat16), "head", [(i, i ^ 1) for i in range(count)]
    ).astype(jnp.float32)
    for level in range(1, depth):
        current = current.reshape(-1, 2, block, current.shape[-1])
        own_bit = (position // (1 << level)) % 2
        kept = lax.dynamic_index_in_dim(current, own_bit, 1, keepdims=False)
        sent = lax.dynamic_index_in_dim(current, 1 - own_bit, 1, keepdims=False)
        arrived = lax.ppermute(
            sent.astype(jnp.bfloat16), "head", [(i, i ^ (1 << level)) for i in range(count)]
        )
        current = kept + arrived.astype(jnp.float32)
    return current.reshape(block, -1).astype(jnp.bfloat16)


def attention_kernel(query_ref, grad_ref, kv_ref, mask_ref, query_out, own_out, sent_out):
    inv_root = HD ** (-0.5)
    kv_cols = kv_ref.shape[1] // 2
    kv_heads = kv_cols // HD
    rows = query_ref.shape[0]
    group_size = query_ref.shape[1] // kv_cols
    if mask_ref.shape[0] == 1:
        allowed = mask_ref[...] > 0
    else:
        allowed = jnp.concatenate([mask_ref[...]] * group_size, axis=0) > 0
    across = (((1,), (1,)), ((), ()))
    down = (((0,), (0,)), ((), ()))
    for kv_head in range(kv_heads):
        key_head = kv_ref[:, kv_head * HD : (kv_head + 1) * HD]
        value_head = kv_ref[:, kv_cols + kv_head * HD : kv_cols + (kv_head + 1) * HD]
        base = kv_head * group_size * HD
        query_stack = jnp.concatenate(
            [query_ref[:, base + m * HD : base + (m + 1) * HD] for m in range(group_size)], axis=0
        )
        grad_stack = jnp.concatenate(
            [grad_ref[:, base + m * HD : base + (m + 1) * HD] for m in range(group_size)], axis=0
        )
        scores = (
            lax.dot_general(query_stack, key_head, across, preferred_element_type=jnp.float32)
            * inv_root
        )
        scores = jnp.where(allowed, scores, masked_score)
        row_max = jnp.max(scores, axis=1, keepdims=True)
        shifted = jnp.exp(scores - row_max)
        row_sum = jnp.sum(shifted, axis=1, keepdims=True)
        weighted = jnp.dot(
            shifted.astype(jnp.bfloat16), value_head, preferred_element_type=jnp.float32
        )
        attended = (weighted / row_sum).astype(jnp.bfloat16)
        probs = shifted * (1.0 / row_sum)
        row_delta = jnp.sum(
            grad_stack.astype(jnp.float32) * attended.astype(jnp.float32), axis=1, keepdims=True
        )
        dprobs = lax.dot_general(grad_stack, value_head, across, preferred_element_type=jnp.float32)
        dscores = (probs * (dprobs - row_delta)).astype(jnp.bfloat16)
        query_term = jnp.dot(dscores, key_head, preferred_element_type=jnp.float32) * inv_root
        for m in range(group_size):
            query_out[:, base + m * HD : base + (m + 1) * HD] = query_term[
                m * rows : (m + 1) * rows
            ].astype(jnp.bfloat16)
        key_sum = lax.dot_general(dscores, query_stack, down, preferred_element_type=jnp.float32)
        value_sum = lax.dot_general(
            probs.astype(jnp.bfloat16), grad_stack, down, preferred_element_type=jnp.float32
        )
        key_sum = key_sum * inv_root
        key_cols = slice(kv_head * HD, (kv_head + 1) * HD)
        value_cols = slice(kv_cols + kv_head * HD, kv_cols + (kv_head + 1) * HD)
        own_out[:, key_cols] = key_sum[:rows]
        own_out[:, value_cols] = value_sum[:rows]
        sent_out[:, key_cols] = key_sum[rows:].astype(jnp.bfloat16)
        sent_out[:, value_cols] = value_sum[rows:].astype(jnp.bfloat16)


def attention_block(queries, out_grad, kv_rows, allowed, interpret=False):
    rows = queries.shape[0]
    return pl.pallas_call(
        attention_kernel,
        out_shape=(
            jax.ShapeDtypeStruct(queries.shape, jnp.bfloat16),
            jax.ShapeDtypeStruct((rows, kv_rows.shape[1]), jnp.float32),
            jax.ShapeDtypeStruct((kv_rows.shape[0] - rows, kv_rows.shape[1]), jnp.bfloat16),
        ),
        interpret=interpret,
    )(queries, out_grad, kv_rows, allowed.astype(jnp.int32))


def local(
    queries, key_states, value_states, out_grad, mask_flags, shard_blocks, key_proj, value_proj
):
    rows_here = queries.shape[0]
    kv_cols = key_states.shape[1]
    kv_heads = kv_cols // HD
    group_size = queries.shape[1] // kv_cols
    inv_root = HD ** (-0.5)
    position = lax.axis_index("ctx")
    query_heads = queries.reshape(rows_here, kv_heads, group_size, HD)
    grad_heads = out_grad.reshape(rows_here, kv_heads, group_size, HD)
    own_blocks = lax.dynamic_slice_in_dim(
        shard_blocks, position * (rows_here // BLK), rows_here // BLK
    )
    own_flags = select_rows(mask_flags, own_blocks)

    kv_rows, sources = gather_slots(
        jnp.concatenate([key_states, value_states], axis=1), "ctx"
    )
    row_count = kv_rows.shape[0]
    blocks_here = rows_here // BLK
    key_blocks = lax.iota(jnp.int32, row_count // BLK)
    key_doc_blocks = pick(
        shard_blocks,
        pick(sources, key_blocks // blocks_here) * blocks_here + key_blocks % blocks_here,
    )
    step_rows = math.gcd(row_count, 512)
    steps = row_count // step_rows

    def chunk(offset):
        block = lax.dynamic_slice_in_dim(kv_rows, offset, step_rows)
        key_heads = block[:, :kv_cols].reshape(step_rows, kv_heads, HD)
        value_heads = block[:, kv_cols:].reshape(step_rows, kv_heads, HD)
        their_blocks = lax.dynamic_slice_in_dim(key_doc_blocks, offset // BLK, step_rows // BLK)
        pair_flags = select_cols(own_flags, their_blocks) > 0
        allowed = jnp.repeat(jnp.repeat(pair_flags, BLK, axis=0), BLK, axis=1)
        scores = (
            jnp.einsum("qkgd,tkd->kgqt", query_heads, key_heads, preferred_element_type=jnp.float32)
            * inv_root
        )
        scores = jnp.where(allowed[None, None], scores, masked_score)
        return key_heads, value_heads, allowed, scores

    def forward_stats(offset, current):
        row_max, row_sum, weighted = current
        key_heads, value_heads, allowed, scores = chunk(offset)
        new_max = jnp.maximum(row_max, jnp.max(scores, axis=-1))
        rescale = jnp.exp(row_max - new_max)
        shifted = jnp.where(allowed[None, None], jnp.exp(scores - new_max[..., None]), 0.0)
        row_sum = row_sum * rescale + jnp.sum(shifted, axis=-1)
        weighted = weighted * rescale[..., None] + jnp.einsum(
            "kgqt,tkd->kgqd",
            shifted.astype(jnp.bfloat16),
            value_heads,
            preferred_element_type=jnp.float32,
        )
        return (new_max, row_sum, weighted)

    def backward_chunk(offset, log_total, row_delta, scores_given=None):
        key_heads, value_heads, allowed, scores = chunk(offset)
        if scores_given is not None:
            scores = scores_given
        probs = jnp.exp(scores - log_total[..., None])
        dprobs = jnp.einsum(
            "qkgd,tkd->kgqt", grad_heads, value_heads, preferred_element_type=jnp.float32
        )
        dscores = (probs * (dprobs - row_delta[..., None])).astype(jnp.bfloat16)
        probs_low = probs.astype(jnp.bfloat16)
        query_term = (
            jnp.einsum("kgqt,tkd->qkgd", dscores, key_heads, preferred_element_type=jnp.float32)
            * inv_root
        )
        key_term = (
            jnp.einsum("kgqt,qkgd->tkd", dscores, query_heads, preferred_element_type=jnp.float32)
            * inv_root
        )
        value_term = jnp.einsum(
            "kgqt,qkgd->tkd", probs_low, grad_heads, preferred_element_type=jnp.float32
        )
        kv_term = jnp.concatenate(
            [key_term.reshape(step_rows, kv_cols), value_term.reshape(step_rows, kv_cols)], axis=1
        )
        return query_term, kv_term

    if steps == 1 and lax.axis_size("ctx") <= 8:
        if rows_here == BLK:
            column_flags = select_cols(own_flags, key_doc_blocks) > 0
            allowed = jnp.repeat(column_flags, BLK, axis=1)
        else:
            allowed = chunk(0)[2]
        query_grad, own_part, sent_part = attention_block(queries, out_grad, kv_rows, allowed)
        kv_grad = scatter_parts(own_part, sent_part, "ctx")
    else:
        start_stats = (
            jnp.full((kv_heads, group_size, rows_here), masked_score, jnp.float32),
            jnp.zeros((kv_heads, group_size, rows_here), jnp.float32),
            jnp.zeros((kv_heads, group_size, rows_here, HD), jnp.float32),
        )
        row_max, row_sum, weighted = lax.fori_loop(
            0, steps, lambda i, c: forward_stats(i * step_rows, c), start_stats
        )
        log_total = row_max + jnp.log(row_sum)
        attended = (weighted / row_sum[..., None]).astype(jnp.bfloat16)
        row_delta = jnp.einsum(
            "kgqd,qkgd->kgq", attended, grad_heads, preferred_element_type=jnp.float32
        )

        def backward_visit(turn_index, current):
            query_now, kv_now = current
            offset = turn_index * step_rows
            query_term, kv_term = backward_chunk(offset, log_total, row_delta)
            kv_now = lax.dynamic_update_slice_in_dim(kv_now, kv_term, offset, 0)
            return (query_now + query_term, kv_now)

        query_acc, kv_acc = lax.fori_loop(
            0,
            steps,
            backward_visit,
            (
                jnp.zeros((rows_here, kv_heads, group_size, HD), jnp.float32),
                jnp.zeros((row_count, 2 * kv_cols), jnp.float32),
            ),
        )
        query_grad = query_acc.reshape(rows_here, -1).astype(jnp.bfloat16)
        kv_grad = scatter_slots(kv_acc, "ctx")

    key_grad = kv_grad[:, :kv_cols].astype(jnp.bfloat16)
    value_grad = kv_grad[:, kv_cols:].astype(jnp.bfloat16)
    input_grad_t = head_reduce(key_proj, value_proj, key_grad, value_grad)
    return (query_grad, key_grad, value_grad, input_grad_t)


def solution(mesh):
    return jax.shard_map(
        local,
        mesh=mesh,
        in_specs=(
            P(("groups", "ctx"), "head"),
            P(("groups", "ctx"), "head"),
            P(("groups", "ctx"), "head"),
            P(("groups", "ctx"), "head"),
            P("groups", None),
            P("groups"),
            P(None, "head"),
            P(None, "head"),
        ),
        out_specs=(
            P(("groups", "ctx"), "head"),
            P(("groups", "ctx"), "head"),
            P(("groups", "ctx"), "head"),
            P("head", ("groups", "ctx")),
        ),
        check_vma=False,
    )
```

```python
import math

import jax
import jax.numpy as jnp
from jax import lax
from jax.experimental import pallas as pl
from jax.experimental.pallas import tpu as pltpu
from jax.sharding import PartitionSpec as P

HD = 128
BLK = 128


masked_score = -1e30


def select_rows(lookup, picked):
    onehot = (picked[:, None] == lax.iota(jnp.int32, lookup.shape[0])[None, :]).astype(jnp.int32)
    return jnp.sum(onehot[:, :, None] * lookup[None, :, :], axis=1)


def select_cols(lookup, picked):
    onehot = (picked[:, None] == lax.iota(jnp.int32, lookup.shape[1])[None, :]).astype(jnp.int32)
    return jnp.sum(lookup[:, None, :] * onehot[None, :, :], axis=2)


def pick(vector, picked):
    onehot = (picked[:, None] == lax.iota(jnp.int32, vector.shape[0])[None, :]).astype(jnp.int32)
    return jnp.sum(onehot * vector[None, :], axis=1)


def shifted_pairs(count, steps):
    return [(source, (source + steps) % count) for source in range(count)]


def gather_slots(block, axis):
    count = lax.axis_size(axis)
    position = lax.axis_index(axis)
    if count > 8:
        gathered = lax.all_gather(block, axis, axis=0, tiled=True)
        return gathered, lax.iota(jnp.int32, count)
    pieces = [block] + [
        lax.ppermute(block, axis, shifted_pairs(count, steps)) for steps in range(1, count)
    ]
    sources = (position - lax.iota(jnp.int32, count)) % count
    return jnp.concatenate(pieces, axis=0), sources


def scatter_slots(slots, axis):
    count = lax.axis_size(axis)
    if count > 8:
        return lax.psum_scatter(slots, axis, scatter_dimension=0, tiled=True)
    rows = slots.shape[0] // count
    total = slots[:rows]
    for steps in range(1, count):
        total = total + lax.ppermute(
            slots[steps * rows : (steps + 1) * rows].astype(jnp.bfloat16),
            axis,
            shifted_pairs(count, -steps),
        ).astype(jnp.float32)
    return total


def scatter_parts(own, sent, axis):
    count = lax.axis_size(axis)
    rows = own.shape[0]
    total = own
    for steps in range(1, count):
        total = total + lax.ppermute(
            sent[(steps - 1) * rows : steps * rows], axis, shifted_pairs(count, -steps)
        ).astype(jnp.float32)
    return total


def copy_to_vmem(source, target):
    pltpu.sync_copy(source, target)


def staged(weights):
    return pl.pallas_call(
        copy_to_vmem,
        out_shape=jax.ShapeDtypeStruct(weights.shape, weights.dtype),
        in_specs=[pl.BlockSpec(memory_space=pl.ANY)],
        out_specs=pl.BlockSpec(memory_space=pltpu.VMEM),
    )(weights)


def head_reduce(key_proj, value_proj, key_grad, value_grad):
    count = lax.axis_size("head")
    position = lax.axis_index("head")
    depth = count.bit_length() - 1
    contraction = (((1,), (1,)), ((), ()))
    if count == 1 or count != 1 << depth:
        partial = lax.dot_general(
            key_proj, key_grad, contraction, preferred_element_type=jnp.float32
        ) + lax.dot_general(value_proj, value_grad, contraction, preferred_element_type=jnp.float32)
        return lax.psum_scatter(partial, "head", scatter_dimension=0, tiled=True).astype(
            jnp.bfloat16
        )
    block = key_proj.shape[0] // count
    key_proj = staged(key_proj)
    value_proj = staged(value_proj)
    key_split = key_proj.reshape(count // 2, 2, block, key_proj.shape[1])
    value_split = value_proj.reshape(count // 2, 2, block, value_proj.shape[1])

    def project(half):
        return jnp.einsum(
            "arf,tf->art",
            lax.dynamic_index_in_dim(key_split, half, 1, keepdims=False),
            key_grad,
            preferred_element_type=jnp.float32,
        ) + jnp.einsum(
            "arf,tf->art",
            lax.dynamic_index_in_dim(value_split, half, 1, keepdims=False),
            value_grad,
            preferred_element_type=jnp.float32,
        )

    own_bit = position % 2
    sent = project(1 - own_bit)
    kept = project(own_bit)
    current = kept + lax.ppermute(
        sent.astype(jnp.bfloat16), "head", [(i, i ^ 1) for i in range(count)]
    ).astype(jnp.float32)
    for level in range(1, depth):
        current = current.reshape(-1, 2, block, current.shape[-1])
        own_bit = (position // (1 << level)) % 2
        kept = lax.dynamic_index_in_dim(current, own_bit, 1, keepdims=False)
        sent = lax.dynamic_index_in_dim(current, 1 - own_bit, 1, keepdims=False)
        arrived = lax.ppermute(
            sent.astype(jnp.bfloat16), "head", [(i, i ^ (1 << level)) for i in range(count)]
        )
        current = kept + arrived.astype(jnp.float32)
    return current.reshape(block, -1).astype(jnp.bfloat16)


def attention_kernel(query_ref, grad_ref, kv_ref, mask_ref, query_out, own_out, sent_out):
    inv_root = HD ** (-0.5)
    kv_cols = kv_ref.shape[1] // 2
    kv_heads = kv_cols // HD
    rows = query_ref.shape[0]
    group_size = query_ref.shape[1] // kv_cols
    if mask_ref.shape[0] == 1:
        allowed = mask_ref[...] > 0
    else:
        allowed = jnp.concatenate([mask_ref[...]] * group_size, axis=0) > 0
    across = (((1,), (1,)), ((), ()))
    down = (((0,), (0,)), ((), ()))
    for kv_head in range(kv_heads):
        key_head = kv_ref[:, kv_head * HD : (kv_head + 1) * HD]
        value_head = kv_ref[:, kv_cols + kv_head * HD : kv_cols + (kv_head + 1) * HD]
        base = kv_head * group_size * HD
        query_stack = jnp.concatenate(
            [query_ref[:, base + m * HD : base + (m + 1) * HD] for m in range(group_size)], axis=0
        )
        grad_stack = jnp.concatenate(
            [grad_ref[:, base + m * HD : base + (m + 1) * HD] for m in range(group_size)], axis=0
        )
        scores = (
            lax.dot_general(query_stack, key_head, across, preferred_element_type=jnp.float32)
            * inv_root
        )
        scores = jnp.where(allowed, scores, masked_score)
        row_max = jnp.max(scores, axis=1, keepdims=True)
        shifted = jnp.exp(scores - row_max)
        row_sum = jnp.sum(shifted, axis=1, keepdims=True)
        weighted = jnp.dot(
            shifted.astype(jnp.bfloat16), value_head, preferred_element_type=jnp.float32
        )
        attended = (weighted / row_sum).astype(jnp.bfloat16)
        probs = shifted * (1.0 / row_sum)
        row_delta = jnp.sum(
            grad_stack.astype(jnp.float32) * attended.astype(jnp.float32), axis=1, keepdims=True
        )
        dprobs = lax.dot_general(grad_stack, value_head, across, preferred_element_type=jnp.float32)
        dscores = (probs * (dprobs - row_delta)).astype(jnp.bfloat16)
        query_term = jnp.dot(dscores, key_head, preferred_element_type=jnp.float32) * inv_root
        for m in range(group_size):
            query_out[:, base + m * HD : base + (m + 1) * HD] = query_term[
                m * rows : (m + 1) * rows
            ].astype(jnp.bfloat16)
        key_sum = lax.dot_general(dscores, query_stack, down, preferred_element_type=jnp.float32)
        value_sum = lax.dot_general(
            probs.astype(jnp.bfloat16), grad_stack, down, preferred_element_type=jnp.float32
        )
        key_sum = key_sum * inv_root
        key_cols = slice(kv_head * HD, (kv_head + 1) * HD)
        value_cols = slice(kv_cols + kv_head * HD, kv_cols + (kv_head + 1) * HD)
        own_out[:, key_cols] = key_sum[:rows]
        own_out[:, value_cols] = value_sum[:rows]
        sent_out[:, key_cols] = key_sum[rows:].astype(jnp.bfloat16)
        sent_out[:, value_cols] = value_sum[rows:].astype(jnp.bfloat16)


def attention_block(queries, out_grad, kv_rows, allowed, interpret=False):
    rows = queries.shape[0]
    return pl.pallas_call(
        attention_kernel,
        out_shape=(
            jax.ShapeDtypeStruct(queries.shape, jnp.bfloat16),
            jax.ShapeDtypeStruct((rows, kv_rows.shape[1]), jnp.float32),
            jax.ShapeDtypeStruct((kv_rows.shape[0] - rows, kv_rows.shape[1]), jnp.bfloat16),
        ),
        interpret=interpret,
    )(queries, out_grad, kv_rows, allowed.astype(jnp.int32))


def local(
    queries, key_states, value_states, out_grad, mask_flags, shard_blocks, key_proj, value_proj
):
    rows_here = queries.shape[0]
    kv_cols = key_states.shape[1]
    kv_heads = kv_cols // HD
    group_size = queries.shape[1] // kv_cols
    inv_root = HD ** (-0.5)
    position = lax.axis_index("ctx")
    query_heads = queries.reshape(rows_here, kv_heads, group_size, HD)
    grad_heads = out_grad.reshape(rows_here, kv_heads, group_size, HD)
    own_blocks = lax.dynamic_slice_in_dim(
        shard_blocks, position * (rows_here // BLK), rows_here // BLK
    )
    own_flags = select_rows(mask_flags, own_blocks)

    kv_rows, sources = gather_slots(
        jnp.concatenate([key_states, value_states], axis=1), "ctx"
    )
    row_count = kv_rows.shape[0]
    blocks_here = rows_here // BLK
    key_blocks = lax.iota(jnp.int32, row_count // BLK)
    key_doc_blocks = pick(
        shard_blocks,
        pick(sources, key_blocks // blocks_here) * blocks_here + key_blocks % blocks_here,
    )
    step_rows = math.gcd(row_count, 512)
    steps = row_count // step_rows

    def chunk(offset):
        block = lax.dynamic_slice_in_dim(kv_rows, offset, step_rows)
        key_heads = block[:, :kv_cols].reshape(step_rows, kv_heads, HD)
        value_heads = block[:, kv_cols:].reshape(step_rows, kv_heads, HD)
        their_blocks = lax.dynamic_slice_in_dim(key_doc_blocks, offset // BLK, step_rows // BLK)
        pair_flags = select_cols(own_flags, their_blocks) > 0
        allowed = jnp.repeat(jnp.repeat(pair_flags, BLK, axis=0), BLK, axis=1)
        scores = (
            jnp.einsum("qkgd,tkd->kgqt", query_heads, key_heads, preferred_element_type=jnp.float32)
            * inv_root
        )
        scores = jnp.where(allowed[None, None], scores, masked_score)
        return key_heads, value_heads, allowed, scores

    def forward_stats(offset, current):
        row_max, row_sum, weighted = current
        key_heads, value_heads, allowed, scores = chunk(offset)
        new_max = jnp.maximum(row_max, jnp.max(scores, axis=-1))
        rescale = jnp.exp(row_max - new_max)
        shifted = jnp.where(allowed[None, None], jnp.exp(scores - new_max[..., None]), 0.0)
        row_sum = row_sum * rescale + jnp.sum(shifted, axis=-1)
        weighted = weighted * rescale[..., None] + jnp.einsum(
            "kgqt,tkd->kgqd",
            shifted.astype(jnp.bfloat16),
            value_heads,
            preferred_element_type=jnp.float32,
        )
        return (new_max, row_sum, weighted)

    def backward_chunk(offset, log_total, row_delta, scores_given=None):
        key_heads, value_heads, allowed, scores = chunk(offset)
        if scores_given is not None:
            scores = scores_given
        probs = jnp.exp(scores - log_total[..., None])
        dprobs = jnp.einsum(
            "qkgd,tkd->kgqt", grad_heads, value_heads, preferred_element_type=jnp.float32
        )
        dscores = (probs * (dprobs - row_delta[..., None])).astype(jnp.bfloat16)
        probs_low = probs.astype(jnp.bfloat16)
        query_term = (
            jnp.einsum("kgqt,tkd->qkgd", dscores, key_heads, preferred_element_type=jnp.float32)
            * inv_root
        )
        key_term = (
            jnp.einsum("kgqt,qkgd->tkd", dscores, query_heads, preferred_element_type=jnp.float32)
            * inv_root
        )
        value_term = jnp.einsum(
            "kgqt,qkgd->tkd", probs_low, grad_heads, preferred_element_type=jnp.float32
        )
        kv_term = jnp.concatenate(
            [key_term.reshape(step_rows, kv_cols), value_term.reshape(step_rows, kv_cols)], axis=1
        )
        return query_term, kv_term

    if steps == 1 and lax.axis_size("ctx") <= 8:
        if rows_here == BLK:
            column_flags = select_cols(own_flags, key_doc_blocks) > 0
            allowed = jnp.repeat(column_flags, BLK, axis=1)
        else:
            allowed = chunk(0)[2]
        query_grad, own_part, sent_part = attention_block(queries, out_grad, kv_rows, allowed)
        kv_grad = scatter_parts(own_part, sent_part, "ctx")
    else:
        start_stats = (
            jnp.full((kv_heads, group_size, rows_here), masked_score, jnp.float32),
            jnp.zeros((kv_heads, group_size, rows_here), jnp.float32),
            jnp.zeros((kv_heads, group_size, rows_here, HD), jnp.float32),
        )
        row_max, row_sum, weighted = lax.fori_loop(
            0, steps, lambda i, c: forward_stats(i * step_rows, c), start_stats
        )
        log_total = row_max + jnp.log(row_sum)
        attended = (weighted / row_sum[..., None]).astype(jnp.bfloat16)
        row_delta = jnp.einsum(
            "kgqd,qkgd->kgq", attended, grad_heads, preferred_element_type=jnp.float32
        )

        def backward_visit(turn_index, current):
            query_now, kv_now = current
            offset = turn_index * step_rows
            query_term, kv_term = backward_chunk(offset, log_total, row_delta)
            kv_now = lax.dynamic_update_slice_in_dim(kv_now, kv_term, offset, 0)
            return (query_now + query_term, kv_now)

        query_acc, kv_acc = lax.fori_loop(
            0,
            steps,
            backward_visit,
            (
                jnp.zeros((rows_here, kv_heads, group_size, HD), jnp.float32),
                jnp.zeros((row_count, 2 * kv_cols), jnp.float32),
            ),
        )
        query_grad = query_acc.reshape(rows_here, -1).astype(jnp.bfloat16)
        kv_grad = scatter_slots(kv_acc, "ctx")

    key_grad = kv_grad[:, :kv_cols].astype(jnp.bfloat16)
    value_grad = kv_grad[:, kv_cols:].astype(jnp.bfloat16)
    input_grad_t = head_reduce(key_proj, value_proj, key_grad, value_grad)
    return (query_grad, key_grad, value_grad, input_grad_t)


def solution(mesh):
    return jax.shard_map(
        local,
        mesh=mesh,
        in_specs=(
            P(("groups", "ctx"), "head"),
            P(("groups", "ctx"), "head"),
            P(("groups", "ctx"), "head"),
            P(("groups", "ctx"), "head"),
            P("groups", None),
            P("groups"),
            P(None, "head"),
            P(None, "head"),
        ),
        out_specs=(
            P(("groups", "ctx"), "head"),
            P(("groups", "ctx"), "head"),
            P(("groups", "ctx"), "head"),
            P("head", ("groups", "ctx")),
        ),
        check_vma=False,
    )
```

```python
import math

import jax
import jax.numpy as jnp
from jax import lax
from jax.experimental import pallas as pl
from jax.experimental.pallas import tpu as pltpu
from jax.sharding import PartitionSpec as P

HD = 128
BLK = 128


masked_score = -1e30


def select_rows(lookup, picked):
    onehot = (picked[:, None] == lax.iota(jnp.int32, lookup.shape[0])[None, :]).astype(jnp.int32)
    return jnp.sum(onehot[:, :, None] * lookup[None, :, :], axis=1)


def select_cols(lookup, picked):
    onehot = (picked[:, None] == lax.iota(jnp.int32, lookup.shape[1])[None, :]).astype(jnp.int32)
    return jnp.sum(lookup[:, None, :] * onehot[None, :, :], axis=2)


def pick(vector, picked):
    onehot = (picked[:, None] == lax.iota(jnp.int32, vector.shape[0])[None, :]).astype(jnp.int32)
    return jnp.sum(onehot * vector[None, :], axis=1)


def shifted_pairs(count, steps):
    return [(source, (source + steps) % count) for source in range(count)]


def gather_slots(block, axis):
    count = lax.axis_size(axis)
    position = lax.axis_index(axis)
    if count > 8:
        gathered = lax.all_gather(block, axis, axis=0, tiled=True)
        return gathered, lax.iota(jnp.int32, count)
    pieces = [block] + [
        lax.ppermute(block, axis, shifted_pairs(count, steps)) for steps in range(1, count)
    ]
    sources = (position - lax.iota(jnp.int32, count)) % count
    return jnp.concatenate(pieces, axis=0), sources


def scatter_slots(slots, axis):
    count = lax.axis_size(axis)
    if count > 8:
        return lax.psum_scatter(slots, axis, scatter_dimension=0, tiled=True)
    rows = slots.shape[0] // count
    total = slots[:rows]
    for steps in range(1, count):
        total = total + lax.ppermute(
            slots[steps * rows : (steps + 1) * rows].astype(jnp.bfloat16),
            axis,
            shifted_pairs(count, -steps),
        ).astype(jnp.float32)
    return total


def scatter_parts(own, sent, axis):
    count = lax.axis_size(axis)
    rows = own.shape[0]
    total = own
    for steps in range(1, count):
        total = total + lax.ppermute(
            sent[(steps - 1) * rows : steps * rows], axis, shifted_pairs(count, -steps)
        ).astype(jnp.float32)
    return total


def copy_to_vmem(source, target):
    pltpu.sync_copy(source, target)


def staged(weights):
    return pl.pallas_call(
        copy_to_vmem,
        out_shape=jax.ShapeDtypeStruct(weights.shape, weights.dtype),
        in_specs=[pl.BlockSpec(memory_space=pl.ANY)],
        out_specs=pl.BlockSpec(memory_space=pltpu.VMEM),
    )(weights)


def head_reduce(key_proj, value_proj, key_grad, value_grad):
    count = lax.axis_size("head")
    position = lax.axis_index("head")
    depth = count.bit_length() - 1
    contraction = (((1,), (1,)), ((), ()))
    if count == 1 or count != 1 << depth:
        partial = lax.dot_general(
            key_proj, key_grad, contraction, preferred_element_type=jnp.float32
        ) + lax.dot_general(value_proj, value_grad, contraction, preferred_element_type=jnp.float32)
        return lax.psum_scatter(partial, "head", scatter_dimension=0, tiled=True).astype(
            jnp.bfloat16
        )
    block = key_proj.shape[0] // count
    key_proj = staged(key_proj)
    value_proj = staged(value_proj)
    key_split = key_proj.reshape(count // 2, 2, block, key_proj.shape[1])
    value_split = value_proj.reshape(count // 2, 2, block, value_proj.shape[1])

    def project(half):
        return jnp.einsum(
            "arf,tf->art",
            lax.dynamic_index_in_dim(key_split, half, 1, keepdims=False),
            key_grad,
            preferred_element_type=jnp.float32,
        ) + jnp.einsum(
            "arf,tf->art",
            lax.dynamic_index_in_dim(value_split, half, 1, keepdims=False),
            value_grad,
            preferred_element_type=jnp.float32,
        )

    own_bit = position % 2
    sent = project(1 - own_bit)
    kept = project(own_bit)
    current = kept + lax.ppermute(
        sent.astype(jnp.bfloat16), "head", [(i, i ^ 1) for i in range(count)]
    ).astype(jnp.float32)
    for level in range(1, depth):
        current = current.reshape(-1, 2, block, current.shape[-1])
        own_bit = (position // (1 << level)) % 2
        kept = lax.dynamic_index_in_dim(current, own_bit, 1, keepdims=False)
        sent = lax.dynamic_index_in_dim(current, 1 - own_bit, 1, keepdims=False)
        arrived = lax.ppermute(
            sent.astype(jnp.bfloat16), "head", [(i, i ^ (1 << level)) for i in range(count)]
        )
        current = kept + arrived.astype(jnp.float32)
    return current.reshape(block, -1).astype(jnp.bfloat16)


def attention_kernel(
    query_ref, grad_ref, key_ref, value_ref, mask_ref, query_out, own_out, sent_out
):
    inv_root = HD ** (-0.5)
    kv_cols = key_ref.shape[1]
    kv_heads = kv_cols // HD
    rows = query_ref.shape[0]
    group_size = query_ref.shape[1] // kv_cols
    if mask_ref.shape[0] == 1:
        allowed = mask_ref[...] > 0
    else:
        allowed = jnp.concatenate([mask_ref[...]] * group_size, axis=0) > 0
    across = (((1,), (1,)), ((), ()))
    down = (((0,), (0,)), ((), ()))
    for kv_head in range(kv_heads):
        key_head = key_ref[:, kv_head * HD : (kv_head + 1) * HD]
        value_head = value_ref[:, kv_head * HD : (kv_head + 1) * HD]
        base = kv_head * group_size * HD
        query_stack = jnp.concatenate(
            [query_ref[:, base + m * HD : base + (m + 1) * HD] for m in range(group_size)], axis=0
        )
        grad_stack = jnp.concatenate(
            [grad_ref[:, base + m * HD : base + (m + 1) * HD] for m in range(group_size)], axis=0
        )
        scores = (
            lax.dot_general(query_stack, key_head, across, preferred_element_type=jnp.float32)
            * inv_root
        )
        scores = jnp.where(allowed, scores, masked_score)
        row_max = jnp.max(scores, axis=1, keepdims=True)
        shifted = jnp.exp(scores - row_max)
        row_sum = jnp.sum(shifted, axis=1, keepdims=True)
        weighted = jnp.dot(
            shifted.astype(jnp.bfloat16), value_head, preferred_element_type=jnp.float32
        )
        attended = (weighted / row_sum).astype(jnp.bfloat16)
        probs = shifted * (1.0 / row_sum)
        row_delta = jnp.sum(
            grad_stack.astype(jnp.float32) * attended.astype(jnp.float32), axis=1, keepdims=True
        )
        dprobs = lax.dot_general(grad_stack, value_head, across, preferred_element_type=jnp.float32)
        dscores = (probs * (dprobs - row_delta)).astype(jnp.bfloat16)
        query_term = jnp.dot(dscores, key_head, preferred_element_type=jnp.float32) * inv_root
        for m in range(group_size):
            query_out[:, base + m * HD : base + (m + 1) * HD] = query_term[
                m * rows : (m + 1) * rows
            ].astype(jnp.bfloat16)
        key_sum = lax.dot_general(dscores, query_stack, down, preferred_element_type=jnp.float32)
        value_sum = lax.dot_general(
            probs.astype(jnp.bfloat16), grad_stack, down, preferred_element_type=jnp.float32
        )
        key_sum = key_sum * inv_root
        key_cols = slice(kv_head * HD, (kv_head + 1) * HD)
        value_cols = slice(kv_cols + kv_head * HD, kv_cols + (kv_head + 1) * HD)
        own_out[:, key_cols] = key_sum[:rows]
        own_out[:, value_cols] = value_sum[:rows]
        sent_out[:, key_cols] = key_sum[rows:].astype(jnp.bfloat16)
        sent_out[:, value_cols] = value_sum[rows:].astype(jnp.bfloat16)


def attention_block(queries, out_grad, key_rows, value_rows, allowed, interpret=False):
    rows = queries.shape[0]
    width = 2 * key_rows.shape[1]
    return pl.pallas_call(
        attention_kernel,
        out_shape=(
            jax.ShapeDtypeStruct(queries.shape, jnp.bfloat16),
            jax.ShapeDtypeStruct((rows, width), jnp.float32),
            jax.ShapeDtypeStruct((key_rows.shape[0] - rows, width), jnp.bfloat16),
        ),
        interpret=interpret,
    )(queries, out_grad, key_rows, value_rows, allowed.astype(jnp.int32))


def local(
    queries, key_states, value_states, out_grad, mask_flags, shard_blocks, key_proj, value_proj
):
    rows_here = queries.shape[0]
    kv_cols = key_states.shape[1]
    kv_heads = kv_cols // HD
    group_size = queries.shape[1] // kv_cols
    inv_root = HD ** (-0.5)
    position = lax.axis_index("ctx")
    query_heads = queries.reshape(rows_here, kv_heads, group_size, HD)
    grad_heads = out_grad.reshape(rows_here, kv_heads, group_size, HD)
    own_blocks = lax.dynamic_slice_in_dim(
        shard_blocks, position * (rows_here // BLK), rows_here // BLK
    )
    own_flags = select_rows(mask_flags, own_blocks)

    key_rows, sources = gather_slots(key_states, "ctx")
    value_rows = gather_slots(value_states, "ctx")[0]
    kv_rows = jnp.concatenate([key_rows, value_rows], axis=1)
    row_count = kv_rows.shape[0]
    blocks_here = rows_here // BLK
    key_blocks = lax.iota(jnp.int32, row_count // BLK)
    key_doc_blocks = pick(
        shard_blocks,
        pick(sources, key_blocks // blocks_here) * blocks_here + key_blocks % blocks_here,
    )
    step_rows = math.gcd(row_count, 512)
    steps = row_count // step_rows

    def chunk(offset):
        block = lax.dynamic_slice_in_dim(kv_rows, offset, step_rows)
        key_heads = block[:, :kv_cols].reshape(step_rows, kv_heads, HD)
        value_heads = block[:, kv_cols:].reshape(step_rows, kv_heads, HD)
        their_blocks = lax.dynamic_slice_in_dim(key_doc_blocks, offset // BLK, step_rows // BLK)
        pair_flags = select_cols(own_flags, their_blocks) > 0
        allowed = jnp.repeat(jnp.repeat(pair_flags, BLK, axis=0), BLK, axis=1)
        scores = (
            jnp.einsum("qkgd,tkd->kgqt", query_heads, key_heads, preferred_element_type=jnp.float32)
            * inv_root
        )
        scores = jnp.where(allowed[None, None], scores, masked_score)
        return key_heads, value_heads, allowed, scores

    def forward_stats(offset, current):
        row_max, row_sum, weighted = current
        key_heads, value_heads, allowed, scores = chunk(offset)
        new_max = jnp.maximum(row_max, jnp.max(scores, axis=-1))
        rescale = jnp.exp(row_max - new_max)
        shifted = jnp.where(allowed[None, None], jnp.exp(scores - new_max[..., None]), 0.0)
        row_sum = row_sum * rescale + jnp.sum(shifted, axis=-1)
        weighted = weighted * rescale[..., None] + jnp.einsum(
            "kgqt,tkd->kgqd",
            shifted.astype(jnp.bfloat16),
            value_heads,
            preferred_element_type=jnp.float32,
        )
        return (new_max, row_sum, weighted)

    def backward_chunk(offset, log_total, row_delta, scores_given=None):
        key_heads, value_heads, allowed, scores = chunk(offset)
        if scores_given is not None:
            scores = scores_given
        probs = jnp.exp(scores - log_total[..., None])
        dprobs = jnp.einsum(
            "qkgd,tkd->kgqt", grad_heads, value_heads, preferred_element_type=jnp.float32
        )
        dscores = (probs * (dprobs - row_delta[..., None])).astype(jnp.bfloat16)
        probs_low = probs.astype(jnp.bfloat16)
        query_term = (
            jnp.einsum("kgqt,tkd->qkgd", dscores, key_heads, preferred_element_type=jnp.float32)
            * inv_root
        )
        key_term = (
            jnp.einsum("kgqt,qkgd->tkd", dscores, query_heads, preferred_element_type=jnp.float32)
            * inv_root
        )
        value_term = jnp.einsum(
            "kgqt,qkgd->tkd", probs_low, grad_heads, preferred_element_type=jnp.float32
        )
        kv_term = jnp.concatenate(
            [key_term.reshape(step_rows, kv_cols), value_term.reshape(step_rows, kv_cols)], axis=1
        )
        return query_term, kv_term

    if steps == 1 and lax.axis_size("ctx") <= 8:
        if rows_here == BLK:
            column_flags = select_cols(own_flags, key_doc_blocks) > 0
            allowed = jnp.repeat(column_flags, BLK, axis=1)
        else:
            allowed = chunk(0)[2]
        query_grad, own_part, sent_part = attention_block(
            queries, out_grad, key_rows, value_rows, allowed
        )
        kv_grad = scatter_parts(own_part, sent_part, "ctx")
    else:
        start_stats = (
            jnp.full((kv_heads, group_size, rows_here), masked_score, jnp.float32),
            jnp.zeros((kv_heads, group_size, rows_here), jnp.float32),
            jnp.zeros((kv_heads, group_size, rows_here, HD), jnp.float32),
        )
        row_max, row_sum, weighted = lax.fori_loop(
            0, steps, lambda i, c: forward_stats(i * step_rows, c), start_stats
        )
        log_total = row_max + jnp.log(row_sum)
        attended = (weighted / row_sum[..., None]).astype(jnp.bfloat16)
        row_delta = jnp.einsum(
            "kgqd,qkgd->kgq", attended, grad_heads, preferred_element_type=jnp.float32
        )

        def backward_visit(turn_index, current):
            query_now, kv_now = current
            offset = turn_index * step_rows
            query_term, kv_term = backward_chunk(offset, log_total, row_delta)
            kv_now = lax.dynamic_update_slice_in_dim(kv_now, kv_term, offset, 0)
            return (query_now + query_term, kv_now)

        query_acc, kv_acc = lax.fori_loop(
            0,
            steps,
            backward_visit,
            (
                jnp.zeros((rows_here, kv_heads, group_size, HD), jnp.float32),
                jnp.zeros((row_count, 2 * kv_cols), jnp.float32),
            ),
        )
        query_grad = query_acc.reshape(rows_here, -1).astype(jnp.bfloat16)
        kv_grad = scatter_slots(kv_acc, "ctx")

    key_grad = kv_grad[:, :kv_cols].astype(jnp.bfloat16)
    value_grad = kv_grad[:, kv_cols:].astype(jnp.bfloat16)
    input_grad_t = head_reduce(key_proj, value_proj, key_grad, value_grad)
    return (query_grad, key_grad, value_grad, input_grad_t)


def solution(mesh):
    return jax.shard_map(
        local,
        mesh=mesh,
        in_specs=(
            P(("groups", "ctx"), "head"),
            P(("groups", "ctx"), "head"),
            P(("groups", "ctx"), "head"),
            P(("groups", "ctx"), "head"),
            P("groups", None),
            P("groups"),
            P(None, "head"),
            P(None, "head"),
        ),
        out_specs=(
            P(("groups", "ctx"), "head"),
            P(("groups", "ctx"), "head"),
            P(("groups", "ctx"), "head"),
            P("head", ("groups", "ctx")),
        ),
        check_vma=False,
    )
```

```python
import math

import jax
import jax.numpy as jnp
from jax import lax
from jax.experimental import pallas as pl
from jax.experimental.pallas import tpu as pltpu
from jax.sharding import PartitionSpec as P

HD = 128
BLK = 128


masked_score = -1e30


def select_rows(lookup, picked):
    onehot = (picked[:, None] == lax.iota(jnp.int32, lookup.shape[0])[None, :]).astype(jnp.int32)
    return jnp.sum(onehot[:, :, None] * lookup[None, :, :], axis=1)


def select_cols(lookup, picked):
    onehot = (picked[:, None] == lax.iota(jnp.int32, lookup.shape[1])[None, :]).astype(jnp.int32)
    return jnp.sum(lookup[:, None, :] * onehot[None, :, :], axis=2)


def pick(vector, picked):
    onehot = (picked[:, None] == lax.iota(jnp.int32, vector.shape[0])[None, :]).astype(jnp.int32)
    return jnp.sum(onehot * vector[None, :], axis=1)


def shifted_pairs(count, steps):
    return [(source, (source + steps) % count) for source in range(count)]


def gather_slots(block, axis):
    count = lax.axis_size(axis)
    position = lax.axis_index(axis)
    if count > 8:
        gathered = lax.all_gather(block, axis, axis=0, tiled=True)
        return gathered, lax.iota(jnp.int32, count)
    pieces = [block] + [
        lax.ppermute(block, axis, shifted_pairs(count, steps)) for steps in range(1, count)
    ]
    sources = (position - lax.iota(jnp.int32, count)) % count
    return jnp.concatenate(pieces, axis=0), sources


def scatter_slots(slots, axis):
    count = lax.axis_size(axis)
    if count > 8:
        return lax.psum_scatter(slots, axis, scatter_dimension=0, tiled=True)
    rows = slots.shape[0] // count
    total = slots[:rows]
    for steps in range(1, count):
        total = total + lax.ppermute(
            slots[steps * rows : (steps + 1) * rows].astype(jnp.bfloat16),
            axis,
            shifted_pairs(count, -steps),
        ).astype(jnp.float32)
    return total


def scatter_parts(own, sent, axis):
    count = lax.axis_size(axis)
    rows = own.shape[0]
    total = own
    for steps in range(1, count):
        total = total + lax.ppermute(
            sent[(steps - 1) * rows : steps * rows], axis, shifted_pairs(count, -steps)
        ).astype(jnp.float32)
    return total


def copy_in_order(order_ref, source, target):
    blocks = order_ref.shape[0]
    rows = target.shape[0] // blocks
    for i in range(blocks):
        pltpu.sync_copy(
            source.at[pl.ds(order_ref[i] * rows, rows)], target.at[pl.ds(i * rows, rows)]
        )


def staged(weights, order):
    return pl.pallas_call(
        copy_in_order,
        out_shape=jax.ShapeDtypeStruct(weights.shape, weights.dtype),
        in_specs=[pl.BlockSpec(memory_space=pltpu.SMEM), pl.BlockSpec(memory_space=pl.ANY)],
        out_specs=pl.BlockSpec(memory_space=pl.ANY),
    )(order, weights)


def head_reduce(key_proj, value_proj, key_grad, value_grad):
    count = lax.axis_size("head")
    position = lax.axis_index("head")
    depth = count.bit_length() - 1
    contraction = (((1,), (1,)), ((), ()))
    if count == 1 or count != 1 << depth:
        partial = lax.dot_general(
            key_proj, key_grad, contraction, preferred_element_type=jnp.float32
        ) + lax.dot_general(value_proj, value_grad, contraction, preferred_element_type=jnp.float32)
        return lax.psum_scatter(partial, "head", scatter_dimension=0, tiled=True).astype(
            jnp.bfloat16
        )
    block = key_proj.shape[0] // count
    own_bit = position % 2
    upper = lax.iota(jnp.int32, count // 2) * 2
    order = jnp.concatenate([upper + 1 - own_bit, upper + own_bit])
    key_split = staged(key_proj, order).reshape(2, count // 2, block, key_proj.shape[1])
    value_split = staged(value_proj, order).reshape(2, count // 2, block, value_proj.shape[1])

    def project(part):
        return jnp.einsum(
            "arf,tf->art", key_split[part], key_grad, preferred_element_type=jnp.float32
        ) + jnp.einsum(
            "arf,tf->art", value_split[part], value_grad, preferred_element_type=jnp.float32
        )

    sent = project(0)
    kept = project(1)
    current = kept + lax.ppermute(
        sent.astype(jnp.bfloat16), "head", [(i, i ^ 1) for i in range(count)]
    ).astype(jnp.float32)
    for level in range(1, depth):
        current = current.reshape(-1, 2, block, current.shape[-1])
        own_bit = (position // (1 << level)) % 2
        kept = lax.dynamic_index_in_dim(current, own_bit, 1, keepdims=False)
        sent = lax.dynamic_index_in_dim(current, 1 - own_bit, 1, keepdims=False)
        arrived = lax.ppermute(
            sent.astype(jnp.bfloat16), "head", [(i, i ^ (1 << level)) for i in range(count)]
        )
        current = kept + arrived.astype(jnp.float32)
    return current.reshape(block, -1).astype(jnp.bfloat16)


def attention_kernel(query_ref, grad_ref, kv_ref, mask_ref, query_out, own_out, sent_out):
    inv_root = HD ** (-0.5)
    kv_cols = kv_ref.shape[1] // 2
    kv_heads = kv_cols // HD
    rows = query_ref.shape[0]
    group_size = query_ref.shape[1] // kv_cols
    if mask_ref.shape[0] == 1:
        allowed = mask_ref[...] > 0
    else:
        allowed = jnp.concatenate([mask_ref[...]] * group_size, axis=0) > 0
    across = (((1,), (1,)), ((), ()))
    down = (((0,), (0,)), ((), ()))
    for kv_head in range(kv_heads):
        key_head = kv_ref[:, kv_head * HD : (kv_head + 1) * HD]
        value_head = kv_ref[:, kv_cols + kv_head * HD : kv_cols + (kv_head + 1) * HD]
        base = kv_head * group_size * HD
        query_stack = jnp.concatenate(
            [query_ref[:, base + m * HD : base + (m + 1) * HD] for m in range(group_size)], axis=0
        )
        grad_stack = jnp.concatenate(
            [grad_ref[:, base + m * HD : base + (m + 1) * HD] for m in range(group_size)], axis=0
        )
        scores = (
            lax.dot_general(query_stack, key_head, across, preferred_element_type=jnp.float32)
            * inv_root
        )
        scores = jnp.where(allowed, scores, masked_score)
        row_max = jnp.max(scores, axis=1, keepdims=True)
        shifted = jnp.exp(scores - row_max)
        row_sum = jnp.sum(shifted, axis=1, keepdims=True)
        weighted = jnp.dot(
            shifted.astype(jnp.bfloat16), value_head, preferred_element_type=jnp.float32
        )
        attended = (weighted / row_sum).astype(jnp.bfloat16)
        probs = shifted * (1.0 / row_sum)
        row_delta = jnp.sum(
            grad_stack.astype(jnp.float32) * attended.astype(jnp.float32), axis=1, keepdims=True
        )
        dprobs = lax.dot_general(grad_stack, value_head, across, preferred_element_type=jnp.float32)
        dscores = (probs * (dprobs - row_delta)).astype(jnp.bfloat16)
        query_term = jnp.dot(dscores, key_head, preferred_element_type=jnp.float32) * inv_root
        for m in range(group_size):
            query_out[:, base + m * HD : base + (m + 1) * HD] = query_term[
                m * rows : (m + 1) * rows
            ].astype(jnp.bfloat16)
        key_sum = lax.dot_general(dscores, query_stack, down, preferred_element_type=jnp.float32)
        value_sum = lax.dot_general(
            probs.astype(jnp.bfloat16), grad_stack, down, preferred_element_type=jnp.float32
        )
        key_sum = key_sum * inv_root
        key_cols = slice(kv_head * HD, (kv_head + 1) * HD)
        value_cols = slice(kv_cols + kv_head * HD, kv_cols + (kv_head + 1) * HD)
        own_out[:, key_cols] = key_sum[:rows]
        own_out[:, value_cols] = value_sum[:rows]
        sent_out[:, key_cols] = key_sum[rows:].astype(jnp.bfloat16)
        sent_out[:, value_cols] = value_sum[rows:].astype(jnp.bfloat16)


def attention_block(queries, out_grad, kv_rows, allowed, interpret=False):
    rows = queries.shape[0]
    return pl.pallas_call(
        attention_kernel,
        out_shape=(
            jax.ShapeDtypeStruct(queries.shape, jnp.bfloat16),
            jax.ShapeDtypeStruct((rows, kv_rows.shape[1]), jnp.float32),
            jax.ShapeDtypeStruct((kv_rows.shape[0] - rows, kv_rows.shape[1]), jnp.bfloat16),
        ),
        interpret=interpret,
    )(queries, out_grad, kv_rows, allowed.astype(jnp.int32))


def local(
    queries, key_states, value_states, out_grad, mask_flags, shard_blocks, key_proj, value_proj
):
    rows_here = queries.shape[0]
    kv_cols = key_states.shape[1]
    kv_heads = kv_cols // HD
    group_size = queries.shape[1] // kv_cols
    inv_root = HD ** (-0.5)
    position = lax.axis_index("ctx")
    query_heads = queries.reshape(rows_here, kv_heads, group_size, HD)
    grad_heads = out_grad.reshape(rows_here, kv_heads, group_size, HD)
    own_blocks = lax.dynamic_slice_in_dim(
        shard_blocks, position * (rows_here // BLK), rows_here // BLK
    )
    own_flags = select_rows(mask_flags, own_blocks)

    kv_rows, sources = gather_slots(
        jnp.concatenate([key_states, value_states], axis=1), "ctx"
    )
    row_count = kv_rows.shape[0]
    blocks_here = rows_here // BLK
    key_blocks = lax.iota(jnp.int32, row_count // BLK)
    key_doc_blocks = pick(
        shard_blocks,
        pick(sources, key_blocks // blocks_here) * blocks_here + key_blocks % blocks_here,
    )
    step_rows = math.gcd(row_count, 512)
    steps = row_count // step_rows

    def chunk(offset):
        block = lax.dynamic_slice_in_dim(kv_rows, offset, step_rows)
        key_heads = block[:, :kv_cols].reshape(step_rows, kv_heads, HD)
        value_heads = block[:, kv_cols:].reshape(step_rows, kv_heads, HD)
        their_blocks = lax.dynamic_slice_in_dim(key_doc_blocks, offset // BLK, step_rows // BLK)
        pair_flags = select_cols(own_flags, their_blocks) > 0
        allowed = jnp.repeat(jnp.repeat(pair_flags, BLK, axis=0), BLK, axis=1)
        scores = (
            jnp.einsum("qkgd,tkd->kgqt", query_heads, key_heads, preferred_element_type=jnp.float32)
            * inv_root
        )
        scores = jnp.where(allowed[None, None], scores, masked_score)
        return key_heads, value_heads, allowed, scores

    def forward_stats(offset, current):
        row_max, row_sum, weighted = current
        key_heads, value_heads, allowed, scores = chunk(offset)
        new_max = jnp.maximum(row_max, jnp.max(scores, axis=-1))
        rescale = jnp.exp(row_max - new_max)
        shifted = jnp.where(allowed[None, None], jnp.exp(scores - new_max[..., None]), 0.0)
        row_sum = row_sum * rescale + jnp.sum(shifted, axis=-1)
        weighted = weighted * rescale[..., None] + jnp.einsum(
            "kgqt,tkd->kgqd",
            shifted.astype(jnp.bfloat16),
            value_heads,
            preferred_element_type=jnp.float32,
        )
        return (new_max, row_sum, weighted)

    def backward_chunk(offset, log_total, row_delta, scores_given=None):
        key_heads, value_heads, allowed, scores = chunk(offset)
        if scores_given is not None:
            scores = scores_given
        probs = jnp.exp(scores - log_total[..., None])
        dprobs = jnp.einsum(
            "qkgd,tkd->kgqt", grad_heads, value_heads, preferred_element_type=jnp.float32
        )
        dscores = (probs * (dprobs - row_delta[..., None])).astype(jnp.bfloat16)
        probs_low = probs.astype(jnp.bfloat16)
        query_term = (
            jnp.einsum("kgqt,tkd->qkgd", dscores, key_heads, preferred_element_type=jnp.float32)
            * inv_root
        )
        key_term = (
            jnp.einsum("kgqt,qkgd->tkd", dscores, query_heads, preferred_element_type=jnp.float32)
            * inv_root
        )
        value_term = jnp.einsum(
            "kgqt,qkgd->tkd", probs_low, grad_heads, preferred_element_type=jnp.float32
        )
        kv_term = jnp.concatenate(
            [key_term.reshape(step_rows, kv_cols), value_term.reshape(step_rows, kv_cols)], axis=1
        )
        return query_term, kv_term

    if steps == 1 and lax.axis_size("ctx") <= 8:
        if rows_here == BLK:
            column_flags = select_cols(own_flags, key_doc_blocks) > 0
            allowed = jnp.repeat(column_flags, BLK, axis=1)
        else:
            allowed = chunk(0)[2]
        query_grad, own_part, sent_part = attention_block(queries, out_grad, kv_rows, allowed)
        kv_grad = scatter_parts(own_part, sent_part, "ctx")
    else:
        start_stats = (
            jnp.full((kv_heads, group_size, rows_here), masked_score, jnp.float32),
            jnp.zeros((kv_heads, group_size, rows_here), jnp.float32),
            jnp.zeros((kv_heads, group_size, rows_here, HD), jnp.float32),
        )
        row_max, row_sum, weighted = lax.fori_loop(
            0, steps, lambda i, c: forward_stats(i * step_rows, c), start_stats
        )
        log_total = row_max + jnp.log(row_sum)
        attended = (weighted / row_sum[..., None]).astype(jnp.bfloat16)
        row_delta = jnp.einsum(
            "kgqd,qkgd->kgq", attended, grad_heads, preferred_element_type=jnp.float32
        )

        def backward_visit(turn_index, current):
            query_now, kv_now = current
            offset = turn_index * step_rows
            query_term, kv_term = backward_chunk(offset, log_total, row_delta)
            kv_now = lax.dynamic_update_slice_in_dim(kv_now, kv_term, offset, 0)
            return (query_now + query_term, kv_now)

        query_acc, kv_acc = lax.fori_loop(
            0,
            steps,
            backward_visit,
            (
                jnp.zeros((rows_here, kv_heads, group_size, HD), jnp.float32),
                jnp.zeros((row_count, 2 * kv_cols), jnp.float32),
            ),
        )
        query_grad = query_acc.reshape(rows_here, -1).astype(jnp.bfloat16)
        kv_grad = scatter_slots(kv_acc, "ctx")

    key_grad = kv_grad[:, :kv_cols].astype(jnp.bfloat16)
    value_grad = kv_grad[:, kv_cols:].astype(jnp.bfloat16)
    input_grad_t = head_reduce(key_proj, value_proj, key_grad, value_grad)
    return (query_grad, key_grad, value_grad, input_grad_t)


def solution(mesh):
    return jax.shard_map(
        local,
        mesh=mesh,
        in_specs=(
            P(("groups", "ctx"), "head"),
            P(("groups", "ctx"), "head"),
            P(("groups", "ctx"), "head"),
            P(("groups", "ctx"), "head"),
            P("groups", None),
            P("groups"),
            P(None, "head"),
            P(None, "head"),
        ),
        out_specs=(
            P(("groups", "ctx"), "head"),
            P(("groups", "ctx"), "head"),
            P(("groups", "ctx"), "head"),
            P("head", ("groups", "ctx")),
        ),
        check_vma=False,
    )
```

```python
import math

import jax
import jax.numpy as jnp
from jax import lax
from jax.experimental import pallas as pl
from jax.experimental.pallas import tpu as pltpu
from jax.sharding import PartitionSpec as P

HD = 128
BLK = 128


masked_score = -1e30


def select_rows(lookup, picked):
    onehot = (picked[:, None] == lax.iota(jnp.int32, lookup.shape[0])[None, :]).astype(jnp.int32)
    return jnp.sum(onehot[:, :, None] * lookup[None, :, :], axis=1)


def select_cols(lookup, picked):
    onehot = (picked[:, None] == lax.iota(jnp.int32, lookup.shape[1])[None, :]).astype(jnp.int32)
    return jnp.sum(lookup[:, None, :] * onehot[None, :, :], axis=2)


def pick(vector, picked):
    onehot = (picked[:, None] == lax.iota(jnp.int32, vector.shape[0])[None, :]).astype(jnp.int32)
    return jnp.sum(onehot * vector[None, :], axis=1)


def shifted_pairs(count, steps):
    return [(source, (source + steps) % count) for source in range(count)]


def gather_slots(block, axis):
    count = lax.axis_size(axis)
    position = lax.axis_index(axis)
    if count > 8:
        gathered = lax.all_gather(block, axis, axis=0, tiled=True)
        return gathered, lax.iota(jnp.int32, count)
    pieces = [block] + [
        lax.ppermute(block, axis, shifted_pairs(count, steps)) for steps in range(1, count)
    ]
    sources = (position - lax.iota(jnp.int32, count)) % count
    return jnp.concatenate(pieces, axis=0), sources


def scatter_slots(slots, axis):
    count = lax.axis_size(axis)
    if count > 8:
        return lax.psum_scatter(slots, axis, scatter_dimension=0, tiled=True)
    rows = slots.shape[0] // count
    total = slots[:rows]
    for steps in range(1, count):
        total = total + lax.ppermute(
            slots[steps * rows : (steps + 1) * rows].astype(jnp.bfloat16),
            axis,
            shifted_pairs(count, -steps),
        ).astype(jnp.float32)
    return total


def scatter_parts(own, sent, axis):
    count = lax.axis_size(axis)
    rows = own.shape[0]
    total = own
    for steps in range(1, count):
        total = total + lax.ppermute(
            sent[steps - 1], axis, shifted_pairs(count, -steps)
        ).astype(jnp.float32)
    return total


def copy_to_vmem(source, target):
    pltpu.sync_copy(source, target)


def staged(weights):
    return pl.pallas_call(
        copy_to_vmem,
        out_shape=jax.ShapeDtypeStruct(weights.shape, weights.dtype),
        in_specs=[pl.BlockSpec(memory_space=pl.ANY)],
        out_specs=pl.BlockSpec(memory_space=pltpu.VMEM),
    )(weights)


def head_reduce(key_proj, value_proj, key_grad, value_grad):
    count = lax.axis_size("head")
    position = lax.axis_index("head")
    depth = count.bit_length() - 1
    contraction = (((1,), (1,)), ((), ()))
    if count == 1 or count != 1 << depth:
        partial = lax.dot_general(
            key_proj, key_grad, contraction, preferred_element_type=jnp.float32
        ) + lax.dot_general(value_proj, value_grad, contraction, preferred_element_type=jnp.float32)
        return lax.psum_scatter(partial, "head", scatter_dimension=0, tiled=True).astype(
            jnp.bfloat16
        )
    block = key_proj.shape[0] // count
    key_proj = staged(key_proj)
    value_proj = staged(value_proj)
    key_split = key_proj.reshape(count // 2, 2, block, key_proj.shape[1])
    value_split = value_proj.reshape(count // 2, 2, block, value_proj.shape[1])

    def project(half):
        return jnp.einsum(
            "arf,tf->art",
            lax.dynamic_index_in_dim(key_split, half, 1, keepdims=False),
            key_grad,
            preferred_element_type=jnp.float32,
        ) + jnp.einsum(
            "arf,tf->art",
            lax.dynamic_index_in_dim(value_split, half, 1, keepdims=False),
            value_grad,
            preferred_element_type=jnp.float32,
        )

    own_bit = position % 2
    sent = project(1 - own_bit)
    kept = project(own_bit)
    current = kept + lax.ppermute(
        sent.astype(jnp.bfloat16), "head", [(i, i ^ 1) for i in range(count)]
    ).astype(jnp.float32)
    for level in range(1, depth):
        current = current.reshape(-1, 2, block, current.shape[-1])
        own_bit = (position // (1 << level)) % 2
        kept = lax.dynamic_index_in_dim(current, own_bit, 1, keepdims=False)
        sent = lax.dynamic_index_in_dim(current, 1 - own_bit, 1, keepdims=False)
        arrived = lax.ppermute(
            sent.astype(jnp.bfloat16), "head", [(i, i ^ (1 << level)) for i in range(count)]
        )
        current = kept + arrived.astype(jnp.float32)
    return current.reshape(block, -1).astype(jnp.bfloat16)


def attention_kernel(query_ref, grad_ref, kv_ref, mask_ref, query_out, own_out, *sent_outs):
    inv_root = HD ** (-0.5)
    kv_cols = kv_ref.shape[1] // 2
    kv_heads = kv_cols // HD
    rows = query_ref.shape[0]
    group_size = query_ref.shape[1] // kv_cols
    if mask_ref.shape[0] == 1:
        allowed = mask_ref[...] > 0
    else:
        allowed = jnp.concatenate([mask_ref[...]] * group_size, axis=0) > 0
    across = (((1,), (1,)), ((), ()))
    down = (((0,), (0,)), ((), ()))
    for kv_head in range(kv_heads):
        key_head = kv_ref[:, kv_head * HD : (kv_head + 1) * HD]
        value_head = kv_ref[:, kv_cols + kv_head * HD : kv_cols + (kv_head + 1) * HD]
        base = kv_head * group_size * HD
        query_stack = jnp.concatenate(
            [query_ref[:, base + m * HD : base + (m + 1) * HD] for m in range(group_size)], axis=0
        )
        grad_stack = jnp.concatenate(
            [grad_ref[:, base + m * HD : base + (m + 1) * HD] for m in range(group_size)], axis=0
        )
        scores = (
            lax.dot_general(query_stack, key_head, across, preferred_element_type=jnp.float32)
            * inv_root
        )
        scores = jnp.where(allowed, scores, masked_score)
        row_max = jnp.max(scores, axis=1, keepdims=True)
        shifted = jnp.exp(scores - row_max)
        row_sum = jnp.sum(shifted, axis=1, keepdims=True)
        weighted = jnp.dot(
            shifted.astype(jnp.bfloat16), value_head, preferred_element_type=jnp.float32
        )
        attended = (weighted / row_sum).astype(jnp.bfloat16)
        probs = shifted * (1.0 / row_sum)
        row_delta = jnp.sum(
            grad_stack.astype(jnp.float32) * attended.astype(jnp.float32), axis=1, keepdims=True
        )
        dprobs = lax.dot_general(grad_stack, value_head, across, preferred_element_type=jnp.float32)
        dscores = (probs * (dprobs - row_delta)).astype(jnp.bfloat16)
        query_term = jnp.dot(dscores, key_head, preferred_element_type=jnp.float32) * inv_root
        for m in range(group_size):
            query_out[:, base + m * HD : base + (m + 1) * HD] = query_term[
                m * rows : (m + 1) * rows
            ].astype(jnp.bfloat16)
        key_sum = lax.dot_general(dscores, query_stack, down, preferred_element_type=jnp.float32)
        value_sum = lax.dot_general(
            probs.astype(jnp.bfloat16), grad_stack, down, preferred_element_type=jnp.float32
        )
        key_sum = key_sum * inv_root
        key_cols = slice(kv_head * HD, (kv_head + 1) * HD)
        value_cols = slice(kv_cols + kv_head * HD, kv_cols + (kv_head + 1) * HD)
        own_out[:, key_cols] = key_sum[:rows]
        own_out[:, value_cols] = value_sum[:rows]
        for slot, sent_out in enumerate(sent_outs, start=1):
            sent_out[:, key_cols] = key_sum[slot * rows : (slot + 1) * rows].astype(jnp.bfloat16)
            sent_out[:, value_cols] = value_sum[slot * rows : (slot + 1) * rows].astype(
                jnp.bfloat16
            )


def attention_block(queries, out_grad, kv_rows, allowed, interpret=False):
    rows = queries.shape[0]
    return pl.pallas_call(
        attention_kernel,
        out_shape=(
            jax.ShapeDtypeStruct(queries.shape, jnp.bfloat16),
            jax.ShapeDtypeStruct((rows, kv_rows.shape[1]), jnp.float32),
        )
        + tuple(
            jax.ShapeDtypeStruct((rows, kv_rows.shape[1]), jnp.bfloat16)
            for _ in range(kv_rows.shape[0] // rows - 1)
        ),
        interpret=interpret,
    )(queries, out_grad, kv_rows, allowed.astype(jnp.int32))


def local(
    queries, key_states, value_states, out_grad, mask_flags, shard_blocks, key_proj, value_proj
):
    rows_here = queries.shape[0]
    kv_cols = key_states.shape[1]
    kv_heads = kv_cols // HD
    group_size = queries.shape[1] // kv_cols
    inv_root = HD ** (-0.5)
    position = lax.axis_index("ctx")
    query_heads = queries.reshape(rows_here, kv_heads, group_size, HD)
    grad_heads = out_grad.reshape(rows_here, kv_heads, group_size, HD)
    own_blocks = lax.dynamic_slice_in_dim(
        shard_blocks, position * (rows_here // BLK), rows_here // BLK
    )
    own_flags = select_rows(mask_flags, own_blocks)

    kv_rows, sources = gather_slots(
        jnp.concatenate([key_states, value_states], axis=1), "ctx"
    )
    row_count = kv_rows.shape[0]
    blocks_here = rows_here // BLK
    key_blocks = lax.iota(jnp.int32, row_count // BLK)
    key_doc_blocks = pick(
        shard_blocks,
        pick(sources, key_blocks // blocks_here) * blocks_here + key_blocks % blocks_here,
    )
    step_rows = math.gcd(row_count, 512)
    steps = row_count // step_rows

    def chunk(offset):
        block = lax.dynamic_slice_in_dim(kv_rows, offset, step_rows)
        key_heads = block[:, :kv_cols].reshape(step_rows, kv_heads, HD)
        value_heads = block[:, kv_cols:].reshape(step_rows, kv_heads, HD)
        their_blocks = lax.dynamic_slice_in_dim(key_doc_blocks, offset // BLK, step_rows // BLK)
        pair_flags = select_cols(own_flags, their_blocks) > 0
        allowed = jnp.repeat(jnp.repeat(pair_flags, BLK, axis=0), BLK, axis=1)
        scores = (
            jnp.einsum("qkgd,tkd->kgqt", query_heads, key_heads, preferred_element_type=jnp.float32)
            * inv_root
        )
        scores = jnp.where(allowed[None, None], scores, masked_score)
        return key_heads, value_heads, allowed, scores

    def forward_stats(offset, current):
        row_max, row_sum, weighted = current
        key_heads, value_heads, allowed, scores = chunk(offset)
        new_max = jnp.maximum(row_max, jnp.max(scores, axis=-1))
        rescale = jnp.exp(row_max - new_max)
        shifted = jnp.where(allowed[None, None], jnp.exp(scores - new_max[..., None]), 0.0)
        row_sum = row_sum * rescale + jnp.sum(shifted, axis=-1)
        weighted = weighted * rescale[..., None] + jnp.einsum(
            "kgqt,tkd->kgqd",
            shifted.astype(jnp.bfloat16),
            value_heads,
            preferred_element_type=jnp.float32,
        )
        return (new_max, row_sum, weighted)

    def backward_chunk(offset, log_total, row_delta, scores_given=None):
        key_heads, value_heads, allowed, scores = chunk(offset)
        if scores_given is not None:
            scores = scores_given
        probs = jnp.exp(scores - log_total[..., None])
        dprobs = jnp.einsum(
            "qkgd,tkd->kgqt", grad_heads, value_heads, preferred_element_type=jnp.float32
        )
        dscores = (probs * (dprobs - row_delta[..., None])).astype(jnp.bfloat16)
        probs_low = probs.astype(jnp.bfloat16)
        query_term = (
            jnp.einsum("kgqt,tkd->qkgd", dscores, key_heads, preferred_element_type=jnp.float32)
            * inv_root
        )
        key_term = (
            jnp.einsum("kgqt,qkgd->tkd", dscores, query_heads, preferred_element_type=jnp.float32)
            * inv_root
        )
        value_term = jnp.einsum(
            "kgqt,qkgd->tkd", probs_low, grad_heads, preferred_element_type=jnp.float32
        )
        kv_term = jnp.concatenate(
            [key_term.reshape(step_rows, kv_cols), value_term.reshape(step_rows, kv_cols)], axis=1
        )
        return query_term, kv_term

    if steps == 1 and lax.axis_size("ctx") <= 8:
        if rows_here == BLK:
            column_flags = select_cols(own_flags, key_doc_blocks) > 0
            allowed = jnp.repeat(column_flags, BLK, axis=1)
        else:
            allowed = chunk(0)[2]
        query_grad, own_part, *sent_parts = attention_block(queries, out_grad, kv_rows, allowed)
        kv_grad = scatter_parts(own_part, sent_parts, "ctx")
    else:
        start_stats = (
            jnp.full((kv_heads, group_size, rows_here), masked_score, jnp.float32),
            jnp.zeros((kv_heads, group_size, rows_here), jnp.float32),
            jnp.zeros((kv_heads, group_size, rows_here, HD), jnp.float32),
        )
        row_max, row_sum, weighted = lax.fori_loop(
            0, steps, lambda i, c: forward_stats(i * step_rows, c), start_stats
        )
        log_total = row_max + jnp.log(row_sum)
        attended = (weighted / row_sum[..., None]).astype(jnp.bfloat16)
        row_delta = jnp.einsum(
            "kgqd,qkgd->kgq", attended, grad_heads, preferred_element_type=jnp.float32
        )

        def backward_visit(turn_index, current):
            query_now, kv_now = current
            offset = turn_index * step_rows
            query_term, kv_term = backward_chunk(offset, log_total, row_delta)
            kv_now = lax.dynamic_update_slice_in_dim(kv_now, kv_term, offset, 0)
            return (query_now + query_term, kv_now)

        query_acc, kv_acc = lax.fori_loop(
            0,
            steps,
            backward_visit,
            (
                jnp.zeros((rows_here, kv_heads, group_size, HD), jnp.float32),
                jnp.zeros((row_count, 2 * kv_cols), jnp.float32),
            ),
        )
        query_grad = query_acc.reshape(rows_here, -1).astype(jnp.bfloat16)
        kv_grad = scatter_slots(kv_acc, "ctx")

    key_grad = kv_grad[:, :kv_cols].astype(jnp.bfloat16)
    value_grad = kv_grad[:, kv_cols:].astype(jnp.bfloat16)
    input_grad_t = head_reduce(key_proj, value_proj, key_grad, value_grad)
    return (query_grad, key_grad, value_grad, input_grad_t)


def solution(mesh):
    return jax.shard_map(
        local,
        mesh=mesh,
        in_specs=(
            P(("groups", "ctx"), "head"),
            P(("groups", "ctx"), "head"),
            P(("groups", "ctx"), "head"),
            P(("groups", "ctx"), "head"),
            P("groups", None),
            P("groups"),
            P(None, "head"),
            P(None, "head"),
        ),
        out_specs=(
            P(("groups", "ctx"), "head"),
            P(("groups", "ctx"), "head"),
            P(("groups", "ctx"), "head"),
            P("head", ("groups", "ctx")),
        ),
        check_vma=False,
    )
```

```python
import math

import jax
import jax.numpy as jnp
from jax import lax
from jax.experimental import pallas as pl
from jax.experimental.pallas import tpu as pltpu
from jax.sharding import PartitionSpec as P

HD = 128
BLK = 128


masked_score = -1e30


def select_rows(lookup, picked):
    onehot = (picked[:, None] == lax.iota(jnp.int32, lookup.shape[0])[None, :]).astype(jnp.int32)
    return jnp.sum(onehot[:, :, None] * lookup[None, :, :], axis=1)


def select_cols(lookup, picked):
    onehot = (picked[:, None] == lax.iota(jnp.int32, lookup.shape[1])[None, :]).astype(jnp.int32)
    return jnp.sum(lookup[:, None, :] * onehot[None, :, :], axis=2)


def pick(vector, picked):
    onehot = (picked[:, None] == lax.iota(jnp.int32, vector.shape[0])[None, :]).astype(jnp.int32)
    return jnp.sum(onehot * vector[None, :], axis=1)


def shifted_pairs(count, steps):
    return [(source, (source + steps) % count) for source in range(count)]


def gather_slots(block, axis):
    count = lax.axis_size(axis)
    position = lax.axis_index(axis)
    if count > 8:
        gathered = lax.all_gather(block, axis, axis=0, tiled=True)
        return [gathered], lax.iota(jnp.int32, count)
    pieces = [block] + [
        lax.ppermute(block, axis, shifted_pairs(count, steps)) for steps in range(1, count)
    ]
    sources = (position - lax.iota(jnp.int32, count)) % count
    return pieces, sources


def scatter_slots(slots, axis):
    count = lax.axis_size(axis)
    if count > 8:
        return lax.psum_scatter(slots, axis, scatter_dimension=0, tiled=True)
    rows = slots.shape[0] // count
    total = slots[:rows]
    for steps in range(1, count):
        total = total + lax.ppermute(
            slots[steps * rows : (steps + 1) * rows].astype(jnp.bfloat16),
            axis,
            shifted_pairs(count, -steps),
        ).astype(jnp.float32)
    return total


def scatter_parts(own, sent, axis):
    count = lax.axis_size(axis)
    rows = own.shape[0]
    total = own
    for steps in range(1, count):
        total = total + lax.ppermute(
            sent[steps - 1], axis, shifted_pairs(count, -steps)
        ).astype(jnp.float32)
    return total


def copy_to_vmem(source, target):
    pltpu.sync_copy(source, target)


def staged(weights):
    return pl.pallas_call(
        copy_to_vmem,
        out_shape=jax.ShapeDtypeStruct(weights.shape, weights.dtype),
        in_specs=[pl.BlockSpec(memory_space=pl.ANY)],
        out_specs=pl.BlockSpec(memory_space=pltpu.VMEM),
    )(weights)


def head_reduce(key_proj, value_proj, key_grad, value_grad):
    count = lax.axis_size("head")
    position = lax.axis_index("head")
    depth = count.bit_length() - 1
    contraction = (((1,), (1,)), ((), ()))
    if count == 1 or count != 1 << depth:
        partial = lax.dot_general(
            key_proj, key_grad, contraction, preferred_element_type=jnp.float32
        ) + lax.dot_general(value_proj, value_grad, contraction, preferred_element_type=jnp.float32)
        return lax.psum_scatter(partial, "head", scatter_dimension=0, tiled=True).astype(
            jnp.bfloat16
        )
    block = key_proj.shape[0] // count
    key_proj = staged(key_proj)
    value_proj = staged(value_proj)
    key_split = key_proj.reshape(count // 2, 2, block, key_proj.shape[1])
    value_split = value_proj.reshape(count // 2, 2, block, value_proj.shape[1])

    def project(half):
        return jnp.einsum(
            "arf,tf->art",
            lax.dynamic_index_in_dim(key_split, half, 1, keepdims=False),
            key_grad,
            preferred_element_type=jnp.float32,
        ) + jnp.einsum(
            "arf,tf->art",
            lax.dynamic_index_in_dim(value_split, half, 1, keepdims=False),
            value_grad,
            preferred_element_type=jnp.float32,
        )

    own_bit = position % 2
    sent = project(1 - own_bit)
    kept = project(own_bit)
    current = kept + lax.ppermute(
        sent.astype(jnp.bfloat16), "head", [(i, i ^ 1) for i in range(count)]
    ).astype(jnp.float32)
    for level in range(1, depth):
        current = current.reshape(-1, 2, block, current.shape[-1])
        own_bit = (position // (1 << level)) % 2
        kept = lax.dynamic_index_in_dim(current, own_bit, 1, keepdims=False)
        sent = lax.dynamic_index_in_dim(current, 1 - own_bit, 1, keepdims=False)
        arrived = lax.ppermute(
            sent.astype(jnp.bfloat16), "head", [(i, i ^ (1 << level)) for i in range(count)]
        )
        current = kept + arrived.astype(jnp.float32)
    return current.reshape(block, -1).astype(jnp.bfloat16)


def attention_kernel(query_ref, grad_ref, mask_ref, *refs):
    slot_count = (len(refs) - 1) // 2
    kv_ref = jnp.concatenate([piece[...] for piece in refs[:slot_count]], axis=0)
    query_out, own_out = refs[slot_count], refs[slot_count + 1]
    sent_outs = refs[slot_count + 2 :]
    inv_root = HD ** (-0.5)
    kv_cols = kv_ref.shape[1] // 2
    kv_heads = kv_cols // HD
    rows = query_ref.shape[0]
    group_size = query_ref.shape[1] // kv_cols
    if mask_ref.shape[0] == 1:
        allowed = mask_ref[...] > 0
    else:
        allowed = jnp.concatenate([mask_ref[...]] * group_size, axis=0) > 0
    across = (((1,), (1,)), ((), ()))
    down = (((0,), (0,)), ((), ()))
    for kv_head in range(kv_heads):
        key_head = kv_ref[:, kv_head * HD : (kv_head + 1) * HD]
        value_head = kv_ref[:, kv_cols + kv_head * HD : kv_cols + (kv_head + 1) * HD]
        base = kv_head * group_size * HD
        query_stack = jnp.concatenate(
            [query_ref[:, base + m * HD : base + (m + 1) * HD] for m in range(group_size)], axis=0
        )
        grad_stack = jnp.concatenate(
            [grad_ref[:, base + m * HD : base + (m + 1) * HD] for m in range(group_size)], axis=0
        )
        scores = (
            lax.dot_general(query_stack, key_head, across, preferred_element_type=jnp.float32)
            * inv_root
        )
        scores = jnp.where(allowed, scores, masked_score)
        row_max = jnp.max(scores, axis=1, keepdims=True)
        shifted = jnp.exp(scores - row_max)
        row_sum = jnp.sum(shifted, axis=1, keepdims=True)
        weighted = jnp.dot(
            shifted.astype(jnp.bfloat16), value_head, preferred_element_type=jnp.float32
        )
        attended = (weighted / row_sum).astype(jnp.bfloat16)
        probs = shifted * (1.0 / row_sum)
        row_delta = jnp.sum(
            grad_stack.astype(jnp.float32) * attended.astype(jnp.float32), axis=1, keepdims=True
        )
        dprobs = lax.dot_general(grad_stack, value_head, across, preferred_element_type=jnp.float32)
        dscores = (probs * (dprobs - row_delta)).astype(jnp.bfloat16)
        query_term = jnp.dot(dscores, key_head, preferred_element_type=jnp.float32) * inv_root
        for m in range(group_size):
            query_out[:, base + m * HD : base + (m + 1) * HD] = query_term[
                m * rows : (m + 1) * rows
            ].astype(jnp.bfloat16)
        key_sum = lax.dot_general(dscores, query_stack, down, preferred_element_type=jnp.float32)
        value_sum = lax.dot_general(
            probs.astype(jnp.bfloat16), grad_stack, down, preferred_element_type=jnp.float32
        )
        key_sum = key_sum * inv_root
        key_cols = slice(kv_head * HD, (kv_head + 1) * HD)
        value_cols = slice(kv_cols + kv_head * HD, kv_cols + (kv_head + 1) * HD)
        own_out[:, key_cols] = key_sum[:rows]
        own_out[:, value_cols] = value_sum[:rows]
        for slot, sent_out in enumerate(sent_outs, start=1):
            sent_out[:, key_cols] = key_sum[slot * rows : (slot + 1) * rows].astype(jnp.bfloat16)
            sent_out[:, value_cols] = value_sum[slot * rows : (slot + 1) * rows].astype(
                jnp.bfloat16
            )


def attention_block(queries, out_grad, kv_pieces, allowed, interpret=False):
    rows = queries.shape[0]
    width = kv_pieces[0].shape[1]
    return pl.pallas_call(
        attention_kernel,
        out_shape=(
            jax.ShapeDtypeStruct(queries.shape, jnp.bfloat16),
            jax.ShapeDtypeStruct((rows, width), jnp.float32),
        )
        + tuple(
            jax.ShapeDtypeStruct((rows, width), jnp.bfloat16) for _ in range(len(kv_pieces) - 1)
        ),
        interpret=interpret,
    )(queries, out_grad, allowed.astype(jnp.int32), *kv_pieces)


def local(
    queries, key_states, value_states, out_grad, mask_flags, shard_blocks, key_proj, value_proj
):
    rows_here = queries.shape[0]
    kv_cols = key_states.shape[1]
    kv_heads = kv_cols // HD
    group_size = queries.shape[1] // kv_cols
    inv_root = HD ** (-0.5)
    position = lax.axis_index("ctx")
    query_heads = queries.reshape(rows_here, kv_heads, group_size, HD)
    grad_heads = out_grad.reshape(rows_here, kv_heads, group_size, HD)
    own_blocks = lax.dynamic_slice_in_dim(
        shard_blocks, position * (rows_here // BLK), rows_here // BLK
    )
    own_flags = select_rows(mask_flags, own_blocks)

    kv_pieces, sources = gather_slots(
        jnp.concatenate([key_states, value_states], axis=1), "ctx"
    )
    kv_rows = jnp.concatenate(kv_pieces, axis=0)
    row_count = kv_rows.shape[0]
    blocks_here = rows_here // BLK
    key_blocks = lax.iota(jnp.int32, row_count // BLK)
    key_doc_blocks = pick(
        shard_blocks,
        pick(sources, key_blocks // blocks_here) * blocks_here + key_blocks % blocks_here,
    )
    step_rows = math.gcd(row_count, 512)
    steps = row_count // step_rows

    def chunk(offset):
        block = lax.dynamic_slice_in_dim(kv_rows, offset, step_rows)
        key_heads = block[:, :kv_cols].reshape(step_rows, kv_heads, HD)
        value_heads = block[:, kv_cols:].reshape(step_rows, kv_heads, HD)
        their_blocks = lax.dynamic_slice_in_dim(key_doc_blocks, offset // BLK, step_rows // BLK)
        pair_flags = select_cols(own_flags, their_blocks) > 0
        allowed = jnp.repeat(jnp.repeat(pair_flags, BLK, axis=0), BLK, axis=1)
        scores = (
            jnp.einsum("qkgd,tkd->kgqt", query_heads, key_heads, preferred_element_type=jnp.float32)
            * inv_root
        )
        scores = jnp.where(allowed[None, None], scores, masked_score)
        return key_heads, value_heads, allowed, scores

    def forward_stats(offset, current):
        row_max, row_sum, weighted = current
        key_heads, value_heads, allowed, scores = chunk(offset)
        new_max = jnp.maximum(row_max, jnp.max(scores, axis=-1))
        rescale = jnp.exp(row_max - new_max)
        shifted = jnp.where(allowed[None, None], jnp.exp(scores - new_max[..., None]), 0.0)
        row_sum = row_sum * rescale + jnp.sum(shifted, axis=-1)
        weighted = weighted * rescale[..., None] + jnp.einsum(
            "kgqt,tkd->kgqd",
            shifted.astype(jnp.bfloat16),
            value_heads,
            preferred_element_type=jnp.float32,
        )
        return (new_max, row_sum, weighted)

    def backward_chunk(offset, log_total, row_delta, scores_given=None):
        key_heads, value_heads, allowed, scores = chunk(offset)
        if scores_given is not None:
            scores = scores_given
        probs = jnp.exp(scores - log_total[..., None])
        dprobs = jnp.einsum(
            "qkgd,tkd->kgqt", grad_heads, value_heads, preferred_element_type=jnp.float32
        )
        dscores = (probs * (dprobs - row_delta[..., None])).astype(jnp.bfloat16)
        probs_low = probs.astype(jnp.bfloat16)
        query_term = (
            jnp.einsum("kgqt,tkd->qkgd", dscores, key_heads, preferred_element_type=jnp.float32)
            * inv_root
        )
        key_term = (
            jnp.einsum("kgqt,qkgd->tkd", dscores, query_heads, preferred_element_type=jnp.float32)
            * inv_root
        )
        value_term = jnp.einsum(
            "kgqt,qkgd->tkd", probs_low, grad_heads, preferred_element_type=jnp.float32
        )
        kv_term = jnp.concatenate(
            [key_term.reshape(step_rows, kv_cols), value_term.reshape(step_rows, kv_cols)], axis=1
        )
        return query_term, kv_term

    if steps == 1 and lax.axis_size("ctx") <= 8:
        if rows_here == BLK:
            column_flags = select_cols(own_flags, key_doc_blocks) > 0
            allowed = jnp.repeat(column_flags, BLK, axis=1)
        else:
            allowed = chunk(0)[2]
        query_grad, own_part, *sent_parts = attention_block(queries, out_grad, kv_pieces, allowed)
        kv_grad = scatter_parts(own_part, sent_parts, "ctx")
    else:
        start_stats = (
            jnp.full((kv_heads, group_size, rows_here), masked_score, jnp.float32),
            jnp.zeros((kv_heads, group_size, rows_here), jnp.float32),
            jnp.zeros((kv_heads, group_size, rows_here, HD), jnp.float32),
        )
        row_max, row_sum, weighted = lax.fori_loop(
            0, steps, lambda i, c: forward_stats(i * step_rows, c), start_stats
        )
        log_total = row_max + jnp.log(row_sum)
        attended = (weighted / row_sum[..., None]).astype(jnp.bfloat16)
        row_delta = jnp.einsum(
            "kgqd,qkgd->kgq", attended, grad_heads, preferred_element_type=jnp.float32
        )

        def backward_visit(turn_index, current):
            query_now, kv_now = current
            offset = turn_index * step_rows
            query_term, kv_term = backward_chunk(offset, log_total, row_delta)
            kv_now = lax.dynamic_update_slice_in_dim(kv_now, kv_term, offset, 0)
            return (query_now + query_term, kv_now)

        query_acc, kv_acc = lax.fori_loop(
            0,
            steps,
            backward_visit,
            (
                jnp.zeros((rows_here, kv_heads, group_size, HD), jnp.float32),
                jnp.zeros((row_count, 2 * kv_cols), jnp.float32),
            ),
        )
        query_grad = query_acc.reshape(rows_here, -1).astype(jnp.bfloat16)
        kv_grad = scatter_slots(kv_acc, "ctx")

    key_grad = kv_grad[:, :kv_cols].astype(jnp.bfloat16)
    value_grad = kv_grad[:, kv_cols:].astype(jnp.bfloat16)
    input_grad_t = head_reduce(key_proj, value_proj, key_grad, value_grad)
    return (query_grad, key_grad, value_grad, input_grad_t)


def solution(mesh):
    return jax.shard_map(
        local,
        mesh=mesh,
        in_specs=(
            P(("groups", "ctx"), "head"),
            P(("groups", "ctx"), "head"),
            P(("groups", "ctx"), "head"),
            P(("groups", "ctx"), "head"),
            P("groups", None),
            P("groups"),
            P(None, "head"),
            P(None, "head"),
        ),
        out_specs=(
            P(("groups", "ctx"), "head"),
            P(("groups", "ctx"), "head"),
            P(("groups", "ctx"), "head"),
            P("head", ("groups", "ctx")),
        ),
        check_vma=False,
    )
```

```python
import math

import jax
import jax.numpy as jnp
from jax import lax
from jax.experimental import pallas as pl
from jax.experimental.pallas import tpu as pltpu
from jax.sharding import PartitionSpec as P

HD = 128
BLK = 128


masked_score = -1e30


def select_rows(lookup, picked):
    onehot = (picked[:, None] == lax.iota(jnp.int32, lookup.shape[0])[None, :]).astype(jnp.int32)
    return jnp.sum(onehot[:, :, None] * lookup[None, :, :], axis=1)


def select_cols(lookup, picked):
    onehot = (picked[:, None] == lax.iota(jnp.int32, lookup.shape[1])[None, :]).astype(jnp.int32)
    return jnp.sum(lookup[:, None, :] * onehot[None, :, :], axis=2)


def pick(vector, picked):
    onehot = (picked[:, None] == lax.iota(jnp.int32, vector.shape[0])[None, :]).astype(jnp.int32)
    return jnp.sum(onehot * vector[None, :], axis=1)


def shifted_pairs(count, steps):
    return [(source, (source + steps) % count) for source in range(count)]


def gather_slots(block, axis):
    count = lax.axis_size(axis)
    position = lax.axis_index(axis)
    if count > 8:
        gathered = lax.all_gather(block, axis, axis=0, tiled=True)
        return [gathered], lax.iota(jnp.int32, count)
    pieces = [block] + [
        lax.ppermute(block, axis, shifted_pairs(count, steps)) for steps in range(1, count)
    ]
    sources = (position - lax.iota(jnp.int32, count)) % count
    return pieces, sources


def scatter_slots(slots, axis):
    count = lax.axis_size(axis)
    if count > 8:
        return lax.psum_scatter(slots, axis, scatter_dimension=0, tiled=True)
    rows = slots.shape[0] // count
    total = slots[:rows]
    for steps in range(1, count):
        total = total + lax.ppermute(
            slots[steps * rows : (steps + 1) * rows].astype(jnp.bfloat16),
            axis,
            shifted_pairs(count, -steps),
        ).astype(jnp.float32)
    return total


def scatter_parts(own, sent, axis):
    count = lax.axis_size(axis)
    rows = own.shape[0]
    total = own
    for steps in range(1, count):
        total = total + lax.ppermute(
            sent[steps - 1], axis, shifted_pairs(count, -steps)
        ).astype(jnp.float32)
    return total


def copy_to_vmem(source, target):
    pltpu.sync_copy(source, target)


def staged(weights):
    return pl.pallas_call(
        copy_to_vmem,
        out_shape=jax.ShapeDtypeStruct(weights.shape, weights.dtype),
        in_specs=[pl.BlockSpec(memory_space=pl.ANY)],
        out_specs=pl.BlockSpec(memory_space=pltpu.VMEM),
    )(weights)


def head_reduce(key_proj, value_proj, key_grad, value_grad):
    count = lax.axis_size("head")
    position = lax.axis_index("head")
    depth = count.bit_length() - 1
    contraction = (((1,), (1,)), ((), ()))
    if count == 1 or count != 1 << depth:
        partial = lax.dot_general(
            key_proj, key_grad, contraction, preferred_element_type=jnp.float32
        ) + lax.dot_general(value_proj, value_grad, contraction, preferred_element_type=jnp.float32)
        return lax.psum_scatter(partial, "head", scatter_dimension=0, tiled=True).astype(
            jnp.bfloat16
        )
    block = key_proj.shape[0] // count
    key_proj = staged(key_proj)
    value_proj = staged(value_proj)
    key_split = key_proj.reshape(count // 2, 2, block, key_proj.shape[1])
    value_split = value_proj.reshape(count // 2, 2, block, value_proj.shape[1])

    def project(half):
        return jnp.einsum(
            "arf,tf->art",
            lax.dynamic_index_in_dim(key_split, half, 1, keepdims=False),
            key_grad,
            preferred_element_type=jnp.float32,
        ) + jnp.einsum(
            "arf,tf->art",
            lax.dynamic_index_in_dim(value_split, half, 1, keepdims=False),
            value_grad,
            preferred_element_type=jnp.float32,
        )

    own_bit = position % 2
    sent = project(1 - own_bit)
    kept = project(own_bit)
    current = kept + lax.ppermute(
        sent.astype(jnp.bfloat16), "head", [(i, i ^ 1) for i in range(count)]
    ).astype(jnp.float32)
    for level in range(1, depth):
        current = current.reshape(-1, 2, block, current.shape[-1])
        own_bit = (position // (1 << level)) % 2
        kept = lax.dynamic_index_in_dim(current, own_bit, 1, keepdims=False)
        sent = lax.dynamic_index_in_dim(current, 1 - own_bit, 1, keepdims=False)
        arrived = lax.ppermute(
            sent.astype(jnp.bfloat16), "head", [(i, i ^ (1 << level)) for i in range(count)]
        )
        current = kept + arrived.astype(jnp.float32)
    return current.reshape(block, -1).astype(jnp.bfloat16)


def attention_kernel(query_ref, grad_ref, mask_ref, *refs):
    slot_count = (len(refs) - 1) // 2
    kv_ref = jnp.concatenate([piece[...] for piece in refs[:slot_count]], axis=0)
    query_out, own_out = refs[slot_count], refs[slot_count + 1]
    sent_outs = refs[slot_count + 2 :]
    inv_root = HD ** (-0.5)
    kv_cols = kv_ref.shape[1] // 2
    kv_heads = kv_cols // HD
    rows = query_ref.shape[0]
    group_size = query_ref.shape[1] // kv_cols
    if mask_ref.shape[0] == 1:
        key_count = refs[0].shape[0] * slot_count
        column_block = lax.broadcasted_iota(jnp.int32, (1, key_count), 1) // BLK
        flags = jnp.zeros((1, key_count), jnp.int32)
        for block in range(mask_ref.shape[1]):
            flags = jnp.where(column_block == block, mask_ref[0, block], flags)
        allowed = flags > 0
    else:
        allowed = jnp.concatenate([mask_ref[...]] * group_size, axis=0) > 0
    across = (((1,), (1,)), ((), ()))
    down = (((0,), (0,)), ((), ()))
    for kv_head in range(kv_heads):
        key_head = kv_ref[:, kv_head * HD : (kv_head + 1) * HD]
        value_head = kv_ref[:, kv_cols + kv_head * HD : kv_cols + (kv_head + 1) * HD]
        base = kv_head * group_size * HD
        query_stack = jnp.concatenate(
            [query_ref[:, base + m * HD : base + (m + 1) * HD] for m in range(group_size)], axis=0
        )
        grad_stack = jnp.concatenate(
            [grad_ref[:, base + m * HD : base + (m + 1) * HD] for m in range(group_size)], axis=0
        )
        scores = (
            lax.dot_general(query_stack, key_head, across, preferred_element_type=jnp.float32)
            * inv_root
        )
        scores = jnp.where(allowed, scores, masked_score)
        row_max = jnp.max(scores, axis=1, keepdims=True)
        shifted = jnp.exp(scores - row_max)
        row_sum = jnp.sum(shifted, axis=1, keepdims=True)
        weighted = jnp.dot(
            shifted.astype(jnp.bfloat16), value_head, preferred_element_type=jnp.float32
        )
        attended = (weighted / row_sum).astype(jnp.bfloat16)
        probs = shifted * (1.0 / row_sum)
        row_delta = jnp.sum(
            grad_stack.astype(jnp.float32) * attended.astype(jnp.float32), axis=1, keepdims=True
        )
        dprobs = lax.dot_general(grad_stack, value_head, across, preferred_element_type=jnp.float32)
        dscores = (probs * (dprobs - row_delta)).astype(jnp.bfloat16)
        query_term = jnp.dot(dscores, key_head, preferred_element_type=jnp.float32) * inv_root
        for m in range(group_size):
            query_out[:, base + m * HD : base + (m + 1) * HD] = query_term[
                m * rows : (m + 1) * rows
            ].astype(jnp.bfloat16)
        key_sum = lax.dot_general(dscores, query_stack, down, preferred_element_type=jnp.float32)
        value_sum = lax.dot_general(
            probs.astype(jnp.bfloat16), grad_stack, down, preferred_element_type=jnp.float32
        )
        key_sum = key_sum * inv_root
        key_cols = slice(kv_head * HD, (kv_head + 1) * HD)
        value_cols = slice(kv_cols + kv_head * HD, kv_cols + (kv_head + 1) * HD)
        own_out[:, key_cols] = key_sum[:rows]
        own_out[:, value_cols] = value_sum[:rows]
        for slot, sent_out in enumerate(sent_outs, start=1):
            sent_out[:, key_cols] = key_sum[slot * rows : (slot + 1) * rows].astype(jnp.bfloat16)
            sent_out[:, value_cols] = value_sum[slot * rows : (slot + 1) * rows].astype(
                jnp.bfloat16
            )


def attention_block(queries, out_grad, kv_pieces, allowed, interpret=False):
    rows = queries.shape[0]
    width = kv_pieces[0].shape[1]
    small_mask = allowed.shape[0] == 1
    mask_spec = pl.BlockSpec(memory_space=pltpu.SMEM if small_mask else pltpu.VMEM)
    other_spec = pl.BlockSpec(memory_space=pltpu.VMEM)
    return pl.pallas_call(
        attention_kernel,
        in_specs=[other_spec, other_spec, mask_spec] + [other_spec] * len(kv_pieces),
        out_shape=(
            jax.ShapeDtypeStruct(queries.shape, jnp.bfloat16),
            jax.ShapeDtypeStruct((rows, width), jnp.float32),
        )
        + tuple(
            jax.ShapeDtypeStruct((rows, width), jnp.bfloat16) for _ in range(len(kv_pieces) - 1)
        ),
        interpret=interpret,
    )(queries, out_grad, allowed.astype(jnp.int32), *kv_pieces)


def local(
    queries, key_states, value_states, out_grad, mask_flags, shard_blocks, key_proj, value_proj
):
    rows_here = queries.shape[0]
    kv_cols = key_states.shape[1]
    kv_heads = kv_cols // HD
    group_size = queries.shape[1] // kv_cols
    inv_root = HD ** (-0.5)
    position = lax.axis_index("ctx")
    query_heads = queries.reshape(rows_here, kv_heads, group_size, HD)
    grad_heads = out_grad.reshape(rows_here, kv_heads, group_size, HD)
    own_blocks = lax.dynamic_slice_in_dim(
        shard_blocks, position * (rows_here // BLK), rows_here // BLK
    )
    own_flags = select_rows(mask_flags, own_blocks)

    kv_pieces, sources = gather_slots(
        jnp.concatenate([key_states, value_states], axis=1), "ctx"
    )
    kv_rows = jnp.concatenate(kv_pieces, axis=0)
    row_count = kv_rows.shape[0]
    blocks_here = rows_here // BLK
    key_blocks = lax.iota(jnp.int32, row_count // BLK)
    key_doc_blocks = pick(
        shard_blocks,
        pick(sources, key_blocks // blocks_here) * blocks_here + key_blocks % blocks_here,
    )
    step_rows = math.gcd(row_count, 512)
    steps = row_count // step_rows

    def chunk(offset):
        block = lax.dynamic_slice_in_dim(kv_rows, offset, step_rows)
        key_heads = block[:, :kv_cols].reshape(step_rows, kv_heads, HD)
        value_heads = block[:, kv_cols:].reshape(step_rows, kv_heads, HD)
        their_blocks = lax.dynamic_slice_in_dim(key_doc_blocks, offset // BLK, step_rows // BLK)
        pair_flags = select_cols(own_flags, their_blocks) > 0
        allowed = jnp.repeat(jnp.repeat(pair_flags, BLK, axis=0), BLK, axis=1)
        scores = (
            jnp.einsum("qkgd,tkd->kgqt", query_heads, key_heads, preferred_element_type=jnp.float32)
            * inv_root
        )
        scores = jnp.where(allowed[None, None], scores, masked_score)
        return key_heads, value_heads, allowed, scores

    def forward_stats(offset, current):
        row_max, row_sum, weighted = current
        key_heads, value_heads, allowed, scores = chunk(offset)
        new_max = jnp.maximum(row_max, jnp.max(scores, axis=-1))
        rescale = jnp.exp(row_max - new_max)
        shifted = jnp.where(allowed[None, None], jnp.exp(scores - new_max[..., None]), 0.0)
        row_sum = row_sum * rescale + jnp.sum(shifted, axis=-1)
        weighted = weighted * rescale[..., None] + jnp.einsum(
            "kgqt,tkd->kgqd",
            shifted.astype(jnp.bfloat16),
            value_heads,
            preferred_element_type=jnp.float32,
        )
        return (new_max, row_sum, weighted)

    def backward_chunk(offset, log_total, row_delta, scores_given=None):
        key_heads, value_heads, allowed, scores = chunk(offset)
        if scores_given is not None:
            scores = scores_given
        probs = jnp.exp(scores - log_total[..., None])
        dprobs = jnp.einsum(
            "qkgd,tkd->kgqt", grad_heads, value_heads, preferred_element_type=jnp.float32
        )
        dscores = (probs * (dprobs - row_delta[..., None])).astype(jnp.bfloat16)
        probs_low = probs.astype(jnp.bfloat16)
        query_term = (
            jnp.einsum("kgqt,tkd->qkgd", dscores, key_heads, preferred_element_type=jnp.float32)
            * inv_root
        )
        key_term = (
            jnp.einsum("kgqt,qkgd->tkd", dscores, query_heads, preferred_element_type=jnp.float32)
            * inv_root
        )
        value_term = jnp.einsum(
            "kgqt,qkgd->tkd", probs_low, grad_heads, preferred_element_type=jnp.float32
        )
        kv_term = jnp.concatenate(
            [key_term.reshape(step_rows, kv_cols), value_term.reshape(step_rows, kv_cols)], axis=1
        )
        return query_term, kv_term

    if steps == 1 and lax.axis_size("ctx") <= 8:
        if rows_here == BLK:
            allowed = select_cols(own_flags, key_doc_blocks) > 0
        else:
            allowed = chunk(0)[2]
        query_grad, own_part, *sent_parts = attention_block(queries, out_grad, kv_pieces, allowed)
        kv_grad = scatter_parts(own_part, sent_parts, "ctx")
    else:
        start_stats = (
            jnp.full((kv_heads, group_size, rows_here), masked_score, jnp.float32),
            jnp.zeros((kv_heads, group_size, rows_here), jnp.float32),
            jnp.zeros((kv_heads, group_size, rows_here, HD), jnp.float32),
        )
        row_max, row_sum, weighted = lax.fori_loop(
            0, steps, lambda i, c: forward_stats(i * step_rows, c), start_stats
        )
        log_total = row_max + jnp.log(row_sum)
        attended = (weighted / row_sum[..., None]).astype(jnp.bfloat16)
        row_delta = jnp.einsum(
            "kgqd,qkgd->kgq", attended, grad_heads, preferred_element_type=jnp.float32
        )

        def backward_visit(turn_index, current):
            query_now, kv_now = current
            offset = turn_index * step_rows
            query_term, kv_term = backward_chunk(offset, log_total, row_delta)
            kv_now = lax.dynamic_update_slice_in_dim(kv_now, kv_term, offset, 0)
            return (query_now + query_term, kv_now)

        query_acc, kv_acc = lax.fori_loop(
            0,
            steps,
            backward_visit,
            (
                jnp.zeros((rows_here, kv_heads, group_size, HD), jnp.float32),
                jnp.zeros((row_count, 2 * kv_cols), jnp.float32),
            ),
        )
        query_grad = query_acc.reshape(rows_here, -1).astype(jnp.bfloat16)
        kv_grad = scatter_slots(kv_acc, "ctx")

    key_grad = kv_grad[:, :kv_cols].astype(jnp.bfloat16)
    value_grad = kv_grad[:, kv_cols:].astype(jnp.bfloat16)
    input_grad_t = head_reduce(key_proj, value_proj, key_grad, value_grad)
    return (query_grad, key_grad, value_grad, input_grad_t)


def solution(mesh):
    return jax.shard_map(
        local,
        mesh=mesh,
        in_specs=(
            P(("groups", "ctx"), "head"),
            P(("groups", "ctx"), "head"),
            P(("groups", "ctx"), "head"),
            P(("groups", "ctx"), "head"),
            P("groups", None),
            P("groups"),
            P(None, "head"),
            P(None, "head"),
        ),
        out_specs=(
            P(("groups", "ctx"), "head"),
            P(("groups", "ctx"), "head"),
            P(("groups", "ctx"), "head"),
            P("head", ("groups", "ctx")),
        ),
        check_vma=False,
    )
```

```python
import math

import jax
import jax.numpy as jnp
from jax import lax
from jax.experimental import pallas as pl
from jax.experimental.pallas import tpu as pltpu
from jax.sharding import PartitionSpec as P

HD = 128
BLK = 128


masked_score = -1e30


def select_rows(lookup, picked):
    onehot = (picked[:, None] == lax.iota(jnp.int32, lookup.shape[0])[None, :]).astype(jnp.int32)
    return jnp.sum(onehot[:, :, None] * lookup[None, :, :], axis=1)


def select_cols(lookup, picked):
    onehot = (picked[:, None] == lax.iota(jnp.int32, lookup.shape[1])[None, :]).astype(jnp.int32)
    return jnp.sum(lookup[:, None, :] * onehot[None, :, :], axis=2)


def pick(vector, picked):
    onehot = (picked[:, None] == lax.iota(jnp.int32, vector.shape[0])[None, :]).astype(jnp.int32)
    return jnp.sum(onehot * vector[None, :], axis=1)


def shifted_pairs(count, steps):
    return [(source, (source + steps) % count) for source in range(count)]


def gather_slots(block, axis):
    count = lax.axis_size(axis)
    position = lax.axis_index(axis)
    if count > 8:
        gathered = lax.all_gather(block, axis, axis=0, tiled=True)
        return [gathered], lax.iota(jnp.int32, count)
    pieces = [block] + [
        lax.ppermute(block, axis, shifted_pairs(count, steps)) for steps in range(1, count)
    ]
    sources = (position - lax.iota(jnp.int32, count)) % count
    return pieces, sources


def scatter_slots(slots, axis):
    count = lax.axis_size(axis)
    if count > 8:
        return lax.psum_scatter(slots, axis, scatter_dimension=0, tiled=True)
    rows = slots.shape[0] // count
    total = slots[:rows]
    for steps in range(1, count):
        total = total + lax.ppermute(
            slots[steps * rows : (steps + 1) * rows].astype(jnp.bfloat16),
            axis,
            shifted_pairs(count, -steps),
        ).astype(jnp.float32)
    return total


def scatter_parts(own, sent, axis):
    count = lax.axis_size(axis)
    rows = own.shape[0]
    total = own
    for steps in range(1, count):
        total = total + lax.ppermute(
            sent[steps - 1], axis, shifted_pairs(count, -steps)
        ).astype(jnp.float32)
    return total


def copy_to_vmem(source, target):
    pltpu.sync_copy(source, target)


def staged(weights):
    return pl.pallas_call(
        copy_to_vmem,
        out_shape=jax.ShapeDtypeStruct(weights.shape, weights.dtype),
        in_specs=[pl.BlockSpec(memory_space=pl.ANY)],
        out_specs=pl.BlockSpec(memory_space=pltpu.VMEM),
    )(weights)


def head_reduce(key_proj, value_proj, key_grad, value_grad):
    count = lax.axis_size("head")
    position = lax.axis_index("head")
    depth = count.bit_length() - 1
    contraction = (((1,), (1,)), ((), ()))
    if count == 1 or count != 1 << depth:
        partial = lax.dot_general(
            key_proj, key_grad, contraction, preferred_element_type=jnp.float32
        ) + lax.dot_general(value_proj, value_grad, contraction, preferred_element_type=jnp.float32)
        return lax.psum_scatter(partial, "head", scatter_dimension=0, tiled=True).astype(
            jnp.bfloat16
        )
    block = key_proj.shape[0] // count
    key_split = key_proj.reshape(count // 2, 2, block, key_proj.shape[1])
    value_split = value_proj.reshape(count // 2, 2, block, value_proj.shape[1])

    def project(half):
        return jnp.einsum(
            "arf,tf->art",
            lax.dynamic_index_in_dim(key_split, half, 1, keepdims=False),
            key_grad,
            preferred_element_type=jnp.float32,
        ) + jnp.einsum(
            "arf,tf->art",
            lax.dynamic_index_in_dim(value_split, half, 1, keepdims=False),
            value_grad,
            preferred_element_type=jnp.float32,
        )

    own_bit = position % 2
    sent = project(1 - own_bit)
    kept = project(own_bit)
    current = kept + lax.ppermute(
        sent.astype(jnp.bfloat16), "head", [(i, i ^ 1) for i in range(count)]
    ).astype(jnp.float32)
    for level in range(1, depth):
        current = current.reshape(-1, 2, block, current.shape[-1])
        own_bit = (position // (1 << level)) % 2
        kept = lax.dynamic_index_in_dim(current, own_bit, 1, keepdims=False)
        sent = lax.dynamic_index_in_dim(current, 1 - own_bit, 1, keepdims=False)
        arrived = lax.ppermute(
            sent.astype(jnp.bfloat16), "head", [(i, i ^ (1 << level)) for i in range(count)]
        )
        current = kept + arrived.astype(jnp.float32)
    return current.reshape(block, -1).astype(jnp.bfloat16)


def attention_kernel(query_ref, grad_ref, mask_ref, *refs):
    slot_count = (len(refs) - 1) // 2
    kv_ref = jnp.concatenate([piece[...] for piece in refs[:slot_count]], axis=0)
    query_out, own_out = refs[slot_count], refs[slot_count + 1]
    sent_outs = refs[slot_count + 2 :]
    inv_root = HD ** (-0.5)
    kv_cols = kv_ref.shape[1] // 2
    kv_heads = kv_cols // HD
    rows = query_ref.shape[0]
    group_size = query_ref.shape[1] // kv_cols
    if mask_ref.shape[0] == 1:
        allowed = mask_ref[...] > 0
    else:
        allowed = jnp.concatenate([mask_ref[...]] * group_size, axis=0) > 0
    across = (((1,), (1,)), ((), ()))
    down = (((0,), (0,)), ((), ()))
    for kv_head in range(kv_heads):
        key_head = kv_ref[:, kv_head * HD : (kv_head + 1) * HD]
        value_head = kv_ref[:, kv_cols + kv_head * HD : kv_cols + (kv_head + 1) * HD]
        base = kv_head * group_size * HD
        query_stack = jnp.concatenate(
            [query_ref[:, base + m * HD : base + (m + 1) * HD] for m in range(group_size)], axis=0
        )
        grad_stack = jnp.concatenate(
            [grad_ref[:, base + m * HD : base + (m + 1) * HD] for m in range(group_size)], axis=0
        )
        scores = (
            lax.dot_general(query_stack, key_head, across, preferred_element_type=jnp.float32)
            * inv_root
        )
        scores = jnp.where(allowed, scores, masked_score)
        row_max = jnp.max(scores, axis=1, keepdims=True)
        shifted = jnp.exp(scores - row_max)
        row_sum = jnp.sum(shifted, axis=1, keepdims=True)
        weighted = jnp.dot(
            shifted.astype(jnp.bfloat16), value_head, preferred_element_type=jnp.float32
        )
        attended = (weighted / row_sum).astype(jnp.bfloat16)
        probs = shifted * (1.0 / row_sum)
        row_delta = jnp.sum(
            grad_stack.astype(jnp.float32) * attended.astype(jnp.float32), axis=1, keepdims=True
        )
        dprobs = lax.dot_general(grad_stack, value_head, across, preferred_element_type=jnp.float32)
        dscores = (probs * (dprobs - row_delta)).astype(jnp.bfloat16)
        query_term = jnp.dot(dscores, key_head, preferred_element_type=jnp.float32) * inv_root
        for m in range(group_size):
            query_out[:, base + m * HD : base + (m + 1) * HD] = query_term[
                m * rows : (m + 1) * rows
            ].astype(jnp.bfloat16)
        key_sum = lax.dot_general(dscores, query_stack, down, preferred_element_type=jnp.float32)
        value_sum = lax.dot_general(
            probs.astype(jnp.bfloat16), grad_stack, down, preferred_element_type=jnp.float32
        )
        key_sum = key_sum * inv_root
        key_cols = slice(kv_head * HD, (kv_head + 1) * HD)
        value_cols = slice(kv_cols + kv_head * HD, kv_cols + (kv_head + 1) * HD)
        own_out[:, key_cols] = key_sum[:rows]
        own_out[:, value_cols] = value_sum[:rows]
        for slot, sent_out in enumerate(sent_outs, start=1):
            sent_out[:, key_cols] = key_sum[slot * rows : (slot + 1) * rows].astype(jnp.bfloat16)
            sent_out[:, value_cols] = value_sum[slot * rows : (slot + 1) * rows].astype(
                jnp.bfloat16
            )


def attention_block(queries, out_grad, kv_pieces, allowed, interpret=False):
    rows = queries.shape[0]
    width = kv_pieces[0].shape[1]
    return pl.pallas_call(
        attention_kernel,
        out_shape=(
            jax.ShapeDtypeStruct(queries.shape, jnp.bfloat16),
            jax.ShapeDtypeStruct((rows, width), jnp.float32),
        )
        + tuple(
            jax.ShapeDtypeStruct((rows, width), jnp.bfloat16) for _ in range(len(kv_pieces) - 1)
        ),
        interpret=interpret,
    )(queries, out_grad, allowed.astype(jnp.int32), *kv_pieces)


def local(
    queries, key_states, value_states, out_grad, mask_flags, shard_blocks, key_proj, value_proj
):
    rows_here = queries.shape[0]
    kv_cols = key_states.shape[1]
    kv_heads = kv_cols // HD
    group_size = queries.shape[1] // kv_cols
    inv_root = HD ** (-0.5)
    position = lax.axis_index("ctx")
    query_heads = queries.reshape(rows_here, kv_heads, group_size, HD)
    grad_heads = out_grad.reshape(rows_here, kv_heads, group_size, HD)
    own_blocks = lax.dynamic_slice_in_dim(
        shard_blocks, position * (rows_here // BLK), rows_here // BLK
    )
    own_flags = select_rows(mask_flags, own_blocks)

    kv_pieces, sources = gather_slots(
        jnp.concatenate([key_states, value_states], axis=1), "ctx"
    )
    kv_rows = jnp.concatenate(kv_pieces, axis=0)
    row_count = kv_rows.shape[0]
    blocks_here = rows_here // BLK
    key_blocks = lax.iota(jnp.int32, row_count // BLK)
    key_doc_blocks = pick(
        shard_blocks,
        pick(sources, key_blocks // blocks_here) * blocks_here + key_blocks % blocks_here,
    )
    step_rows = math.gcd(row_count, 512)
    steps = row_count // step_rows

    def chunk(offset):
        block = lax.dynamic_slice_in_dim(kv_rows, offset, step_rows)
        key_heads = block[:, :kv_cols].reshape(step_rows, kv_heads, HD)
        value_heads = block[:, kv_cols:].reshape(step_rows, kv_heads, HD)
        their_blocks = lax.dynamic_slice_in_dim(key_doc_blocks, offset // BLK, step_rows // BLK)
        pair_flags = select_cols(own_flags, their_blocks) > 0
        allowed = jnp.repeat(jnp.repeat(pair_flags, BLK, axis=0), BLK, axis=1)
        scores = (
            jnp.einsum("qkgd,tkd->kgqt", query_heads, key_heads, preferred_element_type=jnp.float32)
            * inv_root
        )
        scores = jnp.where(allowed[None, None], scores, masked_score)
        return key_heads, value_heads, allowed, scores

    def forward_stats(offset, current):
        row_max, row_sum, weighted = current
        key_heads, value_heads, allowed, scores = chunk(offset)
        new_max = jnp.maximum(row_max, jnp.max(scores, axis=-1))
        rescale = jnp.exp(row_max - new_max)
        shifted = jnp.where(allowed[None, None], jnp.exp(scores - new_max[..., None]), 0.0)
        row_sum = row_sum * rescale + jnp.sum(shifted, axis=-1)
        weighted = weighted * rescale[..., None] + jnp.einsum(
            "kgqt,tkd->kgqd",
            shifted.astype(jnp.bfloat16),
            value_heads,
            preferred_element_type=jnp.float32,
        )
        return (new_max, row_sum, weighted)

    def backward_chunk(offset, log_total, row_delta, scores_given=None):
        key_heads, value_heads, allowed, scores = chunk(offset)
        if scores_given is not None:
            scores = scores_given
        probs = jnp.exp(scores - log_total[..., None])
        dprobs = jnp.einsum(
            "qkgd,tkd->kgqt", grad_heads, value_heads, preferred_element_type=jnp.float32
        )
        dscores = (probs * (dprobs - row_delta[..., None])).astype(jnp.bfloat16)
        probs_low = probs.astype(jnp.bfloat16)
        query_term = (
            jnp.einsum("kgqt,tkd->qkgd", dscores, key_heads, preferred_element_type=jnp.float32)
            * inv_root
        )
        key_term = (
            jnp.einsum("kgqt,qkgd->tkd", dscores, query_heads, preferred_element_type=jnp.float32)
            * inv_root
        )
        value_term = jnp.einsum(
            "kgqt,qkgd->tkd", probs_low, grad_heads, preferred_element_type=jnp.float32
        )
        kv_term = jnp.concatenate(
            [key_term.reshape(step_rows, kv_cols), value_term.reshape(step_rows, kv_cols)], axis=1
        )
        return query_term, kv_term

    if steps == 1 and lax.axis_size("ctx") <= 8:
        if rows_here == BLK:
            column_flags = select_cols(own_flags, key_doc_blocks) > 0
            allowed = jnp.repeat(column_flags, BLK, axis=1)
        else:
            allowed = chunk(0)[2]
        query_grad, own_part, *sent_parts = attention_block(queries, out_grad, kv_pieces, allowed)
        kv_grad = scatter_parts(own_part, sent_parts, "ctx")
    else:
        start_stats = (
            jnp.full((kv_heads, group_size, rows_here), masked_score, jnp.float32),
            jnp.zeros((kv_heads, group_size, rows_here), jnp.float32),
            jnp.zeros((kv_heads, group_size, rows_here, HD), jnp.float32),
        )
        row_max, row_sum, weighted = lax.fori_loop(
            0, steps, lambda i, c: forward_stats(i * step_rows, c), start_stats
        )
        log_total = row_max + jnp.log(row_sum)
        attended = (weighted / row_sum[..., None]).astype(jnp.bfloat16)
        row_delta = jnp.einsum(
            "kgqd,qkgd->kgq", attended, grad_heads, preferred_element_type=jnp.float32
        )

        def backward_visit(turn_index, current):
            query_now, kv_now = current
            offset = turn_index * step_rows
            query_term, kv_term = backward_chunk(offset, log_total, row_delta)
            kv_now = lax.dynamic_update_slice_in_dim(kv_now, kv_term, offset, 0)
            return (query_now + query_term, kv_now)

        query_acc, kv_acc = lax.fori_loop(
            0,
            steps,
            backward_visit,
            (
                jnp.zeros((rows_here, kv_heads, group_size, HD), jnp.float32),
                jnp.zeros((row_count, 2 * kv_cols), jnp.float32),
            ),
        )
        query_grad = query_acc.reshape(rows_here, -1).astype(jnp.bfloat16)
        kv_grad = scatter_slots(kv_acc, "ctx")

    key_grad = kv_grad[:, :kv_cols].astype(jnp.bfloat16)
    value_grad = kv_grad[:, kv_cols:].astype(jnp.bfloat16)
    input_grad_t = head_reduce(key_proj, value_proj, key_grad, value_grad)
    return (query_grad, key_grad, value_grad, input_grad_t)


def solution(mesh):
    return jax.shard_map(
        local,
        mesh=mesh,
        in_specs=(
            P(("groups", "ctx"), "head"),
            P(("groups", "ctx"), "head"),
            P(("groups", "ctx"), "head"),
            P(("groups", "ctx"), "head"),
            P("groups", None),
            P("groups"),
            P(None, "head"),
            P(None, "head"),
        ),
        out_specs=(
            P(("groups", "ctx"), "head"),
            P(("groups", "ctx"), "head"),
            P(("groups", "ctx"), "head"),
            P("head", ("groups", "ctx")),
        ),
        check_vma=False,
    )
```
